32 devices in a mesh: box: 8 (over z, y), dir: 4 (over x, core).
Axes of the slice: x: 2, y: 2, z: 4, core: 2. Of those that a mesh axis runs over, the one named last changes fastest.
Arguments:
- child_pattern: float32 [1024, 4, 128, 128], P('box', None, 'dir'), may hold values from -5 to 5
- octant: int32 [1024], P('box'), may hold values from 0 to 7, as said below
- shift_angle: float32 [8, 256, 256], replicated, may hold values from -3.140625 to 3.140625
- trans_table: bfloat16 [316, 2, 256, 256], P(None, None, 'dir'), may hold values from -2 to 2
- pair_near: int32 [1536], P('box'), may hold values from 0 to 15, as said below
- pair_far: int32 [1536], P('box'), may hold values from 0 to 47, as said below
- pair_class: int32 [1536], P('box'), may hold values from 0 to 315
- pair_live: int32 [1536], P('box'), may hold values from 0 to 1, as said below
Outputs:
- aggregated: float32 [128, 4, 256, 256], P('box', None, 'dir')
- incoming: float32 [128, 4, 256, 256], P('box', None, 'dir')
The draws below stay inside these ranges and needn't reach their ends.
Inputs may be any that keep to these rules, and one draw needn't show every extreme that they name: `octant`: within each parent's eight consecutive children, a permutation of 0 to 7. `pair_near`: index of the pair's first box among the 16 boxes of the device that holds the slot. `pair_far`: index into the boxes of the slot's own device followed by those of the next 2 devices along box; never the pair's first box, never past the last box. `pair_live`: each device's live slots come first; some device has all 192 slots live.
All inputs are finite; a program needn't handle non-finite values.
Results may differ from the reference program's by a relative error of at most 0.0003.
Values sent between devices are 32-bit elements; how exact they have to be, the bound alone decides.
No kernel may reach another device: no remote copies, remote signals or barrier semaphores. Data moves between devices by JAX's collectives and lax.ppermute only.
A program may use at most 384 MiB of HBM per device.

```python
import math
import jax
import jax.numpy as jnp
from jax import lax

BOX_DEV = 16
PAIR_BOX = 12
REACH = 2
CLASSES = 316
THETA1 = 128
PHI1 = 128
THETA2 = 256
PHI2 = 256
NBOX = 128
NCHILD = 1024
PAIRS_DEV = 192
NPAIRS = 1536


def pair_draw(key):
    base_key = jax.random.fold_in(key, 11)
    key_near, key_far, key_rate, key_full = jax.random.split(base_key, 4)
    devices = NBOX // BOX_DEV
    pairs_dev = PAIR_BOX * BOX_DEV
    slot_ids = jnp.arange(devices * pairs_dev, dtype=jnp.int32)
    owner_dev = slot_ids // pairs_dev
    near_box = jax.random.randint(key_near, slot_ids.shape, 0, BOX_DEV, dtype=jnp.int32)
    near_box = jnp.where(slot_ids == 0, 0, near_box)
    near_box = jnp.where(slot_ids == 1, BOX_DEV - 1, near_box)
    span_rows = jnp.minimum(REACH + 1, devices - owner_dev) * BOX_DEV
    far_box = jax.random.randint(key_far, slot_ids.shape, 0, 1 << 24, dtype=jnp.int32) % span_rows
    far_box = jnp.where(slot_ids == 0, (REACH + 1) * BOX_DEV - 1, far_box)
    far_box = jnp.where(slot_ids == 1, 0, far_box)
    far_box = jnp.where(far_box == near_box, (near_box + 1) % BOX_DEV, far_box)
    halving = jax.random.randint(key_rate, (devices,), 0, 4, dtype=jnp.int32)
    fullest = jax.random.randint(key_full, (), 0, devices, dtype=jnp.int32)
    halving = jnp.where(jnp.arange(devices, dtype=jnp.int32) == fullest, 0, halving)
    counts = pairs_dev // jnp.left_shift(jnp.ones_like(halving), halving)
    live_mask = (slot_ids % pairs_dev < counts[owner_dev]).astype(jnp.int32)
    return (near_box, far_box, live_mask)


def draw_pair_near(key, part):
    return pair_draw(key)[0]


def draw_pair_far(key, part):
    return pair_draw(key)[1]


def draw_pair_live(key, part):
    return pair_draw(key)[2]


def draw_octant(key, part):
    scores = jax.random.randint(jax.random.fold_in(key, 5), (NBOX, 8), 0, 1 << 20, dtype=jnp.int32) * 8
    scores = scores + jnp.arange(8, dtype=jnp.int32)[None, :]
    return jnp.argsort(scores, axis=1, stable=True).astype(jnp.int32).reshape(NBOX * 8)


def plant(result, stream_key, least, high):
    shape = result.shape
    place = [jax.random.randint(jax.random.fold_in(stream_key, axis), (), 0, shape[axis]) for axis in range(len(shape))]
    result = result.at[tuple(place)].set(least)
    longest = shape.index(max(shape))
    place[longest] = (place[longest] + 1) % shape[longest]
    return result.at[tuple(place)].set(high)


def steps_of(own_key, shape, shards, least, high):
    def one(position, shards_of):
        heights = jax.random.uniform(jax.random.fold_in(jax.random.fold_in(own_key, 6), position), (shards_of,), jnp.float32, least / len(shards), high / len(shards))
        return jnp.repeat(jnp.exp(heights), shape[position] // shards_of).reshape((-1,) + (1,) * (len(shape) - position - 1))

    factor_of = one(*shards[0])
    for cut in shards[1:]:
        factor_of = factor_of * one(*cut)
    return factor_of


def bell_draw(stream_key, extent, deviation, reach, cuts=(), held_as=jnp.bfloat16):
    gain = steps_of(stream_key, extent, cuts, -0.22, 0.18) if cuts else 1.0
    array = jax.random.normal(stream_key, extent, jnp.float32) * deviation * gain
    return jnp.minimum(jnp.maximum(array, -reach), reach).astype(held_as)


def setup_inputs(seed: int = 0) -> dict:
    keys = jax.random.split(jax.random.key(seed), 9)
    return {
        "child_pattern": bell_draw(keys[0], (NCHILD, 4, PHI1, THETA1), 0.35, 5.0, ((0, 8), (2, 4)), jnp.float32),
        "octant": draw_octant(jax.random.fold_in(keys[8], 71), 0),
        "shift_angle": jnp.clip(jax.random.uniform(keys[2], (8, PHI2, THETA2), jnp.float32, -3.140625, 3.140625), -3.140625, 3.140625),
        "trans_table": bell_draw(keys[3], (CLASSES, 2, PHI2, THETA2), 0.15, 2.0, ((2, 4),)),
        "pair_near": draw_pair_near(jax.random.fold_in(keys[8], 71), 0),
        "pair_far": draw_pair_far(jax.random.fold_in(keys[8], 71), 0),
        "pair_class": plant(jax.random.randint(keys[6], (NPAIRS,), 0, CLASSES), jax.random.fold_in(keys[6], 1), 0, CLASSES - 1).astype(jnp.int32),
        "pair_live": draw_pair_live(jax.random.fold_in(keys[8], 71), 0),
    }


HIGHEST = lax.Precision.HIGHEST


def interp_rows(size_in, size_out, first, count):
    target_pos = first + jnp.arange(count, dtype=jnp.int32)
    source_pos = jnp.arange(size_in, dtype=jnp.int32)
    offset = target_pos[:, None] - 2 * source_pos[None, :]
    is_odd = (offset % 2) == 1
    safe_off = jnp.where(is_odd, offset, 1).astype(jnp.float32)
    kernel = jnp.sin(math.pi * safe_off / 2.0) / (size_in * jnp.tan(math.pi * safe_off / size_out))
    inner = jnp.where(is_odd, kernel, jnp.zeros_like(kernel))
    return jnp.where(offset == 0, jnp.ones_like(kernel), inner)


def interpolate(fields, theta_map, phi_map):
    widened = jnp.einsum('...t,ut->...u', fields, theta_map, precision=HIGHEST)
    return jnp.einsum('qp,...pu->...qu', phi_map, widened, precision=HIGHEST)


def shift_sum(fields, octant_rows, cos_table, sin_table):
    groups = fields.shape[0]
    cosine = jnp.take(cos_table, octant_rows, axis=0)[:, :, None]
    sine = jnp.take(sin_table, octant_rows, axis=0)[:, :, None]
    shaped = fields.reshape(groups, 8, 2, 2, fields.shape[3], fields.shape[4])
    real_part = shaped[:, :, :, 0]
    imag_part = shaped[:, :, :, 1]
    new_real = jnp.sum(cosine * real_part - sine * imag_part, axis=1)
    new_imag = jnp.sum(sine * real_part + cosine * imag_part, axis=1)
    return jnp.stack([new_real, new_imag], axis=2).reshape(groups, 4, fields.shape[3], fields.shape[4])


def translate(table_rows, patterns):
    shaped = patterns.reshape(patterns.shape[:-3] + (2, 2) + patterns.shape[-2:])
    t_real = table_rows[..., 0:1, :, :]
    t_imag = table_rows[..., 1:2, :, :]
    p_real = shaped[..., :, 0, :, :]
    p_imag = shaped[..., :, 1, :, :]
    new_real = t_real * p_real - t_imag * p_imag
    new_imag = t_imag * p_real + t_real * p_imag
    return jnp.stack([new_real, new_imag], axis=-3).reshape(patterns.shape)


def reference(child_pattern, octant, shift_angle, trans_table, pair_near, pair_far, pair_class, pair_live):
    theta_map = interp_rows(THETA1, THETA2, 0, THETA2)
    phi_map = interp_rows(PHI1, PHI2, 0, PHI2)
    cos_table = jnp.cos(shift_angle)
    sin_table = jnp.sin(shift_angle)
    grouped = child_pattern.reshape(NBOX, 8, 4, PHI1, THETA1)
    octant_all = octant.reshape(NBOX, 8)

    def one_parent(item):
        fields, octant_rows = item
        full_dirs = interpolate(fields, theta_map, phi_map)
        return shift_sum(full_dirs[None], octant_rows[None], cos_table, sin_table)[0]

    aggregated = lax.map(one_parent, (grouped, octant_all))
    slot_ids = jnp.arange(pair_near.shape[0], dtype=jnp.int32)
    owner_dev = slot_ids // PAIRS_DEV
    first_box = owner_dev * BOX_DEV + pair_near
    second_box = owner_dev * BOX_DEV + pair_far
    mirror = (pair_class + CLASSES // 2) % CLASSES

    def add_pair(incoming, item):
        box_first, box_second, class_ab, class_ba, alive = item
        is_live = alive > 0
        to_first = translate(trans_table[class_ab].astype(jnp.float32), aggregated[box_second])
        to_second = translate(trans_table[class_ba].astype(jnp.float32), aggregated[box_first])
        incoming = incoming.at[box_first].add(jnp.where(is_live, to_first, jnp.zeros_like(to_first)))
        incoming = incoming.at[box_second].add(jnp.where(is_live, to_second, jnp.zeros_like(to_second)))
        return incoming, None

    incoming = lax.scan(add_pair, jnp.zeros_like(aggregated), (first_box, second_box, pair_class, mirror, pair_live))[0]
    return (aggregated, incoming)
```

```python
import functools
import math

import jax
import jax.numpy as jnp
from jax import lax
from jax.experimental import pallas as pl
from jax.experimental.pallas import tpu as pltpu
from jax.sharding import PartitionSpec as P

REACH = 2
THETA1 = 128
PHI1 = 128
THETA2 = 256
PHI2 = 256
ROWS = 16


HIGHEST = lax.Precision.HIGHEST


def passed_along(value, axis, steps):
    count = lax.axis_size(axis)
    first, last = (max(0, -steps), min(count, count - steps))
    return lax.ppermute(value, axis, [(source, source + steps) for source in range(first, last)])


def interp_rows(size_in, size_out, count):
    target_pos = jnp.arange(count, dtype=jnp.int32)
    source_pos = jnp.arange(size_in, dtype=jnp.int32)
    offset = target_pos[:, None] - 2 * source_pos[None, :]
    is_odd = offset % 2 == 1
    safe_off = jnp.where(is_odd, offset, 1).astype(jnp.float32)
    kernel = jnp.sin(math.pi * safe_off / 2.0) / (size_in * jnp.tan(math.pi * safe_off / size_out))
    inner = jnp.where(is_odd, kernel, jnp.zeros_like(kernel))
    return jnp.where(offset == 0, jnp.ones_like(kernel), inner)


def interpolate(fields, theta_map, phi_map):
    widened = jnp.einsum("...t,ut->...u", fields, theta_map, precision=HIGHEST)
    return jnp.einsum("qp,...pu->...qu", phi_map, widened, precision=HIGHEST)


def select_rows(indices, table):
    count = table.shape[0]
    flat_ids = indices.reshape(-1)
    row_ids = jnp.arange(count, dtype=jnp.int32)
    onehot = (flat_ids[:, None] == row_ids[None, :]).astype(table.dtype)
    flat_table = table.reshape(count, -1)
    picked = jnp.dot(onehot, flat_table, precision=HIGHEST, preferred_element_type=jnp.float32)
    return picked.reshape(indices.shape + table.shape[1:])


def shift_sum(fields, octant_rows, cos_table, sin_table):
    groups = fields.shape[0]
    cosine = select_rows(octant_rows, cos_table)[:, :, None]
    sine = select_rows(octant_rows, sin_table)[:, :, None]
    shaped = fields.reshape(groups, 8, 2, 2, fields.shape[3], fields.shape[4])
    real_part = shaped[:, :, :, 0]
    imag_part = shaped[:, :, :, 1]
    new_real = jnp.sum(cosine * real_part - sine * imag_part, axis=1)
    new_imag = jnp.sum(sine * real_part + cosine * imag_part, axis=1)
    return jnp.stack([new_real, new_imag], axis=2).reshape(
        groups, 4, fields.shape[3], fields.shape[4]
    )


def pair_kernel(tgt_ref, src_ref, cls_ref, live_ref, table_hbm, *rest):
    blocks = rest[:-6]
    out_hbm, table, sources, acc, sems, out_sem = rest[-6:]
    box_dev = blocks[0].shape[0]
    rows = table.shape[2]
    copies = [pltpu.make_async_copy(table_hbm, table, sems.at[0])]
    for b, block in enumerate(blocks):
        copies.append(
            pltpu.make_async_copy(block, sources.at[pl.ds(b * box_dev, box_dev)], sems.at[b + 1])
        )
    for c in copies:
        c.start()
    acc[...] = jnp.zeros_like(acc)
    for c in copies:
        c.wait()

    def item(i, carry):
        @pl.when(live_ref[i] != 0)
        def _():
            t = tgt_ref[i]
            s = src_ref[i]
            k = cls_ref[i]

            def chunk(j, inner):
                r0 = pl.multiple_of(j * ROWS, ROWS)
                win = pl.ds(r0, ROWS)
                tr = table[k, 0, win, :].astype(jnp.float32)
                ti = table[k, 1, win, :].astype(jnp.float32)
                for q in range(2):
                    pr = sources[s, 2 * q, win, :]
                    pi = sources[s, 2 * q + 1, win, :]
                    acc[t, 2 * q, win, :] += tr * pr - ti * pi
                    acc[t, 2 * q + 1, win, :] += ti * pr + tr * pi
                return inner

            lax.fori_loop(0, rows // ROWS, chunk, 0, unroll=True)

        return carry

    lax.fori_loop(0, tgt_ref.shape[0], item, 0)
    done = pltpu.make_async_copy(acc, out_hbm, out_sem.at[0])
    done.start()
    done.wait()


def translate_pairs(items, trans_table, blocks):
    tgt, src, cls, live = items
    box_dev = blocks[0].shape[0]
    shape = blocks[0].shape
    smem = pl.BlockSpec(memory_space=pltpu.SMEM)
    anywhere = pl.BlockSpec(memory_space=pl.ANY)
    return pl.pallas_call(
        pair_kernel,
        out_shape=jax.ShapeDtypeStruct(shape, jnp.float32),
        in_specs=[smem] * 4 + [anywhere] * (1 + len(blocks)),
        out_specs=anywhere,
        scratch_shapes=[
            pltpu.VMEM(trans_table.shape, trans_table.dtype),
            pltpu.VMEM((len(blocks) * box_dev,) + shape[1:], jnp.float32),
            pltpu.VMEM(shape, jnp.float32),
            pltpu.SemaphoreType.DMA((1 + len(blocks),)),
            pltpu.SemaphoreType.DMA((1,)),
        ],
        compiler_params=pltpu.CompilerParams(vmem_limit_bytes=66_000_000),
    )(tgt, src, cls, live, trans_table, *blocks)


def pair_items(pair_near, pair_far, pair_class, pair_live, box_dev, classes):
    packed = jnp.stack([pair_near, pair_far, pair_class, pair_live])
    lists = [packed] + [passed_along(packed, "box", o) for o in range(1, REACH + 1)]
    tgt = [pair_near]
    src = [pair_far]
    cls = [pair_class]
    live = [pair_live]
    for o, lst in enumerate(lists):
        near, far, k, alive = lst[0], lst[1], lst[2], lst[3]
        tgt.append(far - o * box_dev)
        base = 0 if o == 0 else (REACH + o) * box_dev
        src.append(near + base)
        cls.append((k + classes // 2) % classes)
        live.append(jnp.where(far // box_dev == o, alive, 0))
    return [jnp.concatenate(x).astype(jnp.int32) for x in (tgt, src, cls, live)]


def body(
    child_pattern, octant, shift_angle, trans_table, pair_near, pair_far, pair_class, pair_live
):
    dir_count = lax.axis_size("dir")
    dir_index = lax.axis_index("dir")
    box_dev = child_pattern.shape[0] // 8
    classes = trans_table.shape[0]
    theta_map = interp_rows(THETA1, THETA2, THETA2)
    cos_table = jnp.cos(shift_angle)
    sin_table = jnp.sin(shift_angle)
    grouped = child_pattern.reshape(box_dev, 8, 4, PHI1 // dir_count, THETA1)
    gathered = lax.all_to_all(grouped, "dir", split_axis=0, concat_axis=3, tiled=True)
    per_dev = box_dev // dir_count
    octant_rows = lax.dynamic_slice_in_dim(octant, dir_index * (per_dev * 8), per_dev * 8).reshape(
        per_dev, 8
    )
    phi_map = interp_rows(PHI1, PHI2, PHI2)
    full_dirs = interpolate(gathered, theta_map, phi_map)
    summed = shift_sum(full_dirs, octant_rows, cos_table, sin_table)
    aggregated = lax.all_to_all(summed, "dir", split_axis=2, concat_axis=0, tiled=True)
    blocks = [aggregated]
    for offset in range(1, REACH + 1):
        blocks.append(passed_along(aggregated, "box", -offset))
    for offset in range(1, REACH + 1):
        blocks.append(passed_along(aggregated, "box", offset))
    items = pair_items(pair_near, pair_far, pair_class, pair_live, box_dev, classes)
    incoming = translate_pairs(items, trans_table, blocks)
    return (aggregated, incoming)


def solution(mesh):
    placed = (
        P("box", None, "dir", None),
        P("box"),
        P(),
        P(None, None, "dir", None),
        P("box"),
        P("box"),
        P("box"),
        P("box"),
    )
    return jax.shard_map(
        body,
        mesh=mesh,
        in_specs=placed,
        out_specs=(P("box", None, "dir", None), P("box", None, "dir", None)),
        check_vma=False,
    )
```

```python
import functools
import math

import jax
import jax.numpy as jnp
from jax import lax
from jax.experimental import pallas as pl
from jax.experimental.pallas import tpu as pltpu
from jax.sharding import PartitionSpec as P

REACH = 2
THETA1 = 128
PHI1 = 128
THETA2 = 256
PHI2 = 256
ROWS = 16


HIGHEST = lax.Precision.HIGHEST


def passed_along(value, axis, steps):
    count = lax.axis_size(axis)
    first, last = (max(0, -steps), min(count, count - steps))
    return lax.ppermute(value, axis, [(source, source + steps) for source in range(first, last)])


def interp_rows(size_in, size_out, count):
    target_pos = jnp.arange(count, dtype=jnp.int32)
    source_pos = jnp.arange(size_in, dtype=jnp.int32)
    offset = target_pos[:, None] - 2 * source_pos[None, :]
    is_odd = offset % 2 == 1
    safe_off = jnp.where(is_odd, offset, 1).astype(jnp.float32)
    kernel = jnp.sin(math.pi * safe_off / 2.0) / (size_in * jnp.tan(math.pi * safe_off / size_out))
    inner = jnp.where(is_odd, kernel, jnp.zeros_like(kernel))
    return jnp.where(offset == 0, jnp.ones_like(kernel), inner)


def interpolate(fields, theta_map, phi_map):
    widened = jnp.einsum("...t,ut->...u", fields, theta_map, precision=HIGHEST)
    return jnp.einsum("qp,...pu->...qu", phi_map, widened, precision=HIGHEST)


def select_rows(indices, table):
    count = table.shape[0]
    flat_ids = indices.reshape(-1)
    row_ids = jnp.arange(count, dtype=jnp.int32)
    onehot = (flat_ids[:, None] == row_ids[None, :]).astype(table.dtype)
    flat_table = table.reshape(count, -1)
    picked = jnp.dot(onehot, flat_table, precision=HIGHEST, preferred_element_type=jnp.float32)
    return picked.reshape(indices.shape + table.shape[1:])


def shift_sum(fields, octant_rows, cos_table, sin_table):
    groups = fields.shape[0]
    cosine = select_rows(octant_rows, cos_table)[:, :, None]
    sine = select_rows(octant_rows, sin_table)[:, :, None]
    shaped = fields.reshape(groups, 8, 2, 2, fields.shape[3], fields.shape[4])
    real_part = shaped[:, :, :, 0]
    imag_part = shaped[:, :, :, 1]
    new_real = jnp.sum(cosine * real_part - sine * imag_part, axis=1)
    new_imag = jnp.sum(sine * real_part + cosine * imag_part, axis=1)
    return jnp.stack([new_real, new_imag], axis=2).reshape(
        groups, 4, fields.shape[3], fields.shape[4]
    )


def pair_kernel(offsets, tgt_ref, src_ref, cls_ref, live_ref, table_hbm, *rest):
    blocks = rest[:-6]
    out_hbm, table, sources, acc, sems, out_sem = rest[-6:]
    rows = table.shape[2]
    copies = [pltpu.make_async_copy(table_hbm, table, sems.at[0])]
    for b, (block, first) in enumerate(zip(blocks, offsets)):
        copies.append(
            pltpu.make_async_copy(block, sources.at[pl.ds(first, block.shape[0])], sems.at[b + 1])
        )
    for c in copies:
        c.start()
    acc[...] = jnp.zeros_like(acc)
    for c in copies:
        c.wait()

    def item(i, carry):
        @pl.when(live_ref[i] != 0)
        def _():
            t = tgt_ref[i]
            s = src_ref[i]
            k = cls_ref[i]

            def chunk(j, inner):
                r0 = pl.multiple_of(j * ROWS, ROWS)
                win = pl.ds(r0, ROWS)
                tr = table[k, 0, win, :].astype(jnp.float32)
                ti = table[k, 1, win, :].astype(jnp.float32)
                for q in range(2):
                    pr = sources[s, 2 * q, win, :]
                    pi = sources[s, 2 * q + 1, win, :]
                    acc[t, 2 * q, win, :] += tr * pr - ti * pi
                    acc[t, 2 * q + 1, win, :] += ti * pr + tr * pi
                return inner

            lax.fori_loop(0, rows // ROWS, chunk, 0, unroll=True)

        return carry

    lax.fori_loop(0, tgt_ref.shape[0], item, 0)
    done = pltpu.make_async_copy(acc, out_hbm, out_sem.at[0])
    done.start()
    done.wait()


def translate_pairs(items, trans_table, blocks, offsets, box_dev):
    tgt, src, cls, live = items
    shape = (box_dev,) + blocks[0].shape[1:]
    smem = pl.BlockSpec(memory_space=pltpu.SMEM)
    anywhere = pl.BlockSpec(memory_space=pl.ANY)
    return pl.pallas_call(
        functools.partial(pair_kernel, tuple(offsets)),
        out_shape=jax.ShapeDtypeStruct(shape, jnp.float32),
        in_specs=[smem] * 4 + [anywhere] * (1 + len(blocks)),
        out_specs=anywhere,
        scratch_shapes=[
            pltpu.VMEM(trans_table.shape, trans_table.dtype),
            pltpu.VMEM(((2 * REACH + 1) * box_dev,) + shape[1:], jnp.float32),
            pltpu.VMEM(shape, jnp.float32),
            pltpu.SemaphoreType.DMA((1 + len(blocks),)),
            pltpu.SemaphoreType.DMA((1,)),
        ],
        compiler_params=pltpu.CompilerParams(vmem_limit_bytes=66_000_000),
    )(tgt, src, cls, live, trans_table, *blocks)


def pair_items(pair_near, pair_far, pair_class, pair_live, box_dev, classes):
    packed = jnp.stack([pair_near, pair_far, pair_class, pair_live])
    lists = [packed] + [passed_along(packed, "box", o) for o in range(1, REACH + 1)]
    tgt = [pair_near]
    src = [pair_far]
    cls = [pair_class]
    live = [pair_live]
    for o, lst in enumerate(lists):
        near, far, k, alive = lst[0], lst[1], lst[2], lst[3]
        tgt.append(far - o * box_dev)
        base = 0 if o == 0 else (REACH + o) * box_dev
        src.append(near + base)
        cls.append((k + classes // 2) % classes)
        live.append(jnp.where(far // box_dev == o, alive, 0))
    return [jnp.concatenate(x).astype(jnp.int32) for x in (tgt, src, cls, live)]


def body(
    child_pattern, octant, shift_angle, trans_table, pair_near, pair_far, pair_class, pair_live
):
    dir_count = lax.axis_size("dir")
    dir_index = lax.axis_index("dir")
    box_dev = child_pattern.shape[0] // 8
    classes = trans_table.shape[0]
    items = pair_items(pair_near, pair_far, pair_class, pair_live, box_dev, classes)
    theta_map = interp_rows(THETA1, THETA2, THETA2)
    phi_map = interp_rows(PHI1, PHI2, PHI2)
    cos_table = jnp.cos(shift_angle)
    sin_table = jnp.sin(shift_angle)
    grouped = child_pattern.reshape(box_dev, 8, 4, PHI1 // dir_count, THETA1)
    chunks = 2 if box_dev % (2 * dir_count) == 0 else 1
    per_chunk = box_dev // chunks
    per_dev = per_chunk // dir_count
    parts = []
    blocks = []
    offsets = []
    for c in range(chunks):
        piece = grouped[c * per_chunk : (c + 1) * per_chunk]
        gathered = lax.all_to_all(piece, "dir", split_axis=0, concat_axis=3, tiled=True)
        first = (c * per_chunk + dir_index * per_dev) * 8
        octant_rows = lax.dynamic_slice_in_dim(octant, first, per_dev * 8).reshape(per_dev, 8)
        full_dirs = interpolate(gathered, theta_map, phi_map)
        summed = shift_sum(full_dirs, octant_rows, cos_table, sin_table)
        part = lax.all_to_all(summed, "dir", split_axis=2, concat_axis=0, tiled=True)
        parts.append(part)
        moved = [part]
        moved += [passed_along(part, "box", -o) for o in range(1, REACH + 1)]
        moved += [passed_along(part, "box", o) for o in range(1, REACH + 1)]
        for b, block in enumerate(moved):
            blocks.append(block)
            offsets.append(b * box_dev + c * per_chunk)
    aggregated = jnp.concatenate(parts, axis=0) if chunks > 1 else parts[0]
    incoming = translate_pairs(items, trans_table, blocks, offsets, box_dev)
    return (aggregated, incoming)


def solution(mesh):
    placed = (
        P("box", None, "dir", None),
        P("box"),
        P(),
        P(None, None, "dir", None),
        P("box"),
        P("box"),
        P("box"),
        P("box"),
    )
    return jax.shard_map(
        body,
        mesh=mesh,
        in_specs=placed,
        out_specs=(P("box", None, "dir", None), P("box", None, "dir", None)),
        check_vma=False,
    )
```

```python
import functools
import math

import jax
import jax.numpy as jnp
from jax import lax
from jax.experimental import pallas as pl
from jax.experimental.pallas import tpu as pltpu
from jax.sharding import PartitionSpec as P

REACH = 2
THETA1 = 128
PHI1 = 128
THETA2 = 256
PHI2 = 256
ROWS = 16


HIGHEST = lax.Precision.HIGHEST


def passed_along(value, axis, steps):
    count = lax.axis_size(axis)
    first, last = (max(0, -steps), min(count, count - steps))
    return lax.ppermute(value, axis, [(source, source + steps) for source in range(first, last)])


def interp_rows(size_in, size_out, count):
    target_pos = jnp.arange(count, dtype=jnp.int32)
    source_pos = jnp.arange(size_in, dtype=jnp.int32)
    offset = target_pos[:, None] - 2 * source_pos[None, :]
    is_odd = offset % 2 == 1
    safe_off = jnp.where(is_odd, offset, 1).astype(jnp.float32)
    kernel = jnp.sin(math.pi * safe_off / 2.0) / (size_in * jnp.tan(math.pi * safe_off / size_out))
    inner = jnp.where(is_odd, kernel, jnp.zeros_like(kernel))
    return jnp.where(offset == 0, jnp.ones_like(kernel), inner)


def interpolate(fields, theta_map, phi_map):
    widened = jnp.einsum("...t,ut->...u", fields, theta_map, precision=HIGHEST)
    return jnp.einsum("qp,...pu->...qu", phi_map, widened, precision=HIGHEST)


def select_rows(indices, table):
    count = table.shape[0]
    flat_ids = indices.reshape(-1)
    row_ids = jnp.arange(count, dtype=jnp.int32)
    onehot = (flat_ids[:, None] == row_ids[None, :]).astype(table.dtype)
    flat_table = table.reshape(count, -1)
    picked = jnp.dot(onehot, flat_table, precision=HIGHEST, preferred_element_type=jnp.float32)
    return picked.reshape(indices.shape + table.shape[1:])


def shift_sum(fields, cos_table, sin_table):
    groups = fields.shape[0]
    cosine = cos_table[None, :, None]
    sine = sin_table[None, :, None]
    shaped = fields.reshape(groups, 8, 2, 2, fields.shape[3], fields.shape[4])
    real_part = shaped[:, :, :, 0]
    imag_part = shaped[:, :, :, 1]
    new_real = jnp.sum(cosine * real_part - sine * imag_part, axis=1)
    new_imag = jnp.sum(sine * real_part + cosine * imag_part, axis=1)
    return jnp.stack([new_real, new_imag], axis=2).reshape(
        groups, 4, fields.shape[3], fields.shape[4]
    )


def pair_kernel(offsets, tgt_ref, src_ref, cls_ref, live_ref, table_hbm, *rest):
    blocks = rest[:-6]
    out_hbm, table, sources, acc, sems, out_sem = rest[-6:]
    rows = table.shape[2]
    copies = [pltpu.make_async_copy(table_hbm, table, sems.at[0])]
    for b, (block, first) in enumerate(zip(blocks, offsets)):
        copies.append(
            pltpu.make_async_copy(block, sources.at[pl.ds(first, block.shape[0])], sems.at[b + 1])
        )
    for c in copies:
        c.start()
    acc[...] = jnp.zeros_like(acc)
    for c in copies:
        c.wait()

    def item(i, carry):
        @pl.when(live_ref[i] != 0)
        def _():
            t = tgt_ref[i]
            s = src_ref[i]
            k = cls_ref[i]

            def chunk(j, inner):
                r0 = pl.multiple_of(j * ROWS, ROWS)
                win = pl.ds(r0, ROWS)
                tr = table[k, 0, win, :].astype(jnp.float32)
                ti = table[k, 1, win, :].astype(jnp.float32)
                for q in range(2):
                    pr = sources[s, 2 * q, win, :]
                    pi = sources[s, 2 * q + 1, win, :]
                    acc[t, 2 * q, win, :] += tr * pr - ti * pi
                    acc[t, 2 * q + 1, win, :] += ti * pr + tr * pi
                return inner

            lax.fori_loop(0, rows // ROWS, chunk, 0, unroll=True)

        return carry

    lax.fori_loop(0, tgt_ref.shape[0], item, 0)
    done = pltpu.make_async_copy(acc, out_hbm, out_sem.at[0])
    done.start()
    done.wait()


def translate_pairs(items, trans_table, blocks, offsets, box_dev):
    tgt, src, cls, live = items
    shape = (box_dev,) + blocks[0].shape[1:]
    smem = pl.BlockSpec(memory_space=pltpu.SMEM)
    anywhere = pl.BlockSpec(memory_space=pl.ANY)
    return pl.pallas_call(
        functools.partial(pair_kernel, tuple(offsets)),
        out_shape=jax.ShapeDtypeStruct(shape, jnp.float32),
        in_specs=[smem] * 4 + [anywhere] * (1 + len(blocks)),
        out_specs=anywhere,
        scratch_shapes=[
            pltpu.VMEM(trans_table.shape, trans_table.dtype),
            pltpu.VMEM(((2 * REACH + 1) * box_dev,) + shape[1:], jnp.float32),
            pltpu.VMEM(shape, jnp.float32),
            pltpu.SemaphoreType.DMA((1 + len(blocks),)),
            pltpu.SemaphoreType.DMA((1,)),
        ],
        compiler_params=pltpu.CompilerParams(vmem_limit_bytes=66_000_000),
    )(tgt, src, cls, live, trans_table, *blocks)


def pair_items(pair_near, pair_far, pair_class, pair_live, box_dev, classes):
    packed = jnp.stack([pair_near, pair_far, pair_class, pair_live])
    lists = [packed] + [passed_along(packed, "box", o) for o in range(1, REACH + 1)]
    tgt = [pair_near]
    src = [pair_far]
    cls = [pair_class]
    live = [pair_live]
    for o, lst in enumerate(lists):
        near, far, k, alive = lst[0], lst[1], lst[2], lst[3]
        tgt.append(far - o * box_dev)
        base = 0 if o == 0 else (REACH + o) * box_dev
        src.append(near + base)
        cls.append((k + classes // 2) % classes)
        live.append(jnp.where(far // box_dev == o, alive, 0))
    return [jnp.concatenate(x).astype(jnp.int32) for x in (tgt, src, cls, live)]


def body(
    child_pattern, octant, shift_angle, trans_table, pair_near, pair_far, pair_class, pair_live
):
    dir_count = lax.axis_size("dir")
    dir_index = lax.axis_index("dir")
    box_dev = child_pattern.shape[0] // 8
    classes = trans_table.shape[0]
    items = pair_items(pair_near, pair_far, pair_class, pair_live, box_dev, classes)
    theta_map = interp_rows(THETA1, THETA2, THETA2)
    phi_map = interp_rows(PHI1, PHI2, PHI2)
    cos_table = jnp.cos(shift_angle)
    sin_table = jnp.sin(shift_angle)
    grouped = child_pattern.reshape(box_dev, 8, 4, PHI1 // dir_count, THETA1)
    octants = octant.reshape(box_dev, 8)
    slots = jnp.arange(8, dtype=jnp.int32)
    by_octant = jnp.sum(
        jnp.where(octants[:, :, None] == slots[None, None, :], slots[None, :, None], 0), axis=1
    )
    grouped = jnp.take_along_axis(grouped, by_octant[:, :, None, None, None], axis=1)
    chunks = 1
    while chunks < 4 and box_dev % (2 * chunks * dir_count) == 0:
        chunks *= 2
    per_chunk = box_dev // chunks
    per_dev = per_chunk // dir_count
    parts = []
    blocks = []
    offsets = []
    for c in range(chunks):
        piece = grouped[c * per_chunk : (c + 1) * per_chunk]
        gathered = lax.all_to_all(piece, "dir", split_axis=0, concat_axis=3, tiled=True)
        full_dirs = interpolate(gathered, theta_map, phi_map)
        summed = shift_sum(full_dirs, cos_table, sin_table)
        part = lax.all_to_all(summed, "dir", split_axis=2, concat_axis=0, tiled=True)
        parts.append(part)
        moved = [part]
        moved += [passed_along(part, "box", -o) for o in range(1, REACH + 1)]
        moved += [passed_along(part, "box", o) for o in range(1, REACH + 1)]
        for b, block in enumerate(moved):
            blocks.append(block)
            offsets.append(b * box_dev + c * per_chunk)
    aggregated = jnp.concatenate(parts, axis=0) if chunks > 1 else parts[0]
    incoming = translate_pairs(items, trans_table, blocks, offsets, box_dev)
    return (aggregated, incoming)


def solution(mesh):
    placed = (
        P("box", None, "dir", None),
        P("box"),
        P(),
        P(None, None, "dir", None),
        P("box"),
        P("box"),
        P("box"),
        P("box"),
    )
    return jax.shard_map(
        body,
        mesh=mesh,
        in_specs=placed,
        out_specs=(P("box", None, "dir", None), P("box", None, "dir", None)),
        check_vma=False,
    )
```

```python
import functools
import math

import jax
import jax.numpy as jnp
from jax import lax
from jax.experimental import pallas as pl
from jax.experimental.pallas import tpu as pltpu
from jax.sharding import PartitionSpec as P

REACH = 2
THETA1 = 128
PHI1 = 128
THETA2 = 256
PHI2 = 256
ROWS = 16


HIGHEST = lax.Precision.HIGHEST


def passed_along(value, axis, steps):
    count = lax.axis_size(axis)
    first, last = (max(0, -steps), min(count, count - steps))
    return lax.ppermute(value, axis, [(source, source + steps) for source in range(first, last)])


def interp_rows(size_in, size_out, count):
    target_pos = jnp.arange(count, dtype=jnp.int32)
    source_pos = jnp.arange(size_in, dtype=jnp.int32)
    offset = target_pos[:, None] - 2 * source_pos[None, :]
    is_odd = offset % 2 == 1
    safe_off = jnp.where(is_odd, offset, 1).astype(jnp.float32)
    kernel = jnp.sin(math.pi * safe_off / 2.0) / (size_in * jnp.tan(math.pi * safe_off / size_out))
    inner = jnp.where(is_odd, kernel, jnp.zeros_like(kernel))
    return jnp.where(offset == 0, jnp.ones_like(kernel), inner)


def interpolate(fields, theta_map, phi_map):
    widened = jnp.einsum("...t,ut->...u", fields, theta_map, precision=HIGHEST)
    return jnp.einsum("qp,...pu->...qu", phi_map, widened, precision=HIGHEST)


def select_rows(indices, table):
    count = table.shape[0]
    flat_ids = indices.reshape(-1)
    row_ids = jnp.arange(count, dtype=jnp.int32)
    onehot = (flat_ids[:, None] == row_ids[None, :]).astype(table.dtype)
    flat_table = table.reshape(count, -1)
    picked = jnp.dot(onehot, flat_table, precision=HIGHEST, preferred_element_type=jnp.float32)
    return picked.reshape(indices.shape + table.shape[1:])


def shift_sum(fields, cos_table, sin_table):
    groups = fields.shape[0]
    cosine = cos_table[None, :, None]
    sine = sin_table[None, :, None]
    shaped = fields.reshape(groups, 8, 2, 2, fields.shape[3], fields.shape[4])
    real_part = shaped[:, :, :, 0]
    imag_part = shaped[:, :, :, 1]
    new_real = jnp.sum(cosine * real_part - sine * imag_part, axis=1)
    new_imag = jnp.sum(sine * real_part + cosine * imag_part, axis=1)
    return jnp.stack([new_real, new_imag], axis=2).reshape(
        groups, 4, fields.shape[3], fields.shape[4]
    )


def pair_kernel(offsets, tgt_ref, src_ref, cls_ref, live_ref, table_hbm, *rest):
    blocks = rest[:-6]
    out_hbm, table, sources, acc, sems, out_sem = rest[-6:]
    rows = table.shape[2]
    copies = [pltpu.make_async_copy(table_hbm, table, sems.at[0])]
    for b, (block, first) in enumerate(zip(blocks, offsets)):
        copies.append(
            pltpu.make_async_copy(block, sources.at[pl.ds(first, block.shape[0])], sems.at[b + 1])
        )
    for c in copies:
        c.start()
    acc[...] = jnp.zeros_like(acc)
    for c in copies:
        c.wait()

    def item(i, carry):
        @pl.when(live_ref[i] != 0)
        def _():
            t = tgt_ref[i]
            s = src_ref[i]
            k = cls_ref[i]

            def chunk(j, inner):
                r0 = pl.multiple_of(j * ROWS, ROWS)
                win = pl.ds(r0, ROWS)
                tr = table[k, 0, win, :].astype(jnp.float32)
                ti = table[k, 1, win, :].astype(jnp.float32)
                for q in range(2):
                    pr = sources[s, 2 * q, win, :]
                    pi = sources[s, 2 * q + 1, win, :]
                    acc[t, 2 * q, win, :] += tr * pr - ti * pi
                    acc[t, 2 * q + 1, win, :] += ti * pr + tr * pi
                return inner

            lax.fori_loop(0, rows // ROWS, chunk, 0, unroll=True)

        return carry

    lax.fori_loop(0, tgt_ref.shape[0], item, 0)
    done = pltpu.make_async_copy(acc, out_hbm, out_sem.at[0])
    done.start()
    done.wait()


def translate_pairs(items, trans_table, blocks, offsets, box_dev):
    tgt, src, cls, live = items
    shape = (box_dev,) + blocks[0].shape[1:]
    smem = pl.BlockSpec(memory_space=pltpu.SMEM)
    anywhere = pl.BlockSpec(memory_space=pl.ANY)
    return pl.pallas_call(
        functools.partial(pair_kernel, tuple(offsets)),
        out_shape=jax.ShapeDtypeStruct(shape, jnp.float32),
        in_specs=[smem] * 4 + [anywhere] * (1 + len(blocks)),
        out_specs=anywhere,
        scratch_shapes=[
            pltpu.VMEM(trans_table.shape, trans_table.dtype),
            pltpu.VMEM(((2 * REACH + 1) * box_dev,) + shape[1:], jnp.float32),
            pltpu.VMEM(shape, jnp.float32),
            pltpu.SemaphoreType.DMA((1 + len(blocks),)),
            pltpu.SemaphoreType.DMA((1,)),
        ],
        compiler_params=pltpu.CompilerParams(vmem_limit_bytes=66_000_000),
    )(tgt, src, cls, live, trans_table, *blocks)


def pair_lists(pair_near, pair_far, pair_class, pair_live):
    packed = jnp.stack([pair_near, pair_far, pair_class, pair_live])
    return [packed] + [passed_along(packed, "box", o) for o in range(1, REACH + 1)]


def pair_items(lists, pair_near, pair_far, pair_class, pair_live, box_dev, classes):
    tgt = [pair_near]
    src = [pair_far]
    cls = [pair_class]
    live = [pair_live]
    for o, lst in enumerate(lists):
        near, far, k, alive = lst[0], lst[1], lst[2], lst[3]
        tgt.append(far - o * box_dev)
        base = 0 if o == 0 else (REACH + o) * box_dev
        src.append(near + base)
        cls.append((k + classes // 2) % classes)
        live.append(jnp.where(far // box_dev == o, alive, 0))
    return [jnp.concatenate(x).astype(jnp.int32) for x in (tgt, src, cls, live)]


def body(
    child_pattern, octant, shift_angle, trans_table, pair_near, pair_far, pair_class, pair_live
):
    dir_count = lax.axis_size("dir")
    dir_index = lax.axis_index("dir")
    box_dev = child_pattern.shape[0] // 8
    classes = trans_table.shape[0]
    lists = pair_lists(pair_near, pair_far, pair_class, pair_live)
    theta_map = interp_rows(THETA1, THETA2, THETA2)
    phi_map = interp_rows(PHI1, PHI2, PHI2)
    cos_table = jnp.cos(shift_angle)
    sin_table = jnp.sin(shift_angle)
    grouped = child_pattern.reshape(box_dev, 8, 4, PHI1 // dir_count, THETA1)
    octants = octant.reshape(box_dev, 8)
    slots = jnp.arange(8, dtype=jnp.int32)
    by_octant = jnp.sum(
        jnp.where(octants[:, :, None] == slots[None, None, :], slots[None, :, None], 0), axis=1
    )
    grouped = jnp.take_along_axis(grouped, by_octant[:, :, None, None, None], axis=1)
    chunks = 1
    while chunks < 2 and box_dev % (2 * chunks * dir_count) == 0:
        chunks *= 2
    per_chunk = box_dev // chunks
    per_dev = per_chunk // dir_count
    parts = []
    blocks = []
    offsets = []

    def send(c, part):
        moved = [part]
        moved += [passed_along(part, "box", -o) for o in range(1, REACH + 1)]
        moved += [passed_along(part, "box", o) for o in range(1, REACH + 1)]
        for b, block in enumerate(moved):
            blocks.append(block)
            offsets.append(b * box_dev + c * per_chunk)

    for c in range(chunks):
        piece = grouped[c * per_chunk : (c + 1) * per_chunk]
        gathered = lax.all_to_all(piece, "dir", split_axis=0, concat_axis=3, tiled=True)
        if parts:
            parts[-1], gathered = lax.optimization_barrier((parts[-1], gathered))
            send(c - 1, parts[-1])
        else:
            lists, gathered = lax.optimization_barrier((lists, gathered))
        full_dirs = interpolate(gathered, theta_map, phi_map)
        summed = shift_sum(full_dirs, cos_table, sin_table)
        parts.append(lax.all_to_all(summed, "dir", split_axis=2, concat_axis=0, tiled=True))
    send(chunks - 1, parts[-1])
    items = pair_items(lists, pair_near, pair_far, pair_class, pair_live, box_dev, classes)
    aggregated = jnp.concatenate(parts, axis=0) if chunks > 1 else parts[0]
    incoming = translate_pairs(items, trans_table, blocks, offsets, box_dev)
    return (aggregated, incoming)


def solution(mesh):
    placed = (
        P("box", None, "dir", None),
        P("box"),
        P(),
        P(None, None, "dir", None),
        P("box"),
        P("box"),
        P("box"),
        P("box"),
    )
    return jax.shard_map(
        body,
        mesh=mesh,
        in_specs=placed,
        out_specs=(P("box", None, "dir", None), P("box", None, "dir", None)),
        check_vma=False,
    )
```

```python
import functools
import math

import jax
import jax.numpy as jnp
from jax import lax
from jax.experimental import pallas as pl
from jax.experimental.pallas import tpu as pltpu
from jax.sharding import PartitionSpec as P

REACH = 2
THETA1 = 128
PHI1 = 128
THETA2 = 256
PHI2 = 256
ROWS = 16


HIGHEST = lax.Precision.HIGHEST


def passed_along(value, axis, steps):
    count = lax.axis_size(axis)
    first, last = (max(0, -steps), min(count, count - steps))
    return lax.ppermute(value, axis, [(source, source + steps) for source in range(first, last)])


def interp_rows(size_in, size_out, count):
    target_pos = jnp.arange(count, dtype=jnp.int32)
    source_pos = jnp.arange(size_in, dtype=jnp.int32)
    offset = target_pos[:, None] - 2 * source_pos[None, :]
    is_odd = offset % 2 == 1
    safe_off = jnp.where(is_odd, offset, 1).astype(jnp.float32)
    kernel = jnp.sin(math.pi * safe_off / 2.0) / (size_in * jnp.tan(math.pi * safe_off / size_out))
    inner = jnp.where(is_odd, kernel, jnp.zeros_like(kernel))
    return jnp.where(offset == 0, jnp.ones_like(kernel), inner)


def interpolate(fields, theta_map, phi_map):
    widened = jnp.einsum("...t,ut->...u", fields, theta_map, precision=HIGHEST)
    return jnp.einsum("qp,...pu->...qu", phi_map, widened, precision=HIGHEST)


def select_rows(indices, table):
    count = table.shape[0]
    flat_ids = indices.reshape(-1)
    row_ids = jnp.arange(count, dtype=jnp.int32)
    onehot = (flat_ids[:, None] == row_ids[None, :]).astype(table.dtype)
    flat_table = table.reshape(count, -1)
    picked = jnp.dot(onehot, flat_table, precision=HIGHEST, preferred_element_type=jnp.float32)
    return picked.reshape(indices.shape + table.shape[1:])


def shift_sum(fields, cos_table, sin_table):
    groups = fields.shape[0]
    cosine = cos_table[None, :, None]
    sine = sin_table[None, :, None]
    shaped = fields.reshape(groups, 8, 2, 2, fields.shape[3], fields.shape[4])
    real_part = shaped[:, :, :, 0]
    imag_part = shaped[:, :, :, 1]
    new_real = jnp.sum(cosine * real_part - sine * imag_part, axis=1)
    new_imag = jnp.sum(sine * real_part + cosine * imag_part, axis=1)
    return jnp.stack([new_real, new_imag], axis=2).reshape(
        groups, 4, fields.shape[3], fields.shape[4]
    )


def pair_kernel(offsets, tgt_ref, src_ref, cls_ref, live_ref, table_hbm, *rest):
    blocks = rest[:-6]
    out_hbm, table, sources, acc, sems, out_sem = rest[-6:]
    rows = table.shape[2]
    copies = [pltpu.make_async_copy(table_hbm, table, sems.at[0])]
    for b, (block, first) in enumerate(zip(blocks, offsets)):
        copies.append(
            pltpu.make_async_copy(block, sources.at[pl.ds(first, block.shape[0])], sems.at[b + 1])
        )
    for c in copies:
        c.start()
    acc[...] = jnp.zeros_like(acc)
    for c in copies:
        c.wait()

    def item(i, carry):
        @pl.when(live_ref[i] != 0)
        def _():
            t = tgt_ref[i]
            s = src_ref[i]
            k = cls_ref[i]

            def chunk(j, inner):
                r0 = pl.multiple_of(j * ROWS, ROWS)
                win = pl.ds(r0, ROWS)
                tr = table[k, 0, win, :].astype(jnp.float32)
                ti = table[k, 1, win, :].astype(jnp.float32)
                for q in range(2):
                    pr = sources[s, 2 * q, win, :]
                    pi = sources[s, 2 * q + 1, win, :]
                    acc[t, 2 * q, win, :] += tr * pr - ti * pi
                    acc[t, 2 * q + 1, win, :] += ti * pr + tr * pi
                return inner

            lax.fori_loop(0, rows // ROWS, chunk, 0, unroll=True)

        return carry

    lax.fori_loop(0, tgt_ref.shape[0], item, 0)
    done = pltpu.make_async_copy(acc, out_hbm, out_sem.at[0])
    done.start()
    done.wait()


def translate_pairs(items, trans_table, blocks, offsets, box_dev):
    tgt, src, cls, live = items
    shape = (box_dev,) + blocks[0].shape[1:]
    smem = pl.BlockSpec(memory_space=pltpu.SMEM)
    anywhere = pl.BlockSpec(memory_space=pl.ANY)
    return pl.pallas_call(
        functools.partial(pair_kernel, tuple(offsets)),
        out_shape=jax.ShapeDtypeStruct(shape, jnp.float32),
        in_specs=[smem] * 4 + [anywhere] * (1 + len(blocks)),
        out_specs=anywhere,
        scratch_shapes=[
            pltpu.VMEM(trans_table.shape, trans_table.dtype),
            pltpu.VMEM(((2 * REACH + 1) * box_dev,) + shape[1:], jnp.float32),
            pltpu.VMEM(shape, jnp.float32),
            pltpu.SemaphoreType.DMA((1 + len(blocks),)),
            pltpu.SemaphoreType.DMA((1,)),
        ],
        compiler_params=pltpu.CompilerParams(vmem_limit_bytes=66_000_000),
    )(tgt, src, cls, live, trans_table, *blocks)


def pair_lists(pair_near, pair_far, pair_class, pair_live):
    packed = jnp.stack([pair_near, pair_far, pair_class, pair_live])
    return [packed] + [passed_along(packed, "box", o) for o in range(1, REACH + 1)]


def pair_items(lists, pair_near, pair_far, pair_class, pair_live, box_dev, classes):
    tgt = [pair_near]
    src = [pair_far]
    cls = [pair_class]
    live = [pair_live]
    for o, lst in enumerate(lists):
        near, far, k, alive = lst[0], lst[1], lst[2], lst[3]
        tgt.append(far - o * box_dev)
        base = 0 if o == 0 else (REACH + o) * box_dev
        src.append(near + base)
        cls.append((k + classes // 2) % classes)
        live.append(jnp.where(far // box_dev == o, alive, 0))
    return [jnp.concatenate(x).astype(jnp.int32) for x in (tgt, src, cls, live)]


def body(
    child_pattern, octant, shift_angle, trans_table, pair_near, pair_far, pair_class, pair_live
):
    dir_count = lax.axis_size("dir")
    dir_index = lax.axis_index("dir")
    box_dev = child_pattern.shape[0] // 8
    classes = trans_table.shape[0]
    lists = pair_lists(pair_near, pair_far, pair_class, pair_live)
    theta_map = interp_rows(THETA1, THETA2, THETA2)
    phi_map = interp_rows(PHI1, PHI2, PHI2)
    cos_table = jnp.cos(shift_angle)
    sin_table = jnp.sin(shift_angle)
    grouped = child_pattern.reshape(box_dev, 8, 4, PHI1 // dir_count, THETA1)
    octants = octant.reshape(box_dev, 8)
    slots = jnp.arange(8, dtype=jnp.int32)
    by_octant = jnp.sum(
        jnp.where(octants[:, :, None] == slots[None, None, :], slots[None, :, None], 0), axis=1
    )
    grouped = jnp.take_along_axis(grouped, by_octant[:, :, None, None, None], axis=1)
    chunks = 1
    while chunks < 4 and box_dev % (2 * chunks * dir_count) == 0:
        chunks *= 2
    per_chunk = box_dev // chunks
    per_dev = per_chunk // dir_count
    parts = []
    blocks = []
    offsets = []

    def send(c, part):
        moved = [part]
        moved += [passed_along(part, "box", -o) for o in range(1, REACH + 1)]
        moved += [passed_along(part, "box", o) for o in range(1, REACH + 1)]
        for b, block in enumerate(moved):
            blocks.append(block)
            offsets.append(b * box_dev + c * per_chunk)

    for c in range(chunks):
        piece = grouped[c * per_chunk : (c + 1) * per_chunk]
        gathered = lax.all_to_all(piece, "dir", split_axis=0, concat_axis=3, tiled=True)
        if c >= 2:
            lo = (c - 2) * (2 * REACH + 1) + 1
            hi = (c - 1) * (2 * REACH + 1)
            sent, gathered = lax.optimization_barrier((blocks[lo:hi], gathered))
            blocks[lo:hi] = sent
        if parts:
            parts[-1], gathered = lax.optimization_barrier((parts[-1], gathered))
            send(c - 1, parts[-1])
        else:
            lists, gathered = lax.optimization_barrier((lists, gathered))
        full_dirs = interpolate(gathered, theta_map, phi_map)
        summed = shift_sum(full_dirs, cos_table, sin_table)
        parts.append(lax.all_to_all(summed, "dir", split_axis=2, concat_axis=0, tiled=True))
    send(chunks - 1, parts[-1])
    items = pair_items(lists, pair_near, pair_far, pair_class, pair_live, box_dev, classes)
    aggregated = jnp.concatenate(parts, axis=0) if chunks > 1 else parts[0]
    incoming = translate_pairs(items, trans_table, blocks, offsets, box_dev)
    return (aggregated, incoming)


def solution(mesh):
    placed = (
        P("box", None, "dir", None),
        P("box"),
        P(),
        P(None, None, "dir", None),
        P("box"),
        P("box"),
        P("box"),
        P("box"),
    )
    return jax.shard_map(
        body,
        mesh=mesh,
        in_specs=placed,
        out_specs=(P("box", None, "dir", None), P("box", None, "dir", None)),
        check_vma=False,
    )
```

```python
import functools
import math

import jax
import jax.numpy as jnp
from jax import lax
from jax.experimental import pallas as pl
from jax.experimental.pallas import tpu as pltpu
from jax.sharding import PartitionSpec as P

REACH = 2
THETA1 = 128
PHI1 = 128
THETA2 = 256
PHI2 = 256
ROWS = 16


HIGHEST = lax.Precision.HIGHEST


def passed_along(value, axis, steps):
    count = lax.axis_size(axis)
    first, last = (max(0, -steps), min(count, count - steps))
    return lax.ppermute(value, axis, [(source, source + steps) for source in range(first, last)])


def interp_rows(size_in, size_out, count):
    target_pos = jnp.arange(count, dtype=jnp.int32)
    source_pos = jnp.arange(size_in, dtype=jnp.int32)
    offset = target_pos[:, None] - 2 * source_pos[None, :]
    is_odd = offset % 2 == 1
    safe_off = jnp.where(is_odd, offset, 1).astype(jnp.float32)
    kernel = jnp.sin(math.pi * safe_off / 2.0) / (size_in * jnp.tan(math.pi * safe_off / size_out))
    inner = jnp.where(is_odd, kernel, jnp.zeros_like(kernel))
    return jnp.where(offset == 0, jnp.ones_like(kernel), inner)


def interpolate(fields, theta_map, phi_map):
    widened = jnp.einsum("...t,ut->...u", fields, theta_map, precision=HIGHEST)
    return jnp.einsum("qp,...pu->...qu", phi_map, widened, precision=HIGHEST)


def select_rows(indices, table):
    count = table.shape[0]
    flat_ids = indices.reshape(-1)
    row_ids = jnp.arange(count, dtype=jnp.int32)
    onehot = (flat_ids[:, None] == row_ids[None, :]).astype(table.dtype)
    flat_table = table.reshape(count, -1)
    picked = jnp.dot(onehot, flat_table, precision=HIGHEST, preferred_element_type=jnp.float32)
    return picked.reshape(indices.shape + table.shape[1:])


def shift_sum(fields, cos_table, sin_table):
    groups = fields.shape[0]
    cosine = cos_table[None, :, None]
    sine = sin_table[None, :, None]
    shaped = fields.reshape(groups, 8, 2, 2, fields.shape[3], fields.shape[4])
    real_part = shaped[:, :, :, 0]
    imag_part = shaped[:, :, :, 1]
    new_real = jnp.sum(cosine * real_part - sine * imag_part, axis=1)
    new_imag = jnp.sum(sine * real_part + cosine * imag_part, axis=1)
    return jnp.stack([new_real, new_imag], axis=2).reshape(
        groups, 4, fields.shape[3], fields.shape[4]
    )


def pair_kernel(offsets, has_init, tgt_ref, src_ref, cls_ref, live_ref, table_hbm, *rest):
    blocks = rest[: len(offsets)]
    out_hbm, table, sources, acc, sems, out_sem = rest[-6:]
    rows = table.shape[2]
    copies = [pltpu.make_async_copy(table_hbm, table, sems.at[0])]
    for b, (block, first) in enumerate(zip(blocks, offsets)):
        copies.append(
            pltpu.make_async_copy(block, sources.at[pl.ds(first, block.shape[0])], sems.at[b + 1])
        )
    if has_init:
        copies.append(pltpu.make_async_copy(rest[len(offsets)], acc, sems.at[len(blocks) + 1]))
    for c in copies:
        c.start()
    if not has_init:
        acc[...] = jnp.zeros_like(acc)
    for c in copies:
        c.wait()

    def item(i, carry):
        @pl.when(live_ref[i] != 0)
        def _():
            t = tgt_ref[i]
            s = src_ref[i]
            k = cls_ref[i]

            def chunk(j, inner):
                r0 = pl.multiple_of(j * ROWS, ROWS)
                win = pl.ds(r0, ROWS)
                tr = table[k, 0, win, :].astype(jnp.float32)
                ti = table[k, 1, win, :].astype(jnp.float32)
                for q in range(2):
                    pr = sources[s, 2 * q, win, :]
                    pi = sources[s, 2 * q + 1, win, :]
                    acc[t, 2 * q, win, :] += tr * pr - ti * pi
                    acc[t, 2 * q + 1, win, :] += ti * pr + tr * pi
                return inner

            lax.fori_loop(0, rows // ROWS, chunk, 0, unroll=True)

        return carry

    lax.fori_loop(0, tgt_ref.shape[0], item, 0)
    done = pltpu.make_async_copy(acc, out_hbm, out_sem.at[0])
    done.start()
    done.wait()


def translate_pairs(items, trans_table, blocks, offsets, box_dev, init=None):
    tgt, src, cls, live = items
    shape = (box_dev,) + blocks[0].shape[1:]
    smem = pl.BlockSpec(memory_space=pltpu.SMEM)
    anywhere = pl.BlockSpec(memory_space=pl.ANY)
    extra = [] if init is None else [init]
    size = math.prod(shape)
    cost = pl.CostEstimate(
        flops=8 * size * tgt.shape[0] // 4,
        transcendentals=0,
        bytes_accessed=trans_table.size * 2 + 4 * size * (len(blocks) + 2),
    )
    return pl.pallas_call(
        functools.partial(pair_kernel, tuple(offsets), init is not None),
        out_shape=jax.ShapeDtypeStruct(shape, jnp.float32),
        in_specs=[smem] * 4 + [anywhere] * (1 + len(blocks) + len(extra)),
        out_specs=anywhere,
        scratch_shapes=[
            pltpu.VMEM(trans_table.shape, trans_table.dtype),
            pltpu.VMEM(((2 * REACH + 1) * box_dev,) + shape[1:], jnp.float32),
            pltpu.VMEM(shape, jnp.float32),
            pltpu.SemaphoreType.DMA((2 + len(blocks),)),
            pltpu.SemaphoreType.DMA((1,)),
        ],
        input_output_aliases={} if init is None else {5 + len(blocks): 0},
        cost_estimate=cost,
        compiler_params=pltpu.CompilerParams(vmem_limit_bytes=66_000_000),
    )(tgt, src, cls, live, trans_table, *blocks, *extra)


def pair_lists(pair_near, pair_far, pair_class, pair_live):
    packed = jnp.stack([pair_near, pair_far, pair_class, pair_live])
    return [packed] + [passed_along(packed, "box", o) for o in range(1, REACH + 1)]


def pair_items(lists, pair_near, pair_far, pair_class, pair_live, box_dev, classes):
    tgt = [pair_near]
    src = [pair_far]
    cls = [pair_class]
    live = [pair_live]
    for o, lst in enumerate(lists):
        near, far, k, alive = lst[0], lst[1], lst[2], lst[3]
        tgt.append(far - o * box_dev)
        base = 0 if o == 0 else (REACH + o) * box_dev
        src.append(near + base)
        cls.append((k + classes // 2) % classes)
        live.append(jnp.where(far // box_dev == o, alive, 0))
    return [jnp.concatenate(x).astype(jnp.int32) for x in (tgt, src, cls, live)]


def body(
    child_pattern, octant, shift_angle, trans_table, pair_near, pair_far, pair_class, pair_live
):
    dir_count = lax.axis_size("dir")
    dir_index = lax.axis_index("dir")
    box_dev = child_pattern.shape[0] // 8
    classes = trans_table.shape[0]
    lists = pair_lists(pair_near, pair_far, pair_class, pair_live)
    theta_map = interp_rows(THETA1, THETA2, THETA2)
    phi_map = interp_rows(PHI1, PHI2, PHI2)
    cos_table = jnp.cos(shift_angle)
    sin_table = jnp.sin(shift_angle)
    grouped = child_pattern.reshape(box_dev, 8, 4, PHI1 // dir_count, THETA1)
    octants = octant.reshape(box_dev, 8)
    slots = jnp.arange(8, dtype=jnp.int32)
    by_octant = jnp.sum(
        jnp.where(octants[:, :, None] == slots[None, None, :], slots[None, :, None], 0), axis=1
    )
    grouped = jnp.take_along_axis(grouped, by_octant[:, :, None, None, None], axis=1)
    chunks = 1
    while chunks < 4 and box_dev % (2 * chunks * dir_count) == 0:
        chunks *= 2
    per_chunk = box_dev // chunks
    per_dev = per_chunk // dir_count
    parts = []
    blocks = []
    offsets = []

    def send(c, part):
        moved = [part]
        moved += [passed_along(part, "box", -o) for o in range(1, REACH + 1)]
        moved += [passed_along(part, "box", o) for o in range(1, REACH + 1)]
        for b, block in enumerate(moved):
            blocks.append(block)
            offsets.append(b * box_dev + c * per_chunk)

    for c in range(chunks):
        piece = grouped[c * per_chunk : (c + 1) * per_chunk]
        gathered = lax.all_to_all(piece, "dir", split_axis=0, concat_axis=3, tiled=True)
        if c >= 2:
            lo = (c - 2) * (2 * REACH + 1) + 1
            hi = (c - 1) * (2 * REACH + 1)
            sent, gathered = lax.optimization_barrier((blocks[lo:hi], gathered))
            blocks[lo:hi] = sent
        if parts:
            parts[-1], gathered = lax.optimization_barrier((parts[-1], gathered))
            send(c - 1, parts[-1])
        else:
            lists, gathered = lax.optimization_barrier((lists, gathered))
        full_dirs = interpolate(gathered, theta_map, phi_map)
        summed = shift_sum(full_dirs, cos_table, sin_table)
        parts.append(lax.all_to_all(summed, "dir", split_axis=2, concat_axis=0, tiled=True))
    send(chunks - 1, parts[-1])
    items = pair_items(lists, pair_near, pair_far, pair_class, pair_live, box_dev, classes)
    aggregated = jnp.concatenate(parts, axis=0) if chunks > 1 else parts[0]
    tgt, src, cls, live = items
    late = (src >= box_dev) & (src % box_dev >= (chunks - 1) * per_chunk)
    early_items = (tgt, src, cls, jnp.where(late, 0, live))
    late_items = (tgt, src, cls, jnp.where(late, live, 0))
    cut = len(blocks) - 2 * REACH
    partial = translate_pairs(early_items, trans_table, blocks[:cut], offsets[:cut], box_dev)
    incoming = translate_pairs(
        late_items, trans_table, blocks[cut:], offsets[cut:], box_dev, init=partial
    )
    return (aggregated, incoming)


def solution(mesh):
    placed = (
        P("box", None, "dir", None),
        P("box"),
        P(),
        P(None, None, "dir", None),
        P("box"),
        P("box"),
        P("box"),
        P("box"),
    )
    return jax.shard_map(
        body,
        mesh=mesh,
        in_specs=placed,
        out_specs=(P("box", None, "dir", None), P("box", None, "dir", None)),
        check_vma=False,
    )
```

```python
import functools
import math

import jax
import jax.numpy as jnp
from jax import lax
from jax.experimental import pallas as pl
from jax.experimental.pallas import tpu as pltpu
from jax.sharding import PartitionSpec as P

REACH = 2
THETA1 = 128
PHI1 = 128
THETA2 = 256
PHI2 = 256
ROWS = 16
TABLE_PIECES = 4


HIGHEST = lax.Precision.HIGHEST


def passed_along(value, axis, steps):
    count = lax.axis_size(axis)
    first, last = (max(0, -steps), min(count, count - steps))
    return lax.ppermute(value, axis, [(source, source + steps) for source in range(first, last)])


def interp_rows(size_in, size_out, count):
    target_pos = jnp.arange(count, dtype=jnp.int32)
    source_pos = jnp.arange(size_in, dtype=jnp.int32)
    offset = target_pos[:, None] - 2 * source_pos[None, :]
    is_odd = offset % 2 == 1
    safe_off = jnp.where(is_odd, offset, 1).astype(jnp.float32)
    kernel = jnp.sin(math.pi * safe_off / 2.0) / (size_in * jnp.tan(math.pi * safe_off / size_out))
    inner = jnp.where(is_odd, kernel, jnp.zeros_like(kernel))
    return jnp.where(offset == 0, jnp.ones_like(kernel), inner)


def interpolate(fields, theta_map, phi_map):
    widened = jnp.einsum("...t,ut->...u", fields, theta_map, precision=HIGHEST)
    return jnp.einsum("qp,...pu->...qu", phi_map, widened, precision=HIGHEST)


def select_rows(indices, table):
    count = table.shape[0]
    flat_ids = indices.reshape(-1)
    row_ids = jnp.arange(count, dtype=jnp.int32)
    onehot = (flat_ids[:, None] == row_ids[None, :]).astype(table.dtype)
    flat_table = table.reshape(count, -1)
    picked = jnp.dot(onehot, flat_table, precision=HIGHEST, preferred_element_type=jnp.float32)
    return picked.reshape(indices.shape + table.shape[1:])


def shift_sum(fields, cos_table, sin_table):
    groups = fields.shape[0]
    cosine = cos_table[None, :, None]
    sine = sin_table[None, :, None]
    shaped = fields.reshape(groups, 8, 2, 2, fields.shape[3], fields.shape[4])
    real_part = shaped[:, :, :, 0]
    imag_part = shaped[:, :, :, 1]
    new_real = jnp.sum(cosine * real_part - sine * imag_part, axis=1)
    new_imag = jnp.sum(sine * real_part + cosine * imag_part, axis=1)
    return jnp.stack([new_real, new_imag], axis=2).reshape(
        groups, 4, fields.shape[3], fields.shape[4]
    )


def pair_kernel(offsets, has_init, tgt_ref, src_ref, cls_ref, span_ref, table_hbm, *rest):
    blocks = rest[: len(offsets)]
    out_hbm, table, sources, acc, sems, out_sem = rest[-6:]
    rows = table.shape[2]
    classes = table.shape[0]
    pieces = [(p * classes // TABLE_PIECES, (p + 1) * classes // TABLE_PIECES) for p in range(TABLE_PIECES)]
    copies = [
        pltpu.make_async_copy(table_hbm.at[pl.ds(a, b - a)], table.at[pl.ds(a, b - a)], sems.at[p])
        for p, (a, b) in enumerate(pieces)
    ]
    for b, (block, first) in enumerate(zip(blocks, offsets)):
        copies.append(
            pltpu.make_async_copy(
                block, sources.at[pl.ds(first, block.shape[0])], sems.at[TABLE_PIECES + b]
            )
        )
    if has_init:
        copies.append(
            pltpu.make_async_copy(rest[len(offsets)], acc, sems.at[TABLE_PIECES + len(blocks)])
        )
    for c in copies:
        c.start()
    if not has_init:
        acc[...] = jnp.zeros_like(acc)
    for c in copies:
        c.wait()

    def item(i, carry):
        if True:
            t = tgt_ref[i]
            s = src_ref[i]
            k = cls_ref[i]

            def chunk(j, inner):
                r0 = pl.multiple_of(j * ROWS, ROWS)
                win = pl.ds(r0, ROWS)
                tr = table[k, 0, win, :].astype(jnp.float32)
                ti = table[k, 1, win, :].astype(jnp.float32)
                for q in range(2):
                    pr = sources[s, 2 * q, win, :]
                    pi = sources[s, 2 * q + 1, win, :]
                    acc[t, 2 * q, win, :] += tr * pr - ti * pi
                    acc[t, 2 * q + 1, win, :] += ti * pr + tr * pi
                return inner

            lax.fori_loop(0, rows // ROWS, chunk, 0, unroll=True)

        return carry

    lax.fori_loop(span_ref[0], span_ref[1], item, 0)
    done = pltpu.make_async_copy(acc, out_hbm, out_sem.at[0])
    done.start()
    done.wait()


def translate_pairs(items, trans_table, blocks, offsets, box_dev, init=None):
    tgt, src, cls, span = items
    shape = (box_dev,) + blocks[0].shape[1:]
    smem = pl.BlockSpec(memory_space=pltpu.SMEM)
    anywhere = pl.BlockSpec(memory_space=pl.ANY)
    extra = [] if init is None else [init]
    size = math.prod(shape)
    cost = pl.CostEstimate(
        flops=8 * size * tgt.shape[0] // 4,
        transcendentals=0,
        bytes_accessed=trans_table.size * 2 + 4 * size * (len(blocks) + 2),
    )
    return pl.pallas_call(
        functools.partial(pair_kernel, tuple(offsets), init is not None),
        out_shape=jax.ShapeDtypeStruct(shape, jnp.float32),
        in_specs=[smem] * 4 + [anywhere] * (1 + len(blocks) + len(extra)),
        out_specs=anywhere,
        scratch_shapes=[
            pltpu.VMEM(trans_table.shape, trans_table.dtype),
            pltpu.VMEM(((2 * REACH + 1) * box_dev,) + shape[1:], jnp.float32),
            pltpu.VMEM(shape, jnp.float32),
            pltpu.SemaphoreType.DMA((TABLE_PIECES + 1 + len(blocks),)),
            pltpu.SemaphoreType.DMA((1,)),
        ],
        input_output_aliases={} if init is None else {5 + len(blocks): 0},
        cost_estimate=cost,
        compiler_params=pltpu.CompilerParams(vmem_limit_bytes=66_000_000),
    )(tgt, src, cls, span, trans_table, *blocks, *extra)


def pair_lists(pair_near, pair_far, pair_class, pair_live):
    packed = jnp.stack([pair_near, pair_far, pair_class, pair_live])
    return [packed] + [passed_along(packed, "box", o) for o in range(1, REACH + 1)]


def pair_items(lists, pair_near, pair_far, pair_class, pair_live, box_dev, classes):
    tgt = [pair_near]
    src = [pair_far]
    cls = [pair_class]
    live = [pair_live]
    for o, lst in enumerate(lists):
        near, far, k, alive = lst[0], lst[1], lst[2], lst[3]
        tgt.append(far - o * box_dev)
        base = 0 if o == 0 else (REACH + o) * box_dev
        src.append(near + base)
        cls.append((k + classes // 2) % classes)
        live.append(jnp.where(far // box_dev == o, alive, 0))
    return [jnp.concatenate(x).astype(jnp.int32) for x in (tgt, src, cls, live)]


def body(
    child_pattern, octant, shift_angle, trans_table, pair_near, pair_far, pair_class, pair_live
):
    dir_count = lax.axis_size("dir")
    dir_index = lax.axis_index("dir")
    box_dev = child_pattern.shape[0] // 8
    classes = trans_table.shape[0]
    lists = pair_lists(pair_near, pair_far, pair_class, pair_live)
    theta_map = interp_rows(THETA1, THETA2, THETA2)
    phi_map = interp_rows(PHI1, PHI2, PHI2)
    cos_table = jnp.cos(shift_angle)
    sin_table = jnp.sin(shift_angle)
    grouped = child_pattern.reshape(box_dev, 8, 4, PHI1 // dir_count, THETA1)
    octants = octant.reshape(box_dev, 8)
    slots = jnp.arange(8, dtype=jnp.int32)
    by_octant = jnp.sum(
        jnp.where(octants[:, :, None] == slots[None, None, :], slots[None, :, None], 0), axis=1
    )
    chunks = 1
    while chunks < 4 and box_dev % (2 * chunks * dir_count) == 0:
        chunks *= 2
    per_chunk = box_dev // chunks
    per_dev = per_chunk // dir_count
    parts = []
    blocks = []
    offsets = []

    def send(c, part):
        moved = [part]
        moved += [passed_along(part, "box", -o) for o in range(1, REACH + 1)]
        moved += [passed_along(part, "box", o) for o in range(1, REACH + 1)]
        for b, block in enumerate(moved):
            blocks.append(block)
            offsets.append(b * box_dev + c * per_chunk)

    for c in range(chunks):
        piece = jnp.take_along_axis(
            grouped[c * per_chunk : (c + 1) * per_chunk],
            by_octant[c * per_chunk : (c + 1) * per_chunk, :, None, None, None],
            axis=1,
        )
        gathered = lax.all_to_all(piece, "dir", split_axis=0, concat_axis=3, tiled=True)
        if c >= 2:
            lo = (c - 2) * (2 * REACH + 1) + 1
            hi = (c - 1) * (2 * REACH + 1)
            sent, gathered = lax.optimization_barrier((blocks[lo:hi], gathered))
            blocks[lo:hi] = sent
        if parts:
            parts[-1], gathered = lax.optimization_barrier((parts[-1], gathered))
            send(c - 1, parts[-1])
        else:
            lists, gathered = lax.optimization_barrier((lists, gathered))
        full_dirs = interpolate(gathered, theta_map, phi_map)
        summed = shift_sum(full_dirs, cos_table, sin_table)
        parts.append(lax.all_to_all(summed, "dir", split_axis=2, concat_axis=0, tiled=True))
    send(chunks - 1, parts[-1])
    items = pair_items(lists, pair_near, pair_far, pair_class, pair_live, box_dev, classes)
    aggregated = jnp.concatenate(parts, axis=0) if chunks > 1 else parts[0]
    tgt, src, cls, live = items
    late = (src >= box_dev) & (src % box_dev >= (chunks - 1) * per_chunk)
    key = jnp.where(live != 0, late.astype(jnp.int32), 2)
    order = jnp.argsort(key, stable=True)
    tgt, src, cls = (jnp.take(x, order) for x in (tgt, src, cls))
    n_early = jnp.sum(key == 0).astype(jnp.int32)
    n_live = n_early + jnp.sum(key == 1).astype(jnp.int32)
    early_items = (tgt, src, cls, jnp.stack([jnp.int32(0), n_early]))
    late_items = (tgt, src, cls, jnp.stack([n_early, n_live]))
    cut = len(blocks) - 2 * REACH
    partial = translate_pairs(early_items, trans_table, blocks[:cut], offsets[:cut], box_dev)
    incoming = translate_pairs(
        late_items, trans_table, blocks[cut:], offsets[cut:], box_dev, init=partial
    )
    return (aggregated, incoming)


def solution(mesh):
    placed = (
        P("box", None, "dir", None),
        P("box"),
        P(),
        P(None, None, "dir", None),
        P("box"),
        P("box"),
        P("box"),
        P("box"),
    )
    return jax.shard_map(
        body,
        mesh=mesh,
        in_specs=placed,
        out_specs=(P("box", None, "dir", None), P("box", None, "dir", None)),
        check_vma=False,
    )
```

```python
import functools
import math

import jax
import jax.numpy as jnp
from jax import lax
from jax.experimental import pallas as pl
from jax.experimental.pallas import tpu as pltpu
from jax.sharding import PartitionSpec as P

REACH = 2
THETA1 = 128
PHI1 = 128
THETA2 = 256
PHI2 = 256
ROWS = 16
TABLE_PIECES = 4


HIGHEST = lax.Precision.HIGHEST


def passed_along(value, axis, steps):
    count = lax.axis_size(axis)
    first, last = (max(0, -steps), min(count, count - steps))
    return lax.ppermute(value, axis, [(source, source + steps) for source in range(first, last)])


def interp_rows(size_in, size_out, count):
    target_pos = jnp.arange(count, dtype=jnp.int32)
    source_pos = jnp.arange(size_in, dtype=jnp.int32)
    offset = target_pos[:, None] - 2 * source_pos[None, :]
    is_odd = offset % 2 == 1
    safe_off = jnp.where(is_odd, offset, 1).astype(jnp.float32)
    kernel = jnp.sin(math.pi * safe_off / 2.0) / (size_in * jnp.tan(math.pi * safe_off / size_out))
    inner = jnp.where(is_odd, kernel, jnp.zeros_like(kernel))
    return jnp.where(offset == 0, jnp.ones_like(kernel), inner)


def interpolate(fields, theta_map, phi_map):
    widened = jnp.einsum("...t,ut->...u", fields, theta_map, precision=HIGHEST)
    return jnp.einsum("qp,...pu->...qu", phi_map, widened, precision=HIGHEST)


def select_rows(indices, table):
    count = table.shape[0]
    flat_ids = indices.reshape(-1)
    row_ids = jnp.arange(count, dtype=jnp.int32)
    onehot = (flat_ids[:, None] == row_ids[None, :]).astype(table.dtype)
    flat_table = table.reshape(count, -1)
    picked = jnp.dot(onehot, flat_table, precision=HIGHEST, preferred_element_type=jnp.float32)
    return picked.reshape(indices.shape + table.shape[1:])


def shift_sum(fields, cos_table, sin_table):
    groups = fields.shape[0]
    cosine = cos_table[None, :, None]
    sine = sin_table[None, :, None]
    shaped = fields.reshape(groups, 8, 2, 2, fields.shape[3], fields.shape[4])
    real_part = shaped[:, :, :, 0]
    imag_part = shaped[:, :, :, 1]
    new_real = jnp.sum(cosine * real_part - sine * imag_part, axis=1)
    new_imag = jnp.sum(sine * real_part + cosine * imag_part, axis=1)
    return jnp.stack([new_real, new_imag], axis=2).reshape(
        groups, 4, fields.shape[3], fields.shape[4]
    )


def pair_kernel(offsets, has_init, tgt_ref, src_ref, cls_ref, span_ref, table_hbm, *rest):
    blocks = rest[: len(offsets)]
    out_hbm, table, sources, acc, sems, out_sem = rest[-6:]
    rows = table.shape[2]
    classes = table.shape[0]
    pieces = [(p * classes // TABLE_PIECES, (p + 1) * classes // TABLE_PIECES) for p in range(TABLE_PIECES)]
    copies = [
        pltpu.make_async_copy(table_hbm.at[pl.ds(a, b - a)], table.at[pl.ds(a, b - a)], sems.at[p])
        for p, (a, b) in enumerate(pieces)
    ]
    for b, (block, first) in enumerate(zip(blocks, offsets)):
        copies.append(
            pltpu.make_async_copy(
                block, sources.at[pl.ds(first, block.shape[0])], sems.at[TABLE_PIECES + b]
            )
        )
    if has_init:
        copies.append(
            pltpu.make_async_copy(rest[len(offsets)], acc, sems.at[TABLE_PIECES + len(blocks)])
        )
    for c in copies:
        c.start()
    if not has_init:
        acc[...] = jnp.zeros_like(acc)
    for c in copies:
        c.wait()

    def item(i, carry):
        if True:
            t = tgt_ref[i]
            s = src_ref[i]
            k = cls_ref[i]

            def chunk(j, inner):
                r0 = pl.multiple_of(j * ROWS, ROWS)
                win = pl.ds(r0, ROWS)
                tr = table[k, 0, win, :].astype(jnp.float32)
                ti = table[k, 1, win, :].astype(jnp.float32)
                for q in range(2):
                    pr = sources[s, 2 * q, win, :]
                    pi = sources[s, 2 * q + 1, win, :]
                    acc[t, 2 * q, win, :] += tr * pr - ti * pi
                    acc[t, 2 * q + 1, win, :] += ti * pr + tr * pi
                return inner

            lax.fori_loop(0, rows // ROWS, chunk, 0, unroll=True)

        return carry

    lax.fori_loop(span_ref[0], span_ref[1], item, 0)
    done = pltpu.make_async_copy(acc, out_hbm, out_sem.at[0])
    done.start()
    done.wait()


def translate_pairs(items, trans_table, blocks, offsets, box_dev, init=None):
    tgt, src, cls, span = items
    shape = (box_dev,) + blocks[0].shape[1:]
    smem = pl.BlockSpec(memory_space=pltpu.SMEM)
    anywhere = pl.BlockSpec(memory_space=pl.ANY)
    extra = [] if init is None else [init]
    size = math.prod(shape)
    cost = pl.CostEstimate(
        flops=8 * size * tgt.shape[0] // 4,
        transcendentals=0,
        bytes_accessed=trans_table.size * 2 + 4 * size * (len(blocks) + 2),
    )
    return pl.pallas_call(
        functools.partial(pair_kernel, tuple(offsets), init is not None),
        out_shape=jax.ShapeDtypeStruct(shape, jnp.float32),
        in_specs=[smem] * 4 + [anywhere] * (1 + len(blocks) + len(extra)),
        out_specs=anywhere,
        scratch_shapes=[
            pltpu.VMEM(trans_table.shape, trans_table.dtype),
            pltpu.VMEM(((2 * REACH + 1) * box_dev,) + shape[1:], jnp.float32),
            pltpu.VMEM(shape, jnp.float32),
            pltpu.SemaphoreType.DMA((TABLE_PIECES + 1 + len(blocks),)),
            pltpu.SemaphoreType.DMA((1,)),
        ],
        input_output_aliases={} if init is None else {5 + len(blocks): 0},
        cost_estimate=cost,
        compiler_params=pltpu.CompilerParams(vmem_limit_bytes=66_000_000),
    )(tgt, src, cls, span, trans_table, *blocks, *extra)


def pair_lists(pair_near, pair_far, pair_class, pair_live):
    packed = jnp.stack([pair_near, pair_far, pair_class, pair_live])
    return [packed] + [passed_along(packed, "box", o) for o in range(1, REACH + 1)]


def pair_items(lists, pair_near, pair_far, pair_class, pair_live, box_dev, classes):
    tgt = [pair_near]
    src = [pair_far]
    cls = [pair_class]
    live = [pair_live]
    for o, lst in enumerate(lists):
        near, far, k, alive = lst[0], lst[1], lst[2], lst[3]
        tgt.append(far - o * box_dev)
        base = 0 if o == 0 else (REACH + o) * box_dev
        src.append(near + base)
        cls.append((k + classes // 2) % classes)
        live.append(jnp.where(far // box_dev == o, alive, 0))
    return [jnp.concatenate(x).astype(jnp.int32) for x in (tgt, src, cls, live)]


def body(
    child_pattern, octant, shift_angle, trans_table, pair_near, pair_far, pair_class, pair_live
):
    dir_count = lax.axis_size("dir")
    dir_index = lax.axis_index("dir")
    box_dev = child_pattern.shape[0] // 8
    classes = trans_table.shape[0]
    lists = pair_lists(pair_near, pair_far, pair_class, pair_live)
    theta_map = interp_rows(THETA1, THETA2, THETA2)
    phi_map = interp_rows(PHI1, PHI2, PHI2)
    cos_table = jnp.cos(shift_angle)
    sin_table = jnp.sin(shift_angle)
    grouped = child_pattern.reshape(box_dev, 8, 4, PHI1 // dir_count, THETA1)
    octants = octant.reshape(box_dev, 8)
    slots = jnp.arange(8, dtype=jnp.int32)
    by_octant = jnp.sum(
        jnp.where(octants[:, :, None] == slots[None, None, :], slots[None, :, None], 0), axis=1
    )
    chunks = 1
    while chunks < 4 and box_dev % (2 * chunks * dir_count) == 0:
        chunks *= 2
    per_chunk = box_dev // chunks
    per_dev = per_chunk // dir_count
    parts = []
    blocks = []
    offsets = []
    prepared = None

    def prepare(lists):
        tgt, src, cls, live = pair_items(
            lists, pair_near, pair_far, pair_class, pair_live, box_dev, classes
        )
        late = (src >= box_dev) & (src % box_dev >= (chunks - 1) * per_chunk)
        key = jnp.where(live != 0, late.astype(jnp.int32), 2)
        order = jnp.argsort(key, stable=True)
        tgt, src, cls = jnp.take(jnp.stack([tgt, src, cls]), order, axis=1)
        n_early = jnp.sum(key == 0).astype(jnp.int32)
        n_live = n_early + jnp.sum(key == 1).astype(jnp.int32)
        return tgt, src, cls, jnp.stack([jnp.int32(0), n_early]), jnp.stack([n_early, n_live])

    def send(c, part):
        moved = [part]
        moved += [passed_along(part, "box", -o) for o in range(1, REACH + 1)]
        moved += [passed_along(part, "box", o) for o in range(1, REACH + 1)]
        for b, block in enumerate(moved):
            blocks.append(block)
            offsets.append(b * box_dev + c * per_chunk)

    for c in range(chunks):
        piece = jnp.take_along_axis(
            grouped[c * per_chunk : (c + 1) * per_chunk],
            by_octant[c * per_chunk : (c + 1) * per_chunk, :, None, None, None],
            axis=1,
        )
        gathered = lax.all_to_all(piece, "dir", split_axis=0, concat_axis=3, tiled=True)
        if c >= 2:
            lo = (c - 2) * (2 * REACH + 1) + 1
            hi = (c - 1) * (2 * REACH + 1)
            sent, gathered = lax.optimization_barrier((blocks[lo:hi], gathered))
            blocks[lo:hi] = sent
        if parts:
            parts[-1], gathered = lax.optimization_barrier((parts[-1], gathered))
            send(c - 1, parts[-1])
        else:
            lists, gathered = lax.optimization_barrier((lists, gathered))
        if c == 1:
            prepared, gathered = lax.optimization_barrier((prepare(lists), gathered))
        full_dirs = interpolate(gathered, theta_map, phi_map)
        summed = shift_sum(full_dirs, cos_table, sin_table)
        parts.append(lax.all_to_all(summed, "dir", split_axis=2, concat_axis=0, tiled=True))
    send(chunks - 1, parts[-1])
    aggregated = jnp.concatenate(parts, axis=0) if chunks > 1 else parts[0]
    if prepared is None:
        prepared = prepare(lists)
    tgt, src, cls, early_span, late_span = prepared
    early_items = (tgt, src, cls, early_span)
    late_items = (tgt, src, cls, late_span)
    cut = len(blocks) - 2 * REACH
    partial = translate_pairs(early_items, trans_table, blocks[:cut], offsets[:cut], box_dev)
    incoming = translate_pairs(
        late_items, trans_table, blocks[cut:], offsets[cut:], box_dev, init=partial
    )
    return (aggregated, incoming)


def solution(mesh):
    placed = (
        P("box", None, "dir", None),
        P("box"),
        P(),
        P(None, None, "dir", None),
        P("box"),
        P("box"),
        P("box"),
        P("box"),
    )
    return jax.shard_map(
        body,
        mesh=mesh,
        in_specs=placed,
        out_specs=(P("box", None, "dir", None), P("box", None, "dir", None)),
        check_vma=False,
    )
```

```python
import functools
import math

import jax
import jax.numpy as jnp
from jax import lax
from jax.experimental import pallas as pl
from jax.experimental.pallas import tpu as pltpu
from jax.sharding import PartitionSpec as P

REACH = 2
THETA1 = 128
PHI1 = 128
THETA2 = 256
PHI2 = 256
ROWS = 16
TABLE_PIECES = 4


HIGHEST = lax.Precision.HIGHEST


def passed_along(value, axis, steps):
    count = lax.axis_size(axis)
    first, last = (max(0, -steps), min(count, count - steps))
    return lax.ppermute(value, axis, [(source, source + steps) for source in range(first, last)])


def interp_rows(size_in, size_out, count):
    target_pos = jnp.arange(count, dtype=jnp.int32)
    source_pos = jnp.arange(size_in, dtype=jnp.int32)
    offset = target_pos[:, None] - 2 * source_pos[None, :]
    is_odd = offset % 2 == 1
    safe_off = jnp.where(is_odd, offset, 1).astype(jnp.float32)
    kernel = jnp.sin(math.pi * safe_off / 2.0) / (size_in * jnp.tan(math.pi * safe_off / size_out))
    inner = jnp.where(is_odd, kernel, jnp.zeros_like(kernel))
    return jnp.where(offset == 0, jnp.ones_like(kernel), inner)


def interpolate(fields, theta_map, phi_map):
    widened = jnp.einsum("...t,ut->...u", fields, theta_map, precision=lax.Precision.HIGH)
    return jnp.einsum("qp,...pu->...qu", phi_map, widened, precision=lax.Precision.HIGH)


def select_rows(indices, table):
    count = table.shape[0]
    flat_ids = indices.reshape(-1)
    row_ids = jnp.arange(count, dtype=jnp.int32)
    onehot = (flat_ids[:, None] == row_ids[None, :]).astype(table.dtype)
    flat_table = table.reshape(count, -1)
    picked = jnp.dot(onehot, flat_table, precision=HIGHEST, preferred_element_type=jnp.float32)
    return picked.reshape(indices.shape + table.shape[1:])


def shift_sum(fields, cos_table, sin_table):
    groups = fields.shape[0]
    cosine = cos_table[None, :, None]
    sine = sin_table[None, :, None]
    shaped = fields.reshape(groups, 8, 2, 2, fields.shape[3], fields.shape[4])
    real_part = shaped[:, :, :, 0]
    imag_part = shaped[:, :, :, 1]
    new_real = jnp.sum(cosine * real_part - sine * imag_part, axis=1)
    new_imag = jnp.sum(sine * real_part + cosine * imag_part, axis=1)
    return jnp.stack([new_real, new_imag], axis=2).reshape(
        groups, 4, fields.shape[3], fields.shape[4]
    )


def pair_kernel(offsets, has_init, tgt_ref, src_ref, cls_ref, span_ref, table_hbm, *rest):
    blocks = rest[: len(offsets)]
    out_hbm, table, sources, acc, sems, out_sem = rest[-6:]
    rows = table.shape[2]
    classes = table.shape[0]
    pieces = [(p * classes // TABLE_PIECES, (p + 1) * classes // TABLE_PIECES) for p in range(TABLE_PIECES)]
    copies = [
        pltpu.make_async_copy(table_hbm.at[pl.ds(a, b - a)], table.at[pl.ds(a, b - a)], sems.at[p])
        for p, (a, b) in enumerate(pieces)
    ]
    for b, (block, first) in enumerate(zip(blocks, offsets)):
        copies.append(
            pltpu.make_async_copy(
                block, sources.at[pl.ds(first, block.shape[0])], sems.at[TABLE_PIECES + b]
            )
        )
    if has_init:
        copies.append(
            pltpu.make_async_copy(rest[len(offsets)], acc, sems.at[TABLE_PIECES + len(blocks)])
        )
    for c in copies:
        c.start()
    if not has_init:
        acc[...] = jnp.zeros_like(acc)
    for c in copies:
        c.wait()

    def item(i, carry):
        if True:
            t = tgt_ref[i]
            s = src_ref[i]
            k = cls_ref[i]

            def chunk(j, inner):
                r0 = pl.multiple_of(j * ROWS, ROWS)
                win = pl.ds(r0, ROWS)
                tr = table[k, 0, win, :].astype(jnp.float32)
                ti = table[k, 1, win, :].astype(jnp.float32)
                for q in range(2):
                    pr = sources[s, 2 * q, win, :]
                    pi = sources[s, 2 * q + 1, win, :]
                    acc[t, 2 * q, win, :] += tr * pr - ti * pi
                    acc[t, 2 * q + 1, win, :] += ti * pr + tr * pi
                return inner

            lax.fori_loop(0, rows // ROWS, chunk, 0, unroll=True)

        return carry

    lax.fori_loop(span_ref[0], span_ref[1], item, 0)
    done = pltpu.make_async_copy(acc, out_hbm, out_sem.at[0])
    done.start()
    done.wait()


def translate_pairs(items, trans_table, blocks, offsets, box_dev, init=None):
    tgt, src, cls, span = items
    shape = (box_dev,) + blocks[0].shape[1:]
    smem = pl.BlockSpec(memory_space=pltpu.SMEM)
    anywhere = pl.BlockSpec(memory_space=pl.ANY)
    extra = [] if init is None else [init]
    size = math.prod(shape)
    cost = pl.CostEstimate(
        flops=8 * size * tgt.shape[0] // 4,
        transcendentals=0,
        bytes_accessed=trans_table.size * 2 + 4 * size * (len(blocks) + 2),
    )
    return pl.pallas_call(
        functools.partial(pair_kernel, tuple(offsets), init is not None),
        out_shape=jax.ShapeDtypeStruct(shape, jnp.float32),
        in_specs=[smem] * 4 + [anywhere] * (1 + len(blocks) + len(extra)),
        out_specs=anywhere,
        scratch_shapes=[
            pltpu.VMEM(trans_table.shape, trans_table.dtype),
            pltpu.VMEM(((2 * REACH + 1) * box_dev,) + shape[1:], jnp.float32),
            pltpu.VMEM(shape, jnp.float32),
            pltpu.SemaphoreType.DMA((TABLE_PIECES + 1 + len(blocks),)),
            pltpu.SemaphoreType.DMA((1,)),
        ],
        input_output_aliases={} if init is None else {5 + len(blocks): 0},
        cost_estimate=cost,
        compiler_params=pltpu.CompilerParams(vmem_limit_bytes=66_000_000),
    )(tgt, src, cls, span, trans_table, *blocks, *extra)


def pair_lists(pair_near, pair_far, pair_class, pair_live):
    packed = jnp.stack([pair_near, pair_far, pair_class, pair_live])
    return [packed] + [passed_along(packed, "box", o) for o in range(1, REACH + 1)]


def pair_items(lists, pair_near, pair_far, pair_class, pair_live, box_dev, classes):
    tgt = [pair_near]
    src = [pair_far]
    cls = [pair_class]
    live = [pair_live]
    for o, lst in enumerate(lists):
        near, far, k, alive = lst[0], lst[1], lst[2], lst[3]
        tgt.append(far - o * box_dev)
        base = 0 if o == 0 else (REACH + o) * box_dev
        src.append(near + base)
        cls.append((k + classes // 2) % classes)
        live.append(jnp.where(far // box_dev == o, alive, 0))
    return [jnp.concatenate(x).astype(jnp.int32) for x in (tgt, src, cls, live)]


def body(
    child_pattern, octant, shift_angle, trans_table, pair_near, pair_far, pair_class, pair_live
):
    dir_count = lax.axis_size("dir")
    dir_index = lax.axis_index("dir")
    box_dev = child_pattern.shape[0] // 8
    classes = trans_table.shape[0]
    lists = pair_lists(pair_near, pair_far, pair_class, pair_live)
    theta_map = interp_rows(THETA1, THETA2, THETA2)
    phi_map = interp_rows(PHI1, PHI2, PHI2)
    cos_table = jnp.cos(shift_angle)
    sin_table = jnp.sin(shift_angle)
    grouped = child_pattern.reshape(box_dev, 8, 4, PHI1 // dir_count, THETA1)
    octants = octant.reshape(box_dev, 8)
    slots = jnp.arange(8, dtype=jnp.int32)
    by_octant = jnp.sum(
        jnp.where(octants[:, :, None] == slots[None, None, :], slots[None, :, None], 0), axis=1
    )
    chunks = 1
    while chunks < 4 and box_dev % (2 * chunks * dir_count) == 0:
        chunks *= 2
    per_chunk = box_dev // chunks
    per_dev = per_chunk // dir_count
    parts = []
    blocks = []
    offsets = []

    def send(c, part):
        moved = [part]
        moved += [passed_along(part, "box", -o) for o in range(1, REACH + 1)]
        moved += [passed_along(part, "box", o) for o in range(1, REACH + 1)]
        for b, block in enumerate(moved):
            blocks.append(block)
            offsets.append(b * box_dev + c * per_chunk)

    for c in range(chunks):
        piece = jnp.take_along_axis(
            grouped[c * per_chunk : (c + 1) * per_chunk],
            by_octant[c * per_chunk : (c + 1) * per_chunk, :, None, None, None],
            axis=1,
        )
        gathered = lax.all_to_all(piece, "dir", split_axis=0, concat_axis=3, tiled=True)
        if c >= 2:
            lo = (c - 2) * (2 * REACH + 1) + 1
            hi = (c - 1) * (2 * REACH + 1)
            sent, gathered = lax.optimization_barrier((blocks[lo:hi], gathered))
            blocks[lo:hi] = sent
        if parts:
            parts[-1], gathered = lax.optimization_barrier((parts[-1], gathered))
            send(c - 1, parts[-1])
        else:
            lists, gathered = lax.optimization_barrier((lists, gathered))
        full_dirs = interpolate(gathered, theta_map, phi_map)
        summed = shift_sum(full_dirs, cos_table, sin_table)
        parts.append(lax.all_to_all(summed, "dir", split_axis=2, concat_axis=0, tiled=True))
    send(chunks - 1, parts[-1])
    items = pair_items(lists, pair_near, pair_far, pair_class, pair_live, box_dev, classes)
    aggregated = jnp.concatenate(parts, axis=0) if chunks > 1 else parts[0]
    tgt, src, cls, live = items
    late = (src >= box_dev) & (src % box_dev >= (chunks - 1) * per_chunk)
    key = jnp.where(live != 0, late.astype(jnp.int32), 2)
    order = jnp.argsort(key, stable=True)
    tgt, src, cls = (jnp.take(x, order) for x in (tgt, src, cls))
    n_early = jnp.sum(key == 0).astype(jnp.int32)
    n_live = n_early + jnp.sum(key == 1).astype(jnp.int32)
    early_items = (tgt, src, cls, jnp.stack([jnp.int32(0), n_early]))
    late_items = (tgt, src, cls, jnp.stack([n_early, n_live]))
    cut = len(blocks) - 2 * REACH
    partial = translate_pairs(early_items, trans_table, blocks[:cut], offsets[:cut], box_dev)
    incoming = translate_pairs(
        late_items, trans_table, blocks[cut:], offsets[cut:], box_dev, init=partial
    )
    return (aggregated, incoming)


def solution(mesh):
    placed = (
        P("box", None, "dir", None),
        P("box"),
        P(),
        P(None, None, "dir", None),
        P("box"),
        P("box"),
        P("box"),
        P("box"),
    )
    return jax.shard_map(
        body,
        mesh=mesh,
        in_specs=placed,
        out_specs=(P("box", None, "dir", None), P("box", None, "dir", None)),
        check_vma=False,
    )
```

```python
import functools
import math

import jax
import jax.numpy as jnp
from jax import lax
from jax.experimental import pallas as pl
from jax.experimental.pallas import tpu as pltpu
from jax.sharding import PartitionSpec as P

REACH = 2
THETA1 = 128
PHI1 = 128
THETA2 = 256
PHI2 = 256
ROWS = 16
TABLE_PIECES = 4


HIGHEST = lax.Precision.HIGHEST


def passed_along(value, axis, steps):
    count = lax.axis_size(axis)
    first, last = (max(0, -steps), min(count, count - steps))
    return lax.ppermute(value, axis, [(source, source + steps) for source in range(first, last)])


def interp_rows(size_in, size_out, count):
    target_pos = jnp.arange(count, dtype=jnp.int32)
    source_pos = jnp.arange(size_in, dtype=jnp.int32)
    offset = target_pos[:, None] - 2 * source_pos[None, :]
    is_odd = offset % 2 == 1
    safe_off = jnp.where(is_odd, offset, 1).astype(jnp.float32)
    kernel = jnp.sin(math.pi * safe_off / 2.0) / (size_in * jnp.tan(math.pi * safe_off / size_out))
    inner = jnp.where(is_odd, kernel, jnp.zeros_like(kernel))
    return jnp.where(offset == 0, jnp.ones_like(kernel), inner)


def interpolate(fields, theta_map, phi_map):
    widened = jnp.einsum("...t,ut->...u", fields, theta_map, precision=lax.Precision.HIGH)
    return jnp.einsum("qp,...pu->...qu", phi_map, widened, precision=lax.Precision.HIGH)


def select_rows(indices, table):
    count = table.shape[0]
    flat_ids = indices.reshape(-1)
    row_ids = jnp.arange(count, dtype=jnp.int32)
    onehot = (flat_ids[:, None] == row_ids[None, :]).astype(table.dtype)
    flat_table = table.reshape(count, -1)
    picked = jnp.dot(onehot, flat_table, precision=HIGHEST, preferred_element_type=jnp.float32)
    return picked.reshape(indices.shape + table.shape[1:])


def shift_sum(fields, cos_table, sin_table):
    groups = fields.shape[0]
    cosine = cos_table[None, :, None]
    sine = sin_table[None, :, None]
    shaped = fields.reshape(groups, 8, 2, 2, fields.shape[3], fields.shape[4])
    real_part = shaped[:, :, :, 0]
    imag_part = shaped[:, :, :, 1]
    new_real = jnp.sum(cosine * real_part - sine * imag_part, axis=1)
    new_imag = jnp.sum(sine * real_part + cosine * imag_part, axis=1)
    return jnp.stack([new_real, new_imag], axis=2).reshape(
        groups, 4, fields.shape[3], fields.shape[4]
    )


def pair_kernel(offsets, has_init, tgt_ref, src_ref, cls_ref, span_ref, table_hbm, *rest):
    blocks = rest[: len(offsets)]
    out_hbm, table, sources, acc, sems, out_sem = rest[-6:]
    rows = table.shape[2]
    classes = table.shape[0]
    pieces = [(p * classes // TABLE_PIECES, (p + 1) * classes // TABLE_PIECES) for p in range(TABLE_PIECES)]
    copies = [
        pltpu.make_async_copy(table_hbm.at[pl.ds(a, b - a)], table.at[pl.ds(a, b - a)], sems.at[p])
        for p, (a, b) in enumerate(pieces)
    ]
    for b, (block, first) in enumerate(zip(blocks, offsets)):
        copies.append(
            pltpu.make_async_copy(
                block, sources.at[pl.ds(first, block.shape[0])], sems.at[TABLE_PIECES + b]
            )
        )
    if has_init:
        copies.append(
            pltpu.make_async_copy(rest[len(offsets)], acc, sems.at[TABLE_PIECES + len(blocks)])
        )
    for c in copies:
        c.start()
    if not has_init:
        acc[...] = jnp.zeros_like(acc)
    for c in copies:
        c.wait()

    def item(i, carry):
        if True:
            t = tgt_ref[i]
            s = src_ref[i]
            k = cls_ref[i]

            def chunk(j, inner):
                r0 = pl.multiple_of(j * ROWS, ROWS)
                win = pl.ds(r0, ROWS)
                tr = table[k, 0, win, :].astype(jnp.float32)
                ti = table[k, 1, win, :].astype(jnp.float32)
                for q in range(2):
                    pr = sources[s, 2 * q, win, :]
                    pi = sources[s, 2 * q + 1, win, :]
                    acc[t, 2 * q, win, :] += tr * pr - ti * pi
                    acc[t, 2 * q + 1, win, :] += ti * pr + tr * pi
                return inner

            lax.fori_loop(0, rows // ROWS, chunk, 0, unroll=True)

        return carry

    lax.fori_loop(span_ref[0], span_ref[1], item, 0)
    done = pltpu.make_async_copy(acc, out_hbm, out_sem.at[0])
    done.start()
    done.wait()


def translate_pairs(items, trans_table, blocks, offsets, box_dev, init=None):
    tgt, src, cls, span = items
    shape = (box_dev,) + blocks[0].shape[1:]
    smem = pl.BlockSpec(memory_space=pltpu.SMEM)
    anywhere = pl.BlockSpec(memory_space=pl.ANY)
    extra = [] if init is None else [init]
    size = math.prod(shape)
    cost = pl.CostEstimate(
        flops=8 * size * tgt.shape[0] // 4,
        transcendentals=0,
        bytes_accessed=trans_table.size * 2 + 4 * size * (len(blocks) + 2),
    )
    return pl.pallas_call(
        functools.partial(pair_kernel, tuple(offsets), init is not None),
        out_shape=jax.ShapeDtypeStruct(shape, jnp.float32),
        in_specs=[smem] * 4 + [anywhere] * (1 + len(blocks) + len(extra)),
        out_specs=anywhere,
        scratch_shapes=[
            pltpu.VMEM(trans_table.shape, trans_table.dtype),
            pltpu.VMEM(((2 * REACH + 1) * box_dev,) + shape[1:], jnp.float32),
            pltpu.VMEM(shape, jnp.float32),
            pltpu.SemaphoreType.DMA((TABLE_PIECES + 1 + len(blocks),)),
            pltpu.SemaphoreType.DMA((1,)),
        ],
        input_output_aliases={} if init is None else {5 + len(blocks): 0},
        cost_estimate=cost,
        compiler_params=pltpu.CompilerParams(vmem_limit_bytes=66_000_000),
    )(tgt, src, cls, span, trans_table, *blocks, *extra)


def pair_lists(pair_near, pair_far, pair_class, pair_live):
    packed = jnp.stack([pair_near, pair_far, pair_class, pair_live])
    return [packed] + [passed_along(packed, "box", o) for o in range(1, REACH + 1)]


def pair_items(lists, pair_near, pair_far, pair_class, pair_live, box_dev, classes):
    tgt = [pair_near]
    src = [pair_far]
    cls = [pair_class]
    live = [pair_live]
    for o, lst in enumerate(lists):
        near, far, k, alive = lst[0], lst[1], lst[2], lst[3]
        tgt.append(far - o * box_dev)
        base = 0 if o == 0 else (REACH + o) * box_dev
        src.append(near + base)
        cls.append((k + classes // 2) % classes)
        live.append(jnp.where(far // box_dev == o, alive, 0))
    return [jnp.concatenate(x).astype(jnp.int32) for x in (tgt, src, cls, live)]


def body(
    child_pattern, octant, shift_angle, trans_table, pair_near, pair_far, pair_class, pair_live
):
    dir_count = lax.axis_size("dir")
    dir_index = lax.axis_index("dir")
    box_dev = child_pattern.shape[0] // 8
    classes = trans_table.shape[0]
    lists = pair_lists(pair_near, pair_far, pair_class, pair_live)
    theta_map = interp_rows(THETA1, THETA2, THETA2)
    phi_map = interp_rows(PHI1, PHI2, PHI2)
    cos_table = jnp.cos(shift_angle)
    sin_table = jnp.sin(shift_angle)
    grouped = child_pattern.reshape(box_dev, 8, 4, PHI1 // dir_count, THETA1)
    octants = octant.reshape(box_dev, 8)
    flat_children = child_pattern.reshape(box_dev * 8, -1)
    slots = jnp.arange(8, dtype=jnp.int32)
    by_octant = jnp.sum(
        jnp.where(octants[:, :, None] == slots[None, None, :], slots[None, :, None], 0), axis=1
    )
    chunks = 1
    while chunks < 4 and box_dev % (2 * chunks * dir_count) == 0:
        chunks *= 2
    per_chunk = box_dev // chunks
    per_dev = per_chunk // dir_count
    parts = []
    blocks = []
    offsets = []

    def send(c, part):
        moved = [part]
        moved += [passed_along(part, "box", -o) for o in range(1, REACH + 1)]
        moved += [passed_along(part, "box", o) for o in range(1, REACH + 1)]
        for b, block in enumerate(moved):
            blocks.append(block)
            offsets.append(b * box_dev + c * per_chunk)

    for c in range(chunks):
        rows = (c * per_chunk + jnp.arange(per_chunk, dtype=jnp.int32))[:, None] * 8
        rows = (rows + by_octant[c * per_chunk : (c + 1) * per_chunk]).reshape(-1)
        piece = jnp.take(flat_children, rows, axis=0).reshape((per_chunk,) + grouped.shape[1:])
        gathered = lax.all_to_all(piece, "dir", split_axis=0, concat_axis=3, tiled=True)
        if c >= 2:
            lo = (c - 2) * (2 * REACH + 1) + 1
            hi = (c - 1) * (2 * REACH + 1)
            sent, gathered = lax.optimization_barrier((blocks[lo:hi], gathered))
            blocks[lo:hi] = sent
        if parts:
            parts[-1], gathered = lax.optimization_barrier((parts[-1], gathered))
            send(c - 1, parts[-1])
        else:
            lists, gathered = lax.optimization_barrier((lists, gathered))
        full_dirs = interpolate(gathered, theta_map, phi_map)
        summed = shift_sum(full_dirs, cos_table, sin_table)
        parts.append(lax.all_to_all(summed, "dir", split_axis=2, concat_axis=0, tiled=True))
    send(chunks - 1, parts[-1])
    items = pair_items(lists, pair_near, pair_far, pair_class, pair_live, box_dev, classes)
    aggregated = jnp.concatenate(parts, axis=0) if chunks > 1 else parts[0]
    tgt, src, cls, live = items
    late = (src >= box_dev) & (src % box_dev >= (chunks - 1) * per_chunk)
    key = jnp.where(live != 0, late.astype(jnp.int32), 2)
    order = jnp.argsort(key, stable=True)
    tgt, src, cls = jnp.take(jnp.stack([tgt, src, cls]), order, axis=1)
    n_early = jnp.sum(key == 0).astype(jnp.int32)
    n_live = n_early + jnp.sum(key == 1).astype(jnp.int32)
    early_items = (tgt, src, cls, jnp.stack([jnp.int32(0), n_early]))
    late_items = (tgt, src, cls, jnp.stack([n_early, n_live]))
    cut = len(blocks) - 2 * REACH
    partial = translate_pairs(early_items, trans_table, blocks[:cut], offsets[:cut], box_dev)
    incoming = translate_pairs(
        late_items, trans_table, blocks[cut:], offsets[cut:], box_dev, init=partial
    )
    return (aggregated, incoming)


def solution(mesh):
    placed = (
        P("box", None, "dir", None),
        P("box"),
        P(),
        P(None, None, "dir", None),
        P("box"),
        P("box"),
        P("box"),
        P("box"),
    )
    return jax.shard_map(
        body,
        mesh=mesh,
        in_specs=placed,
        out_specs=(P("box", None, "dir", None), P("box", None, "dir", None)),
        check_vma=False,
    )
```

```python
import functools
import math

import jax
import jax.numpy as jnp
from jax import lax
from jax.experimental import pallas as pl
from jax.experimental.pallas import tpu as pltpu
from jax.sharding import PartitionSpec as P

REACH = 2
THETA1 = 128
PHI1 = 128
THETA2 = 256
PHI2 = 256
ROWS = 16
TABLE_PIECES = 4


HIGHEST = lax.Precision.HIGHEST


def passed_along(value, axis, steps):
    count = lax.axis_size(axis)
    first, last = (max(0, -steps), min(count, count - steps))
    return lax.ppermute(value, axis, [(source, source + steps) for source in range(first, last)])


def interp_rows(size_in, size_out, count):
    target_pos = jnp.arange(count, dtype=jnp.int32)
    source_pos = jnp.arange(size_in, dtype=jnp.int32)
    offset = target_pos[:, None] - 2 * source_pos[None, :]
    is_odd = offset % 2 == 1
    safe_off = jnp.where(is_odd, offset, 1).astype(jnp.float32)
    kernel = jnp.sin(math.pi * safe_off / 2.0) / (size_in * jnp.tan(math.pi * safe_off / size_out))
    inner = jnp.where(is_odd, kernel, jnp.zeros_like(kernel))
    return jnp.where(offset == 0, jnp.ones_like(kernel), inner)


def interpolate(fields, theta_map, phi_map):
    widened = jnp.einsum("...t,ut->...u", fields, theta_map, precision=lax.Precision.HIGH)
    return jnp.einsum("qp,...pu->...qu", phi_map, widened, precision=lax.Precision.HIGH)


def select_rows(indices, table):
    count = table.shape[0]
    flat_ids = indices.reshape(-1)
    row_ids = jnp.arange(count, dtype=jnp.int32)
    onehot = (flat_ids[:, None] == row_ids[None, :]).astype(table.dtype)
    flat_table = table.reshape(count, -1)
    picked = jnp.dot(onehot, flat_table, precision=HIGHEST, preferred_element_type=jnp.float32)
    return picked.reshape(indices.shape + table.shape[1:])


def shift_sum(fields, cos_table, sin_table):
    groups = fields.shape[0]
    cosine = cos_table[None, :, None]
    sine = sin_table[None, :, None]
    shaped = fields.reshape(groups, 8, 2, 2, fields.shape[3], fields.shape[4])
    real_part = shaped[:, :, :, 0]
    imag_part = shaped[:, :, :, 1]
    new_real = jnp.sum(cosine * real_part - sine * imag_part, axis=1)
    new_imag = jnp.sum(sine * real_part + cosine * imag_part, axis=1)
    return jnp.stack([new_real, new_imag], axis=2).reshape(
        groups, 4, fields.shape[3], fields.shape[4]
    )


def pair_kernel(offsets, has_init, tgt_ref, src_ref, cls_ref, span_ref, table_hbm, *rest):
    blocks = rest[: len(offsets)]
    out_hbm, table, sources, acc, sems, out_sem = rest[-6:]
    rows = table.shape[2]
    classes = table.shape[0]
    pieces = [(p * classes // TABLE_PIECES, (p + 1) * classes // TABLE_PIECES) for p in range(TABLE_PIECES)]
    copies = [
        pltpu.make_async_copy(table_hbm.at[pl.ds(a, b - a)], table.at[pl.ds(a, b - a)], sems.at[p])
        for p, (a, b) in enumerate(pieces)
    ]
    for b, (block, first) in enumerate(zip(blocks, offsets)):
        copies.append(
            pltpu.make_async_copy(
                block, sources.at[pl.ds(first, block.shape[0])], sems.at[TABLE_PIECES + b]
            )
        )
    if has_init:
        copies.append(
            pltpu.make_async_copy(rest[len(offsets)], acc, sems.at[TABLE_PIECES + len(blocks)])
        )
    for c in copies:
        c.start()
    if not has_init:
        acc[...] = jnp.zeros_like(acc)
    for c in copies:
        c.wait()

    def item(i, carry):
        if True:
            t = tgt_ref[i]
            s = src_ref[i]
            k = cls_ref[i]

            def chunk(j, inner):
                r0 = pl.multiple_of(j * ROWS, ROWS)
                win = pl.ds(r0, ROWS)
                tr = table[k, 0, win, :].astype(jnp.float32)
                ti = table[k, 1, win, :].astype(jnp.float32)
                for q in range(2):
                    pr = sources[s, 2 * q, win, :]
                    pi = sources[s, 2 * q + 1, win, :]
                    acc[t, 2 * q, win, :] += tr * pr - ti * pi
                    acc[t, 2 * q + 1, win, :] += ti * pr + tr * pi
                return inner

            lax.fori_loop(0, rows // ROWS, chunk, 0, unroll=True)

        return carry

    lax.fori_loop(span_ref[0], span_ref[1], item, 0)
    done = pltpu.make_async_copy(acc, out_hbm, out_sem.at[0])
    done.start()
    done.wait()


def translate_pairs(items, trans_table, blocks, offsets, box_dev, init=None):
    tgt, src, cls, span = items
    shape = (box_dev,) + blocks[0].shape[1:]
    smem = pl.BlockSpec(memory_space=pltpu.SMEM)
    anywhere = pl.BlockSpec(memory_space=pl.ANY)
    extra = [] if init is None else [init]
    size = math.prod(shape)
    cost = pl.CostEstimate(
        flops=8 * size * tgt.shape[0] // 4,
        transcendentals=0,
        bytes_accessed=trans_table.size * 2 + 4 * size * (len(blocks) + 2),
    )
    return pl.pallas_call(
        functools.partial(pair_kernel, tuple(offsets), init is not None),
        out_shape=jax.ShapeDtypeStruct(shape, jnp.float32),
        in_specs=[smem] * 4 + [anywhere] * (1 + len(blocks) + len(extra)),
        out_specs=anywhere,
        scratch_shapes=[
            pltpu.VMEM(trans_table.shape, trans_table.dtype),
            pltpu.VMEM(((2 * REACH + 1) * box_dev,) + shape[1:], jnp.float32),
            pltpu.VMEM(shape, jnp.float32),
            pltpu.SemaphoreType.DMA((TABLE_PIECES + 1 + len(blocks),)),
            pltpu.SemaphoreType.DMA((1,)),
        ],
        input_output_aliases={} if init is None else {5 + len(blocks): 0},
        cost_estimate=cost,
        compiler_params=pltpu.CompilerParams(vmem_limit_bytes=66_000_000),
    )(tgt, src, cls, span, trans_table, *blocks, *extra)


def pair_lists(pair_near, pair_far, pair_class, pair_live):
    packed = jnp.stack([pair_near, pair_far, pair_class, pair_live])
    return [packed] + [passed_along(packed, "box", o) for o in range(1, REACH + 1)]


def pair_items(lists, pair_near, pair_far, pair_class, pair_live, box_dev, classes):
    tgt = [pair_near]
    src = [pair_far]
    cls = [pair_class]
    live = [pair_live]
    for o, lst in enumerate(lists):
        near, far, k, alive = lst[0], lst[1], lst[2], lst[3]
        tgt.append(far - o * box_dev)
        base = 0 if o == 0 else (REACH + o) * box_dev
        src.append(near + base)
        cls.append((k + classes // 2) % classes)
        live.append(jnp.where(far // box_dev == o, alive, 0))
    return [jnp.concatenate(x).astype(jnp.int32) for x in (tgt, src, cls, live)]


def body(
    child_pattern, octant, shift_angle, trans_table, pair_near, pair_far, pair_class, pair_live
):
    dir_count = lax.axis_size("dir")
    dir_index = lax.axis_index("dir")
    box_dev = child_pattern.shape[0] // 8
    classes = trans_table.shape[0]
    lists = pair_lists(pair_near, pair_far, pair_class, pair_live)
    theta_map = interp_rows(THETA1, THETA2, THETA2)
    phi_map = interp_rows(PHI1, PHI2, PHI2)
    cos_table = jnp.cos(shift_angle)
    sin_table = jnp.sin(shift_angle)
    grouped = child_pattern.reshape(box_dev, 8, 4, PHI1 // dir_count, THETA1)
    octants = octant.reshape(box_dev, 8)
    slots = jnp.arange(8, dtype=jnp.int32)
    by_octant = jnp.sum(
        jnp.where(octants[:, :, None] == slots[None, None, :], slots[None, :, None], 0), axis=1
    )
    chunks = 1
    while chunks < 4 and box_dev % (2 * chunks * dir_count) == 0:
        chunks *= 2
    per_chunk = box_dev // chunks
    per_dev = per_chunk // dir_count
    parts = []
    blocks = []
    offsets = []

    def send(c, part):
        moved = [part]
        moved += [passed_along(part, "box", -o) for o in range(1, REACH + 1)]
        moved += [passed_along(part, "box", o) for o in range(1, REACH + 1)]
        for b, block in enumerate(moved):
            blocks.append(block)
            offsets.append(b * box_dev + c * per_chunk)

    for c in range(chunks):
        piece = jnp.take_along_axis(
            grouped[c * per_chunk : (c + 1) * per_chunk],
            by_octant[c * per_chunk : (c + 1) * per_chunk, :, None, None, None],
            axis=1,
        )
        gathered = lax.all_to_all(piece, "dir", split_axis=0, concat_axis=3, tiled=True)
        if c >= 2:
            lo = (c - 2) * (2 * REACH + 1) + 1
            hi = (c - 1) * (2 * REACH + 1)
            sent, gathered = lax.optimization_barrier((blocks[lo:hi], gathered))
            blocks[lo:hi] = sent
        if parts:
            parts[-1], gathered = lax.optimization_barrier((parts[-1], gathered))
            send(c - 1, parts[-1])
        else:
            lists, gathered = lax.optimization_barrier((lists, gathered))
        full_dirs = interpolate(gathered, theta_map, phi_map)
        summed = shift_sum(full_dirs, cos_table, sin_table)
        parts.append(lax.all_to_all(summed, "dir", split_axis=2, concat_axis=0, tiled=True))
    send(chunks - 1, parts[-1])
    items = pair_items(lists, pair_near, pair_far, pair_class, pair_live, box_dev, classes)
    aggregated = jnp.concatenate(parts, axis=0) if chunks > 1 else parts[0]
    tgt, src, cls, live = items
    late = (src >= box_dev) & (src % box_dev >= (chunks - 1) * per_chunk)
    key = jnp.where(live != 0, late.astype(jnp.int32), 2)
    order = jnp.argsort(key, stable=True)
    tgt, src, cls = jnp.take(jnp.stack([tgt, src, cls]), order, axis=1)
    n_early = jnp.sum(key == 0).astype(jnp.int32)
    n_live = n_early + jnp.sum(key == 1).astype(jnp.int32)
    early_items = (tgt, src, cls, jnp.stack([jnp.int32(0), n_early]))
    late_items = (tgt, src, cls, jnp.stack([n_early, n_live]))
    cut = len(blocks) - 2 * REACH
    partial = translate_pairs(early_items, trans_table, blocks[:cut], offsets[:cut], box_dev)
    incoming = translate_pairs(
        late_items, trans_table, blocks[cut:], offsets[cut:], box_dev, init=partial
    )
    return (aggregated, incoming)


def solution(mesh):
    placed = (
        P("box", None, "dir", None),
        P("box"),
        P(),
        P(None, None, "dir", None),
        P("box"),
        P("box"),
        P("box"),
        P("box"),
    )
    return jax.shard_map(
        body,
        mesh=mesh,
        in_specs=placed,
        out_specs=(P("box", None, "dir", None), P("box", None, "dir", None)),
        check_vma=False,
    )
```

```python
import functools
import math

import jax
import jax.numpy as jnp
from jax import lax
from jax.experimental import pallas as pl
from jax.experimental.pallas import tpu as pltpu
from jax.sharding import PartitionSpec as P

REACH = 2
THETA1 = 128
PHI1 = 128
THETA2 = 256
PHI2 = 256
ROWS = 16
TABLE_PIECES = 4


HIGHEST = lax.Precision.HIGHEST


def passed_along(value, axis, steps):
    count = lax.axis_size(axis)
    first, last = (max(0, -steps), min(count, count - steps))
    return lax.ppermute(value, axis, [(source, source + steps) for source in range(first, last)])


def interp_rows(size_in, size_out, count):
    target_pos = jnp.arange(count, dtype=jnp.int32)
    source_pos = jnp.arange(size_in, dtype=jnp.int32)
    offset = target_pos[:, None] - 2 * source_pos[None, :]
    is_odd = offset % 2 == 1
    safe_off = jnp.where(is_odd, offset, 1).astype(jnp.float32)
    kernel = jnp.sin(math.pi * safe_off / 2.0) / (size_in * jnp.tan(math.pi * safe_off / size_out))
    inner = jnp.where(is_odd, kernel, jnp.zeros_like(kernel))
    return jnp.where(offset == 0, jnp.ones_like(kernel), inner)


def interpolate(fields, theta_map, phi_map):
    widened = jnp.einsum("...t,ut->...u", fields, theta_map, precision=lax.Precision.HIGH)
    return jnp.einsum("qp,...pu->...qu", phi_map, widened, precision=lax.Precision.HIGH)


def select_rows(indices, table):
    count = table.shape[0]
    flat_ids = indices.reshape(-1)
    row_ids = jnp.arange(count, dtype=jnp.int32)
    onehot = (flat_ids[:, None] == row_ids[None, :]).astype(table.dtype)
    flat_table = table.reshape(count, -1)
    picked = jnp.dot(onehot, flat_table, precision=HIGHEST, preferred_element_type=jnp.float32)
    return picked.reshape(indices.shape + table.shape[1:])


def shift_sum(fields, cos_table, sin_table):
    groups = fields.shape[0]
    cosine = cos_table[None, :, None]
    sine = sin_table[None, :, None]
    shaped = fields.reshape(groups, 8, 2, 2, fields.shape[3], fields.shape[4])
    real_part = shaped[:, :, :, 0]
    imag_part = shaped[:, :, :, 1]
    new_real = jnp.sum(cosine * real_part - sine * imag_part, axis=1)
    new_imag = jnp.sum(sine * real_part + cosine * imag_part, axis=1)
    return jnp.stack([new_real, new_imag], axis=2).reshape(
        groups, 4, fields.shape[3], fields.shape[4]
    )


def pair_kernel(offsets, has_init, tgt_ref, src_ref, cls_ref, span_ref, table_hbm, *rest):
    blocks = rest[: len(offsets)]
    out_hbm, table, sources, acc, sems, out_sem = rest[-6:]
    rows = table.shape[2]
    classes = table.shape[0]
    pieces = [(p * classes // TABLE_PIECES, (p + 1) * classes // TABLE_PIECES) for p in range(TABLE_PIECES)]
    copies = [
        pltpu.make_async_copy(table_hbm.at[pl.ds(a, b - a)], table.at[pl.ds(a, b - a)], sems.at[p])
        for p, (a, b) in enumerate(pieces)
    ]
    for b, (block, first) in enumerate(zip(blocks, offsets)):
        copies.append(
            pltpu.make_async_copy(
                block, sources.at[pl.ds(first, block.shape[0])], sems.at[TABLE_PIECES + b]
            )
        )
    if has_init:
        copies.append(
            pltpu.make_async_copy(rest[len(offsets)], acc, sems.at[TABLE_PIECES + len(blocks)])
        )
    for c in copies:
        c.start()
    if not has_init:
        acc[...] = jnp.zeros_like(acc)
    for c in copies[TABLE_PIECES:]:
        c.wait()

    def item(i, carry):
        if True:
            t = tgt_ref[i]
            s = src_ref[i]
            k = cls_ref[i]

            def chunk(j, inner):
                r0 = pl.multiple_of(j * ROWS, ROWS)
                win = pl.ds(r0, ROWS)
                tr = table[k, 0, win, :].astype(jnp.float32)
                ti = table[k, 1, win, :].astype(jnp.float32)
                for q in range(2):
                    pr = sources[s, 2 * q, win, :]
                    pi = sources[s, 2 * q + 1, win, :]
                    acc[t, 2 * q, win, :] += tr * pr - ti * pi
                    acc[t, 2 * q + 1, win, :] += ti * pr + tr * pi
                return inner

            lax.fori_loop(0, rows // ROWS, chunk, 0, unroll=True)

        return carry

    for p in range(TABLE_PIECES):
        copies[p].wait()
        lax.fori_loop(span_ref[p], span_ref[p + 1], item, 0)
    done = pltpu.make_async_copy(acc, out_hbm, out_sem.at[0])
    done.start()
    done.wait()


def translate_pairs(items, trans_table, blocks, offsets, box_dev, init=None):
    tgt, src, cls, span = items
    shape = (box_dev,) + blocks[0].shape[1:]
    smem = pl.BlockSpec(memory_space=pltpu.SMEM)
    anywhere = pl.BlockSpec(memory_space=pl.ANY)
    extra = [] if init is None else [init]
    size = math.prod(shape)
    cost = pl.CostEstimate(
        flops=8 * size * tgt.shape[0] // 4,
        transcendentals=0,
        bytes_accessed=trans_table.size * 2 + 4 * size * (len(blocks) + 2),
    )
    return pl.pallas_call(
        functools.partial(pair_kernel, tuple(offsets), init is not None),
        out_shape=jax.ShapeDtypeStruct(shape, jnp.float32),
        in_specs=[smem] * 4 + [anywhere] * (1 + len(blocks) + len(extra)),
        out_specs=anywhere,
        scratch_shapes=[
            pltpu.VMEM(trans_table.shape, trans_table.dtype),
            pltpu.VMEM(((2 * REACH + 1) * box_dev,) + shape[1:], jnp.float32),
            pltpu.VMEM(shape, jnp.float32),
            pltpu.SemaphoreType.DMA((TABLE_PIECES + 1 + len(blocks),)),
            pltpu.SemaphoreType.DMA((1,)),
        ],
        input_output_aliases={} if init is None else {5 + len(blocks): 0},
        cost_estimate=cost,
        compiler_params=pltpu.CompilerParams(vmem_limit_bytes=66_000_000),
    )(tgt, src, cls, span, trans_table, *blocks, *extra)


def pair_lists(pair_near, pair_far, pair_class, pair_live):
    packed = jnp.stack([pair_near, pair_far, pair_class, pair_live])
    return [packed] + [passed_along(packed, "box", o) for o in range(1, REACH + 1)]


def pair_items(lists, pair_near, pair_far, pair_class, pair_live, box_dev, classes):
    tgt = [pair_near]
    src = [pair_far]
    cls = [pair_class]
    live = [pair_live]
    for o, lst in enumerate(lists):
        near, far, k, alive = lst[0], lst[1], lst[2], lst[3]
        tgt.append(far - o * box_dev)
        base = 0 if o == 0 else (REACH + o) * box_dev
        src.append(near + base)
        cls.append((k + classes // 2) % classes)
        live.append(jnp.where(far // box_dev == o, alive, 0))
    return [jnp.concatenate(x).astype(jnp.int32) for x in (tgt, src, cls, live)]


def body(
    child_pattern, octant, shift_angle, trans_table, pair_near, pair_far, pair_class, pair_live
):
    dir_count = lax.axis_size("dir")
    dir_index = lax.axis_index("dir")
    box_dev = child_pattern.shape[0] // 8
    classes = trans_table.shape[0]
    lists = pair_lists(pair_near, pair_far, pair_class, pair_live)
    theta_map = interp_rows(THETA1, THETA2, THETA2)
    phi_map = interp_rows(PHI1, PHI2, PHI2)
    cos_table = jnp.cos(shift_angle)
    sin_table = jnp.sin(shift_angle)
    grouped = child_pattern.reshape(box_dev, 8, 4, PHI1 // dir_count, THETA1)
    octants = octant.reshape(box_dev, 8)
    slots = jnp.arange(8, dtype=jnp.int32)
    by_octant = jnp.sum(
        jnp.where(octants[:, :, None] == slots[None, None, :], slots[None, :, None], 0), axis=1
    )
    chunks = 1
    while chunks < 4 and box_dev % (2 * chunks * dir_count) == 0:
        chunks *= 2
    per_chunk = box_dev // chunks
    per_dev = per_chunk // dir_count
    parts = []
    blocks = []
    offsets = []

    def send(c, part):
        moved = [part]
        moved += [passed_along(part, "box", -o) for o in range(1, REACH + 1)]
        moved += [passed_along(part, "box", o) for o in range(1, REACH + 1)]
        for b, block in enumerate(moved):
            blocks.append(block)
            offsets.append(b * box_dev + c * per_chunk)

    for c in range(chunks):
        piece = jnp.take_along_axis(
            grouped[c * per_chunk : (c + 1) * per_chunk],
            by_octant[c * per_chunk : (c + 1) * per_chunk, :, None, None, None],
            axis=1,
        )
        gathered = lax.all_to_all(piece, "dir", split_axis=0, concat_axis=3, tiled=True)
        if c >= 2:
            lo = (c - 2) * (2 * REACH + 1) + 1
            hi = (c - 1) * (2 * REACH + 1)
            sent, gathered = lax.optimization_barrier((blocks[lo:hi], gathered))
            blocks[lo:hi] = sent
        if parts:
            parts[-1], gathered = lax.optimization_barrier((parts[-1], gathered))
            send(c - 1, parts[-1])
        else:
            lists, gathered = lax.optimization_barrier((lists, gathered))
        full_dirs = interpolate(gathered, theta_map, phi_map)
        summed = shift_sum(full_dirs, cos_table, sin_table)
        parts.append(lax.all_to_all(summed, "dir", split_axis=2, concat_axis=0, tiled=True))
    send(chunks - 1, parts[-1])
    items = pair_items(lists, pair_near, pair_far, pair_class, pair_live, box_dev, classes)
    aggregated = jnp.concatenate(parts, axis=0) if chunks > 1 else parts[0]
    tgt, src, cls, live = items
    late = (src >= box_dev) & (src % box_dev >= (chunks - 1) * per_chunk)
    piece = sum(
        (cls >= q * classes // TABLE_PIECES).astype(jnp.int32) for q in range(1, TABLE_PIECES)
    )
    buckets = 2 * TABLE_PIECES
    key = jnp.where(live != 0, late.astype(jnp.int32) * TABLE_PIECES + piece, buckets)
    order = jnp.argsort(key, stable=True)
    tgt, src, cls = (jnp.take(x, order) for x in (tgt, src, cls))
    counts = jnp.sum(key[None, :] == jnp.arange(buckets, dtype=jnp.int32)[:, None], axis=1)
    spans = jnp.concatenate([jnp.zeros((1,), jnp.int32), jnp.cumsum(counts).astype(jnp.int32)])
    early_items = (tgt, src, cls, spans[: TABLE_PIECES + 1])
    late_items = (tgt, src, cls, spans[TABLE_PIECES:])
    cut = len(blocks) - 2 * REACH
    partial = translate_pairs(early_items, trans_table, blocks[:cut], offsets[:cut], box_dev)
    incoming = translate_pairs(
        late_items, trans_table, blocks[cut:], offsets[cut:], box_dev, init=partial
    )
    return (aggregated, incoming)


def solution(mesh):
    placed = (
        P("box", None, "dir", None),
        P("box"),
        P(),
        P(None, None, "dir", None),
        P("box"),
        P("box"),
        P("box"),
        P("box"),
    )
    return jax.shard_map(
        body,
        mesh=mesh,
        in_specs=placed,
        out_specs=(P("box", None, "dir", None), P("box", None, "dir", None)),
        check_vma=False,
    )
```

```python
import functools
import math

import jax
import jax.numpy as jnp
from jax import lax
from jax.experimental import pallas as pl
from jax.experimental.pallas import tpu as pltpu
from jax.sharding import PartitionSpec as P

REACH = 2
THETA1 = 128
PHI1 = 128
THETA2 = 256
PHI2 = 256
ROWS = 16
TABLE_PIECES = 4


HIGHEST = lax.Precision.HIGHEST


def passed_along(value, axis, steps):
    count = lax.axis_size(axis)
    first, last = (max(0, -steps), min(count, count - steps))
    return lax.ppermute(value, axis, [(source, source + steps) for source in range(first, last)])


def interp_rows(size_in, size_out, count):
    target_pos = jnp.arange(count, dtype=jnp.int32)
    source_pos = jnp.arange(size_in, dtype=jnp.int32)
    offset = target_pos[:, None] - 2 * source_pos[None, :]
    is_odd = offset % 2 == 1
    safe_off = jnp.where(is_odd, offset, 1).astype(jnp.float32)
    kernel = jnp.sin(math.pi * safe_off / 2.0) / (size_in * jnp.tan(math.pi * safe_off / size_out))
    inner = jnp.where(is_odd, kernel, jnp.zeros_like(kernel))
    return jnp.where(offset == 0, jnp.ones_like(kernel), inner)


def interpolate(fields, theta_map, phi_map):
    widened = jnp.einsum("...t,ut->...u", fields, theta_map, precision=lax.Precision.HIGH)
    return jnp.einsum("qp,...pu->...qu", phi_map, widened, precision=lax.Precision.HIGH)


def select_rows(indices, table):
    count = table.shape[0]
    flat_ids = indices.reshape(-1)
    row_ids = jnp.arange(count, dtype=jnp.int32)
    onehot = (flat_ids[:, None] == row_ids[None, :]).astype(table.dtype)
    flat_table = table.reshape(count, -1)
    picked = jnp.dot(onehot, flat_table, precision=HIGHEST, preferred_element_type=jnp.float32)
    return picked.reshape(indices.shape + table.shape[1:])


def shift_sum(fields, cos_table, sin_table):
    groups = fields.shape[0]
    cosine = cos_table[None, :, None]
    sine = sin_table[None, :, None]
    shaped = fields.reshape(groups, 8, 2, 2, fields.shape[3], fields.shape[4])
    real_part = shaped[:, :, :, 0]
    imag_part = shaped[:, :, :, 1]
    new_real = jnp.sum(cosine * real_part - sine * imag_part, axis=1)
    new_imag = jnp.sum(sine * real_part + cosine * imag_part, axis=1)
    return jnp.stack([new_real, new_imag], axis=2).reshape(
        groups, 4, fields.shape[3], fields.shape[4]
    )


def pair_kernel(offsets, has_init, tgt_ref, src_ref, cls_ref, order_ref, span_ref, table_hbm, *rest):
    blocks = rest[: len(offsets)]
    out_hbm, table, sources, acc, sems, out_sem = rest[-6:]
    rows = table.shape[2]
    classes = table.shape[0]
    pieces = [(p * classes // TABLE_PIECES, (p + 1) * classes // TABLE_PIECES) for p in range(TABLE_PIECES)]
    copies = [
        pltpu.make_async_copy(table_hbm.at[pl.ds(a, b - a)], table.at[pl.ds(a, b - a)], sems.at[p])
        for p, (a, b) in enumerate(pieces)
    ]
    for b, (block, first) in enumerate(zip(blocks, offsets)):
        copies.append(
            pltpu.make_async_copy(
                block, sources.at[pl.ds(first, block.shape[0])], sems.at[TABLE_PIECES + b]
            )
        )
    if has_init:
        copies.append(
            pltpu.make_async_copy(rest[len(offsets)], acc, sems.at[TABLE_PIECES + len(blocks)])
        )
    for c in copies:
        c.start()
    if not has_init:
        acc[...] = jnp.zeros_like(acc)
    for c in copies:
        c.wait()

    def item(i, carry):
        if True:
            j = order_ref[i]
            t = tgt_ref[j]
            s = src_ref[j]
            k = cls_ref[j]

            def chunk(j, inner):
                r0 = pl.multiple_of(j * ROWS, ROWS)
                win = pl.ds(r0, ROWS)
                tr = table[k, 0, win, :].astype(jnp.float32)
                ti = table[k, 1, win, :].astype(jnp.float32)
                for q in range(2):
                    pr = sources[s, 2 * q, win, :]
                    pi = sources[s, 2 * q + 1, win, :]
                    acc[t, 2 * q, win, :] += tr * pr - ti * pi
                    acc[t, 2 * q + 1, win, :] += ti * pr + tr * pi
                return inner

            lax.fori_loop(0, rows // ROWS, chunk, 0, unroll=True)

        return carry

    lax.fori_loop(span_ref[0], span_ref[1], item, 0)
    done = pltpu.make_async_copy(acc, out_hbm, out_sem.at[0])
    done.start()
    done.wait()


def translate_pairs(items, trans_table, blocks, offsets, box_dev, init=None):
    tgt, src, cls, order, span = items
    shape = (box_dev,) + blocks[0].shape[1:]
    smem = pl.BlockSpec(memory_space=pltpu.SMEM)
    anywhere = pl.BlockSpec(memory_space=pl.ANY)
    extra = [] if init is None else [init]
    size = math.prod(shape)
    cost = pl.CostEstimate(
        flops=8 * size * tgt.shape[0] // 4,
        transcendentals=0,
        bytes_accessed=trans_table.size * 2 + 4 * size * (len(blocks) + 2),
    )
    return pl.pallas_call(
        functools.partial(pair_kernel, tuple(offsets), init is not None),
        out_shape=jax.ShapeDtypeStruct(shape, jnp.float32),
        in_specs=[smem] * 5 + [anywhere] * (1 + len(blocks) + len(extra)),
        out_specs=anywhere,
        scratch_shapes=[
            pltpu.VMEM(trans_table.shape, trans_table.dtype),
            pltpu.VMEM(((2 * REACH + 1) * box_dev,) + shape[1:], jnp.float32),
            pltpu.VMEM(shape, jnp.float32),
            pltpu.SemaphoreType.DMA((TABLE_PIECES + 1 + len(blocks),)),
            pltpu.SemaphoreType.DMA((1,)),
        ],
        input_output_aliases={} if init is None else {6 + len(blocks): 0},
        cost_estimate=cost,
        compiler_params=pltpu.CompilerParams(vmem_limit_bytes=66_000_000),
    )(tgt, src, cls, order, span, trans_table, *blocks, *extra)


def pair_lists(pair_near, pair_far, pair_class, pair_live):
    packed = jnp.stack([pair_near, pair_far, pair_class, pair_live])
    return [packed] + [passed_along(packed, "box", o) for o in range(1, REACH + 1)]


def pair_items(lists, pair_near, pair_far, pair_class, pair_live, box_dev, classes):
    tgt = [pair_near]
    src = [pair_far]
    cls = [pair_class]
    live = [pair_live]
    for o, lst in enumerate(lists):
        near, far, k, alive = lst[0], lst[1], lst[2], lst[3]
        tgt.append(far - o * box_dev)
        base = 0 if o == 0 else (REACH + o) * box_dev
        src.append(near + base)
        cls.append((k + classes // 2) % classes)
        live.append(jnp.where(far // box_dev == o, alive, 0))
    return [jnp.concatenate(x).astype(jnp.int32) for x in (tgt, src, cls, live)]


def body(
    child_pattern, octant, shift_angle, trans_table, pair_near, pair_far, pair_class, pair_live
):
    dir_count = lax.axis_size("dir")
    dir_index = lax.axis_index("dir")
    box_dev = child_pattern.shape[0] // 8
    classes = trans_table.shape[0]
    lists = pair_lists(pair_near, pair_far, pair_class, pair_live)
    theta_map = interp_rows(THETA1, THETA2, THETA2)
    phi_map = interp_rows(PHI1, PHI2, PHI2)
    cos_table = jnp.cos(shift_angle)
    sin_table = jnp.sin(shift_angle)
    grouped = child_pattern.reshape(box_dev, 8, 4, PHI1 // dir_count, THETA1)
    octants = octant.reshape(box_dev, 8)
    slots = jnp.arange(8, dtype=jnp.int32)
    by_octant = jnp.sum(
        jnp.where(octants[:, :, None] == slots[None, None, :], slots[None, :, None], 0), axis=1
    )
    chunks = 1
    while chunks < 4 and box_dev % (2 * chunks * dir_count) == 0:
        chunks *= 2
    per_chunk = box_dev // chunks
    per_dev = per_chunk // dir_count
    parts = []
    blocks = []
    offsets = []

    def send(c, part):
        moved = [part]
        moved += [passed_along(part, "box", -o) for o in range(1, REACH + 1)]
        moved += [passed_along(part, "box", o) for o in range(1, REACH + 1)]
        for b, block in enumerate(moved):
            blocks.append(block)
            offsets.append(b * box_dev + c * per_chunk)

    for c in range(chunks):
        piece = jnp.take_along_axis(
            grouped[c * per_chunk : (c + 1) * per_chunk],
            by_octant[c * per_chunk : (c + 1) * per_chunk, :, None, None, None],
            axis=1,
        )
        gathered = lax.all_to_all(piece, "dir", split_axis=0, concat_axis=3, tiled=True)
        if c >= 2:
            lo = (c - 2) * (2 * REACH + 1) + 1
            hi = (c - 1) * (2 * REACH + 1)
            sent, gathered = lax.optimization_barrier((blocks[lo:hi], gathered))
            blocks[lo:hi] = sent
        if parts:
            parts[-1], gathered = lax.optimization_barrier((parts[-1], gathered))
            send(c - 1, parts[-1])
        else:
            lists, gathered = lax.optimization_barrier((lists, gathered))
        full_dirs = interpolate(gathered, theta_map, phi_map)
        summed = shift_sum(full_dirs, cos_table, sin_table)
        parts.append(lax.all_to_all(summed, "dir", split_axis=2, concat_axis=0, tiled=True))
    send(chunks - 1, parts[-1])
    items = pair_items(lists, pair_near, pair_far, pair_class, pair_live, box_dev, classes)
    aggregated = jnp.concatenate(parts, axis=0) if chunks > 1 else parts[0]
    tgt, src, cls, live = items
    late = (src >= box_dev) & (src % box_dev >= (chunks - 1) * per_chunk)
    key = jnp.where(live != 0, late.astype(jnp.int32), 2)
    order = jnp.argsort(key, stable=True).astype(jnp.int32)
    n_early = jnp.sum(key == 0).astype(jnp.int32)
    n_live = n_early + jnp.sum(key == 1).astype(jnp.int32)
    early_items = (tgt, src, cls, order, jnp.stack([jnp.int32(0), n_early]))
    late_items = (tgt, src, cls, order, jnp.stack([n_early, n_live]))
    cut = len(blocks) - 2 * REACH
    partial = translate_pairs(early_items, trans_table, blocks[:cut], offsets[:cut], box_dev)
    incoming = translate_pairs(
        late_items, trans_table, blocks[cut:], offsets[cut:], box_dev, init=partial
    )
    return (aggregated, incoming)


def solution(mesh):
    placed = (
        P("box", None, "dir", None),
        P("box"),
        P(),
        P(None, None, "dir", None),
        P("box"),
        P("box"),
        P("box"),
        P("box"),
    )
    return jax.shard_map(
        body,
        mesh=mesh,
        in_specs=placed,
        out_specs=(P("box", None, "dir", None), P("box", None, "dir", None)),
        check_vma=False,
    )
```

```python
import functools
import math

import jax
import jax.numpy as jnp
from jax import lax
from jax.experimental import pallas as pl
from jax.experimental.pallas import tpu as pltpu
from jax.sharding import PartitionSpec as P

REACH = 2
THETA1 = 128
PHI1 = 128
THETA2 = 256
PHI2 = 256
ROWS = 16
TABLE_PIECES = 4


HIGHEST = lax.Precision.HIGHEST


def passed_along(value, axis, steps):
    count = lax.axis_size(axis)
    first, last = (max(0, -steps), min(count, count - steps))
    return lax.ppermute(value, axis, [(source, source + steps) for source in range(first, last)])


def interp_rows(size_in, size_out, count):
    target_pos = jnp.arange(count, dtype=jnp.int32)
    source_pos = jnp.arange(size_in, dtype=jnp.int32)
    offset = target_pos[:, None] - 2 * source_pos[None, :]
    is_odd = offset % 2 == 1
    safe_off = jnp.where(is_odd, offset, 1).astype(jnp.float32)
    kernel = jnp.sin(math.pi * safe_off / 2.0) / (size_in * jnp.tan(math.pi * safe_off / size_out))
    inner = jnp.where(is_odd, kernel, jnp.zeros_like(kernel))
    return jnp.where(offset == 0, jnp.ones_like(kernel), inner)


def interpolate(fields, theta_map, phi_map):
    widened = jnp.einsum("...t,ut->...u", fields, theta_map, precision=lax.Precision.HIGH)
    return jnp.einsum("qp,...pu->...qu", phi_map, widened, precision=lax.Precision.HIGH)


def select_rows(indices, table):
    count = table.shape[0]
    flat_ids = indices.reshape(-1)
    row_ids = jnp.arange(count, dtype=jnp.int32)
    onehot = (flat_ids[:, None] == row_ids[None, :]).astype(table.dtype)
    flat_table = table.reshape(count, -1)
    picked = jnp.dot(onehot, flat_table, precision=HIGHEST, preferred_element_type=jnp.float32)
    return picked.reshape(indices.shape + table.shape[1:])


def shift_sum(fields, cos_table, sin_table):
    groups = fields.shape[0]
    cosine = cos_table[None, :, None]
    sine = sin_table[None, :, None]
    shaped = fields.reshape(groups, 8, 2, 2, fields.shape[3], fields.shape[4])
    real_part = shaped[:, :, :, 0]
    imag_part = shaped[:, :, :, 1]
    new_real = jnp.sum(cosine * real_part - sine * imag_part, axis=1)
    new_imag = jnp.sum(sine * real_part + cosine * imag_part, axis=1)
    return jnp.stack([new_real, new_imag], axis=2).reshape(
        groups, 4, fields.shape[3], fields.shape[4]
    )


def pair_kernel(offsets, has_init, tgt_ref, src_ref, cls_ref, order_ref, span_ref, table_hbm, *rest):
    blocks = rest[: len(offsets)]
    out_hbm, table, sources, acc, sems, out_sem = rest[-6:]
    agg_hbm = None if has_init else rest[-7]
    if agg_hbm is not None:
        out_hbm, agg_hbm = agg_hbm, out_hbm
    rows = table.shape[2]
    classes = table.shape[0]
    pieces = [(p * classes // TABLE_PIECES, (p + 1) * classes // TABLE_PIECES) for p in range(TABLE_PIECES)]
    copies = [
        pltpu.make_async_copy(table_hbm.at[pl.ds(a, b - a)], table.at[pl.ds(a, b - a)], sems.at[p])
        for p, (a, b) in enumerate(pieces)
    ]
    for b, (block, first) in enumerate(zip(blocks, offsets)):
        copies.append(
            pltpu.make_async_copy(
                block, sources.at[pl.ds(first, block.shape[0])], sems.at[TABLE_PIECES + b]
            )
        )
    if has_init:
        copies.append(
            pltpu.make_async_copy(rest[len(offsets)], acc, sems.at[TABLE_PIECES + len(blocks)])
        )
    for c in copies:
        c.start()
    if not has_init:
        acc[...] = jnp.zeros_like(acc)
    for c in copies:
        c.wait()

    def item(i, carry):
        if True:
            j = order_ref[i]
            t = tgt_ref[j]
            s = src_ref[j]
            k = cls_ref[j]

            def chunk(j, inner):
                r0 = pl.multiple_of(j * ROWS, ROWS)
                win = pl.ds(r0, ROWS)
                tr = table[k, 0, win, :].astype(jnp.float32)
                ti = table[k, 1, win, :].astype(jnp.float32)
                for q in range(2):
                    pr = sources[s, 2 * q, win, :]
                    pi = sources[s, 2 * q + 1, win, :]
                    acc[t, 2 * q, win, :] += tr * pr - ti * pi
                    acc[t, 2 * q + 1, win, :] += ti * pr + tr * pi
                return inner

            lax.fori_loop(0, rows // ROWS, chunk, 0, unroll=True)

        return carry

    if agg_hbm is not None:
        local = pltpu.make_async_copy(sources.at[pl.ds(0, acc.shape[0])], agg_hbm, out_sem.at[1])
        local.start()
    lax.fori_loop(span_ref[0], span_ref[1], item, 0)
    done = pltpu.make_async_copy(acc, out_hbm, out_sem.at[0])
    done.start()
    done.wait()
    if agg_hbm is not None:
        local.wait()


def translate_pairs(items, trans_table, blocks, offsets, box_dev, init=None):
    tgt, src, cls, order, span = items
    shape = (box_dev,) + blocks[0].shape[1:]
    smem = pl.BlockSpec(memory_space=pltpu.SMEM)
    anywhere = pl.BlockSpec(memory_space=pl.ANY)
    extra = [] if init is None else [init]
    size = math.prod(shape)
    cost = pl.CostEstimate(
        flops=8 * size * tgt.shape[0] // 4,
        transcendentals=0,
        bytes_accessed=trans_table.size * 2 + 4 * size * (len(blocks) + 2),
    )
    return pl.pallas_call(
        functools.partial(pair_kernel, tuple(offsets), init is not None),
        out_shape=[jax.ShapeDtypeStruct(shape, jnp.float32)] * (1 if init is not None else 2),
        in_specs=[smem] * 5 + [anywhere] * (1 + len(blocks) + len(extra)),
        out_specs=[anywhere] * (1 if init is not None else 2),
        scratch_shapes=[
            pltpu.VMEM(trans_table.shape, trans_table.dtype),
            pltpu.VMEM(((2 * REACH + 1) * box_dev,) + shape[1:], jnp.float32),
            pltpu.VMEM(shape, jnp.float32),
            pltpu.SemaphoreType.DMA((TABLE_PIECES + 1 + len(blocks),)),
            pltpu.SemaphoreType.DMA((2,)),
        ],
        input_output_aliases={} if init is None else {6 + len(blocks): 0},
        cost_estimate=cost,
        compiler_params=pltpu.CompilerParams(vmem_limit_bytes=66_000_000),
    )(tgt, src, cls, order, span, trans_table, *blocks, *extra)


def pair_lists(pair_near, pair_far, pair_class, pair_live):
    packed = jnp.stack([pair_near, pair_far, pair_class, pair_live])
    return [packed] + [passed_along(packed, "box", o) for o in range(1, REACH + 1)]


def pair_items(lists, pair_near, pair_far, pair_class, pair_live, box_dev, classes):
    tgt = [pair_near]
    src = [pair_far]
    cls = [pair_class]
    live = [pair_live]
    for o, lst in enumerate(lists):
        near, far, k, alive = lst[0], lst[1], lst[2], lst[3]
        tgt.append(far - o * box_dev)
        base = 0 if o == 0 else (REACH + o) * box_dev
        src.append(near + base)
        cls.append((k + classes // 2) % classes)
        live.append(jnp.where(far // box_dev == o, alive, 0))
    return [jnp.concatenate(x).astype(jnp.int32) for x in (tgt, src, cls, live)]


def body(
    child_pattern, octant, shift_angle, trans_table, pair_near, pair_far, pair_class, pair_live
):
    dir_count = lax.axis_size("dir")
    dir_index = lax.axis_index("dir")
    box_dev = child_pattern.shape[0] // 8
    classes = trans_table.shape[0]
    lists = pair_lists(pair_near, pair_far, pair_class, pair_live)
    theta_map = interp_rows(THETA1, THETA2, THETA2)
    phi_map = interp_rows(PHI1, PHI2, PHI2)
    cos_table = jnp.cos(shift_angle)
    sin_table = jnp.sin(shift_angle)
    grouped = child_pattern.reshape(box_dev, 8, 4, PHI1 // dir_count, THETA1)
    octants = octant.reshape(box_dev, 8)
    slots = jnp.arange(8, dtype=jnp.int32)
    by_octant = jnp.sum(
        jnp.where(octants[:, :, None] == slots[None, None, :], slots[None, :, None], 0), axis=1
    )
    chunks = 1
    while chunks < 4 and box_dev % (2 * chunks * dir_count) == 0:
        chunks *= 2
    per_chunk = box_dev // chunks
    per_dev = per_chunk // dir_count
    parts = []
    blocks = []
    offsets = []

    def send(c, part):
        moved = [part]
        moved += [passed_along(part, "box", -o) for o in range(1, REACH + 1)]
        moved += [passed_along(part, "box", o) for o in range(1, REACH + 1)]
        for b, block in enumerate(moved):
            blocks.append(block)
            offsets.append(b * box_dev + c * per_chunk)

    for c in range(chunks):
        piece = jnp.take_along_axis(
            grouped[c * per_chunk : (c + 1) * per_chunk],
            by_octant[c * per_chunk : (c + 1) * per_chunk, :, None, None, None],
            axis=1,
        )
        gathered = lax.all_to_all(piece, "dir", split_axis=0, concat_axis=3, tiled=True)
        if c >= 2:
            lo = (c - 2) * (2 * REACH + 1) + 1
            hi = (c - 1) * (2 * REACH + 1)
            sent, gathered = lax.optimization_barrier((blocks[lo:hi], gathered))
            blocks[lo:hi] = sent
        if parts:
            parts[-1], gathered = lax.optimization_barrier((parts[-1], gathered))
            send(c - 1, parts[-1])
        else:
            lists, gathered = lax.optimization_barrier((lists, gathered))
        full_dirs = interpolate(gathered, theta_map, phi_map)
        summed = shift_sum(full_dirs, cos_table, sin_table)
        parts.append(lax.all_to_all(summed, "dir", split_axis=2, concat_axis=0, tiled=True))
    send(chunks - 1, parts[-1])
    items = pair_items(lists, pair_near, pair_far, pair_class, pair_live, box_dev, classes)
    tgt, src, cls, live = items
    late = (src >= box_dev) & (src % box_dev >= (chunks - 1) * per_chunk)
    key = jnp.where(live != 0, late.astype(jnp.int32), 2)
    order = jnp.argsort(key, stable=True).astype(jnp.int32)
    n_early = jnp.sum(key == 0).astype(jnp.int32)
    n_live = n_early + jnp.sum(key == 1).astype(jnp.int32)
    early_items = (tgt, src, cls, order, jnp.stack([jnp.int32(0), n_early]))
    late_items = (tgt, src, cls, order, jnp.stack([n_early, n_live]))
    cut = len(blocks) - 2 * REACH
    partial, aggregated = translate_pairs(
        early_items, trans_table, blocks[:cut], offsets[:cut], box_dev
    )
    (incoming,) = translate_pairs(
        late_items, trans_table, blocks[cut:], offsets[cut:], box_dev, init=partial
    )
    return (aggregated, incoming)


def solution(mesh):
    placed = (
        P("box", None, "dir", None),
        P("box"),
        P(),
        P(None, None, "dir", None),
        P("box"),
        P("box"),
        P("box"),
        P("box"),
    )
    return jax.shard_map(
        body,
        mesh=mesh,
        in_specs=placed,
        out_specs=(P("box", None, "dir", None), P("box", None, "dir", None)),
        check_vma=False,
    )
```

```python
import functools
import math

import jax
import jax.numpy as jnp
from jax import lax
from jax.experimental import pallas as pl
from jax.experimental.pallas import tpu as pltpu
from jax.sharding import PartitionSpec as P

REACH = 2
THETA1 = 128
PHI1 = 128
THETA2 = 256
PHI2 = 256
ROWS = 16
TABLE_PIECES = 4


HIGHEST = lax.Precision.HIGHEST


def passed_along(value, axis, steps):
    count = lax.axis_size(axis)
    first, last = (max(0, -steps), min(count, count - steps))
    return lax.ppermute(value, axis, [(source, source + steps) for source in range(first, last)])


def interp_rows(size_in, size_out, count):
    target_pos = jnp.arange(count, dtype=jnp.int32)
    source_pos = jnp.arange(size_in, dtype=jnp.int32)
    offset = target_pos[:, None] - 2 * source_pos[None, :]
    is_odd = offset % 2 == 1
    safe_off = jnp.where(is_odd, offset, 1).astype(jnp.float32)
    kernel = jnp.sin(math.pi * safe_off / 2.0) / (size_in * jnp.tan(math.pi * safe_off / size_out))
    inner = jnp.where(is_odd, kernel, jnp.zeros_like(kernel))
    return jnp.where(offset == 0, jnp.ones_like(kernel), inner)


def interpolate(fields, theta_map, phi_map):
    widened = jnp.einsum("...t,ut->...u", fields, theta_map, precision=lax.Precision.HIGH)
    return jnp.einsum("qp,...pu->...qu", phi_map, widened, precision=lax.Precision.HIGH)


def select_rows(indices, table):
    count = table.shape[0]
    flat_ids = indices.reshape(-1)
    row_ids = jnp.arange(count, dtype=jnp.int32)
    onehot = (flat_ids[:, None] == row_ids[None, :]).astype(table.dtype)
    flat_table = table.reshape(count, -1)
    picked = jnp.dot(onehot, flat_table, precision=HIGHEST, preferred_element_type=jnp.float32)
    return picked.reshape(indices.shape + table.shape[1:])


def shift_sum(fields, cos_table, sin_table):
    groups = fields.shape[0]
    cosine = cos_table[None, :, None]
    sine = sin_table[None, :, None]
    shaped = fields.reshape(groups, 8, 2, 2, fields.shape[3], fields.shape[4])
    real_part = shaped[:, :, :, 0]
    imag_part = shaped[:, :, :, 1]
    new_real = jnp.sum(cosine * real_part - sine * imag_part, axis=1)
    new_imag = jnp.sum(sine * real_part + cosine * imag_part, axis=1)
    return jnp.stack([new_real, new_imag], axis=2).reshape(
        groups, 4, fields.shape[3], fields.shape[4]
    )


def pair_kernel(offsets, has_init, tgt_ref, src_ref, cls_ref, order_ref, span_ref, table_hbm, *rest):
    blocks = rest[: len(offsets)]
    out_hbm, table, sources, acc, sems, out_sem = rest[-6:]
    agg_hbm = None if has_init else rest[-7]
    if agg_hbm is not None:
        out_hbm, agg_hbm = agg_hbm, out_hbm
    rows = table.shape[2]
    classes = table.shape[0]
    pieces = [(p * classes // TABLE_PIECES, (p + 1) * classes // TABLE_PIECES) for p in range(TABLE_PIECES)]
    copies = [
        pltpu.make_async_copy(table_hbm.at[pl.ds(a, b - a)], table.at[pl.ds(a, b - a)], sems.at[p])
        for p, (a, b) in enumerate(pieces)
    ]
    for b, (block, first) in enumerate(zip(blocks, offsets)):
        copies.append(
            pltpu.make_async_copy(
                block, sources.at[pl.ds(first, block.shape[0])], sems.at[TABLE_PIECES + b]
            )
        )
    if has_init:
        copies.append(
            pltpu.make_async_copy(rest[len(offsets)], acc, sems.at[TABLE_PIECES + len(blocks)])
        )
    for c in copies:
        c.start()
    if not has_init:
        acc[...] = jnp.zeros_like(acc)
    for c in copies[TABLE_PIECES:] if has_init else copies:
        c.wait()

    def item(i, carry, low=0, high=classes):
        j = order_ref[i]
        k = cls_ref[j]

        @pl.when((k >= low) & (k < high))
        def _():
            t = tgt_ref[j]
            s = src_ref[j]

            def chunk(j, inner):
                r0 = pl.multiple_of(j * ROWS, ROWS)
                win = pl.ds(r0, ROWS)
                tr = table[k, 0, win, :].astype(jnp.float32)
                ti = table[k, 1, win, :].astype(jnp.float32)
                for q in range(2):
                    pr = sources[s, 2 * q, win, :]
                    pi = sources[s, 2 * q + 1, win, :]
                    acc[t, 2 * q, win, :] += tr * pr - ti * pi
                    acc[t, 2 * q + 1, win, :] += ti * pr + tr * pi
                return inner

            lax.fori_loop(0, rows // ROWS, chunk, 0, unroll=True)

        return carry

    if agg_hbm is not None:
        local = pltpu.make_async_copy(sources.at[pl.ds(0, acc.shape[0])], agg_hbm, out_sem.at[1])
        local.start()
    if has_init:
        for p, (a, b) in enumerate(pieces):
            copies[p].wait()
            lax.fori_loop(
                span_ref[0], span_ref[1], functools.partial(item, low=a, high=b), 0
            )
    else:
        lax.fori_loop(span_ref[0], span_ref[1], item, 0)
    done = pltpu.make_async_copy(acc, out_hbm, out_sem.at[0])
    done.start()
    done.wait()
    if agg_hbm is not None:
        local.wait()


def translate_pairs(items, trans_table, blocks, offsets, box_dev, init=None):
    tgt, src, cls, order, span = items
    shape = (box_dev,) + blocks[0].shape[1:]
    smem = pl.BlockSpec(memory_space=pltpu.SMEM)
    anywhere = pl.BlockSpec(memory_space=pl.ANY)
    extra = [] if init is None else [init]
    size = math.prod(shape)
    cost = pl.CostEstimate(
        flops=8 * size * tgt.shape[0] // 4,
        transcendentals=0,
        bytes_accessed=trans_table.size * 2 + 4 * size * (len(blocks) + 2),
    )
    return pl.pallas_call(
        functools.partial(pair_kernel, tuple(offsets), init is not None),
        out_shape=[jax.ShapeDtypeStruct(shape, jnp.float32)] * (1 if init is not None else 2),
        in_specs=[smem] * 5 + [anywhere] * (1 + len(blocks) + len(extra)),
        out_specs=[anywhere] * (1 if init is not None else 2),
        scratch_shapes=[
            pltpu.VMEM(trans_table.shape, trans_table.dtype),
            pltpu.VMEM(((2 * REACH + 1) * box_dev,) + shape[1:], jnp.float32),
            pltpu.VMEM(shape, jnp.float32),
            pltpu.SemaphoreType.DMA((TABLE_PIECES + 1 + len(blocks),)),
            pltpu.SemaphoreType.DMA((2,)),
        ],
        input_output_aliases={} if init is None else {6 + len(blocks): 0},
        cost_estimate=cost,
        compiler_params=pltpu.CompilerParams(vmem_limit_bytes=66_000_000),
    )(tgt, src, cls, order, span, trans_table, *blocks, *extra)


def pair_lists(pair_near, pair_far, pair_class, pair_live):
    packed = jnp.stack([pair_near, pair_far, pair_class, pair_live])
    return [packed] + [passed_along(packed, "box", o) for o in range(1, REACH + 1)]


def pair_items(lists, pair_near, pair_far, pair_class, pair_live, box_dev, classes):
    tgt = [pair_near]
    src = [pair_far]
    cls = [pair_class]
    live = [pair_live]
    for o, lst in enumerate(lists):
        near, far, k, alive = lst[0], lst[1], lst[2], lst[3]
        tgt.append(far - o * box_dev)
        base = 0 if o == 0 else (REACH + o) * box_dev
        src.append(near + base)
        cls.append((k + classes // 2) % classes)
        live.append(jnp.where(far // box_dev == o, alive, 0))
    return [jnp.concatenate(x).astype(jnp.int32) for x in (tgt, src, cls, live)]


def body(
    child_pattern, octant, shift_angle, trans_table, pair_near, pair_far, pair_class, pair_live
):
    dir_count = lax.axis_size("dir")
    dir_index = lax.axis_index("dir")
    box_dev = child_pattern.shape[0] // 8
    classes = trans_table.shape[0]
    lists = pair_lists(pair_near, pair_far, pair_class, pair_live)
    theta_map = interp_rows(THETA1, THETA2, THETA2)
    phi_map = interp_rows(PHI1, PHI2, PHI2)
    cos_table = jnp.cos(shift_angle)
    sin_table = jnp.sin(shift_angle)
    grouped = child_pattern.reshape(box_dev, 8, 4, PHI1 // dir_count, THETA1)
    octants = octant.reshape(box_dev, 8)
    slots = jnp.arange(8, dtype=jnp.int32)
    by_octant = jnp.sum(
        jnp.where(octants[:, :, None] == slots[None, None, :], slots[None, :, None], 0), axis=1
    )
    chunks = 1
    while chunks < 4 and box_dev % (2 * chunks * dir_count) == 0:
        chunks *= 2
    per_chunk = box_dev // chunks
    per_dev = per_chunk // dir_count
    parts = []
    blocks = []
    offsets = []

    def send(c, part):
        moved = [part]
        moved += [passed_along(part, "box", -o) for o in range(1, REACH + 1)]
        moved += [passed_along(part, "box", o) for o in range(1, REACH + 1)]
        for b, block in enumerate(moved):
            blocks.append(block)
            offsets.append(b * box_dev + c * per_chunk)

    for c in range(chunks):
        piece = jnp.take_along_axis(
            grouped[c * per_chunk : (c + 1) * per_chunk],
            by_octant[c * per_chunk : (c + 1) * per_chunk, :, None, None, None],
            axis=1,
        )
        gathered = lax.all_to_all(piece, "dir", split_axis=0, concat_axis=3, tiled=True)
        if c >= 2:
            lo = (c - 2) * (2 * REACH + 1) + 1
            hi = (c - 1) * (2 * REACH + 1)
            sent, gathered = lax.optimization_barrier((blocks[lo:hi], gathered))
            blocks[lo:hi] = sent
        if parts:
            parts[-1], gathered = lax.optimization_barrier((parts[-1], gathered))
            send(c - 1, parts[-1])
        else:
            lists, gathered = lax.optimization_barrier((lists, gathered))
        full_dirs = interpolate(gathered, theta_map, phi_map)
        summed = shift_sum(full_dirs, cos_table, sin_table)
        parts.append(lax.all_to_all(summed, "dir", split_axis=2, concat_axis=0, tiled=True))
    send(chunks - 1, parts[-1])
    items = pair_items(lists, pair_near, pair_far, pair_class, pair_live, box_dev, classes)
    tgt, src, cls, live = items
    late = (src >= box_dev) & (src % box_dev >= (chunks - 1) * per_chunk)
    key = jnp.where(live != 0, late.astype(jnp.int32), 2)
    order = jnp.argsort(key, stable=True).astype(jnp.int32)
    n_early = jnp.sum(key == 0).astype(jnp.int32)
    n_live = n_early + jnp.sum(key == 1).astype(jnp.int32)
    early_items = (tgt, src, cls, order, jnp.stack([jnp.int32(0), n_early]))
    late_items = (tgt, src, cls, order, jnp.stack([n_early, n_live]))
    cut = len(blocks) - 2 * REACH
    partial, aggregated = translate_pairs(
        early_items, trans_table, blocks[:cut], offsets[:cut], box_dev
    )
    (incoming,) = translate_pairs(
        late_items, trans_table, blocks[cut:], offsets[cut:], box_dev, init=partial
    )
    return (aggregated, incoming)


def solution(mesh):
    placed = (
        P("box", None, "dir", None),
        P("box"),
        P(),
        P(None, None, "dir", None),
        P("box"),
        P("box"),
        P("box"),
        P("box"),
    )
    return jax.shard_map(
        body,
        mesh=mesh,
        in_specs=placed,
        out_specs=(P("box", None, "dir", None), P("box", None, "dir", None)),
        check_vma=False,
    )
```

```python
import functools
import math

import jax
import jax.numpy as jnp
from jax import lax
from jax.experimental import pallas as pl
from jax.experimental.pallas import tpu as pltpu
from jax.sharding import PartitionSpec as P

REACH = 2
THETA1 = 128
PHI1 = 128
THETA2 = 256
PHI2 = 256
ROWS = 16
TABLE_PIECES = 4


HIGHEST = lax.Precision.HIGHEST


def passed_along(value, axis, steps):
    count = lax.axis_size(axis)
    first, last = (max(0, -steps), min(count, count - steps))
    return lax.ppermute(value, axis, [(source, source + steps) for source in range(first, last)])


def interp_rows(size_in, size_out, count):
    target_pos = jnp.arange(count, dtype=jnp.int32)
    source_pos = jnp.arange(size_in, dtype=jnp.int32)
    offset = target_pos[:, None] - 2 * source_pos[None, :]
    is_odd = offset % 2 == 1
    safe_off = jnp.where(is_odd, offset, 1).astype(jnp.float32)
    kernel = jnp.sin(math.pi * safe_off / 2.0) / (size_in * jnp.tan(math.pi * safe_off / size_out))
    inner = jnp.where(is_odd, kernel, jnp.zeros_like(kernel))
    return jnp.where(offset == 0, jnp.ones_like(kernel), inner)


def interpolate(fields, theta_map, phi_map):
    widened = jnp.einsum("...t,ut->...u", fields, theta_map, precision=lax.Precision.HIGH)
    return jnp.einsum("qp,...pu->...qu", phi_map, widened, precision=lax.Precision.HIGH)


def select_rows(indices, table):
    count = table.shape[0]
    flat_ids = indices.reshape(-1)
    row_ids = jnp.arange(count, dtype=jnp.int32)
    onehot = (flat_ids[:, None] == row_ids[None, :]).astype(table.dtype)
    flat_table = table.reshape(count, -1)
    picked = jnp.dot(onehot, flat_table, precision=HIGHEST, preferred_element_type=jnp.float32)
    return picked.reshape(indices.shape + table.shape[1:])


def shift_sum(fields, cos_table, sin_table):
    groups = fields.shape[0]
    cosine = cos_table[None, :, None]
    sine = sin_table[None, :, None]
    shaped = fields.reshape(groups, 8, 2, 2, fields.shape[3], fields.shape[4])
    real_part = shaped[:, :, :, 0]
    imag_part = shaped[:, :, :, 1]
    new_real = jnp.sum(cosine * real_part - sine * imag_part, axis=1)
    new_imag = jnp.sum(sine * real_part + cosine * imag_part, axis=1)
    return jnp.stack([new_real, new_imag], axis=2).reshape(
        groups, 4, fields.shape[3], fields.shape[4]
    )


def pair_kernel(offsets, has_init, tgt_ref, src_ref, cls_ref, order_ref, span_ref, table_hbm, *rest):
    blocks = rest[: len(offsets)]
    out_hbm, table, sources, acc, sems, out_sem = rest[-6:]
    agg_hbm = None if has_init else rest[-7]
    if agg_hbm is not None:
        out_hbm, agg_hbm = agg_hbm, out_hbm
    rows = table.shape[2]
    classes = table.shape[0]
    pieces = [(p * classes // TABLE_PIECES, (p + 1) * classes // TABLE_PIECES) for p in range(TABLE_PIECES)]
    copies = [
        pltpu.make_async_copy(table_hbm.at[pl.ds(a, b - a)], table.at[pl.ds(a, b - a)], sems.at[p])
        for p, (a, b) in enumerate(pieces)
    ]
    for b, (block, first) in enumerate(zip(blocks, offsets)):
        copies.append(
            pltpu.make_async_copy(
                block, sources.at[pl.ds(first, block.shape[0])], sems.at[TABLE_PIECES + b]
            )
        )
    if has_init:
        copies.append(
            pltpu.make_async_copy(rest[len(offsets)], acc, sems.at[TABLE_PIECES + len(blocks)])
        )
    for c in copies:
        c.start()
    if not has_init:
        acc[...] = jnp.zeros_like(acc)
    for c in copies:
        c.wait()

    def item(i, carry):
        if True:
            j = order_ref[i]
            t = tgt_ref[j]
            s = src_ref[j]
            k = cls_ref[j]

            def chunk(j, inner):
                r0 = pl.multiple_of(j * ROWS, ROWS)
                win = pl.ds(r0, ROWS)
                tr = table[k, 0, win, :].astype(jnp.float32)
                ti = table[k, 1, win, :].astype(jnp.float32)
                for q in range(2):
                    pr = sources[s, 2 * q, win, :]
                    pi = sources[s, 2 * q + 1, win, :]
                    acc[t, 2 * q, win, :] += tr * pr - ti * pi
                    acc[t, 2 * q + 1, win, :] += ti * pr + tr * pi
                return inner

            lax.fori_loop(0, rows // ROWS, chunk, 0, unroll=True)

        return carry

    if agg_hbm is not None:
        local = pltpu.make_async_copy(sources.at[pl.ds(0, acc.shape[0])], agg_hbm, out_sem.at[1])
        local.start()
    lax.fori_loop(span_ref[0], span_ref[1], item, 0)
    done = pltpu.make_async_copy(acc, out_hbm, out_sem.at[0])
    done.start()
    done.wait()
    if agg_hbm is not None:
        local.wait()


def translate_pairs(items, trans_table, blocks, offsets, box_dev, init=None):
    tgt, src, cls, order, span = items
    shape = (box_dev,) + blocks[0].shape[1:]
    smem = pl.BlockSpec(memory_space=pltpu.SMEM)
    anywhere = pl.BlockSpec(memory_space=pl.ANY)
    extra = [] if init is None else [init]
    size = math.prod(shape)
    cost = pl.CostEstimate(
        flops=8 * size * tgt.shape[0] // 4,
        transcendentals=0,
        bytes_accessed=trans_table.size * 2 + 4 * size * (len(blocks) + 2),
    )
    return pl.pallas_call(
        functools.partial(pair_kernel, tuple(offsets), init is not None),
        out_shape=[jax.ShapeDtypeStruct(shape, jnp.float32)] * (1 if init is not None else 2),
        in_specs=[smem] * 5 + [anywhere] * (1 + len(blocks) + len(extra)),
        out_specs=[anywhere] * (1 if init is not None else 2),
        scratch_shapes=[
            pltpu.VMEM(trans_table.shape, trans_table.dtype),
            pltpu.VMEM(((2 * REACH + 1) * box_dev,) + shape[1:], jnp.float32),
            pltpu.VMEM(shape, jnp.float32),
            pltpu.SemaphoreType.DMA((TABLE_PIECES + 1 + len(blocks),)),
            pltpu.SemaphoreType.DMA((2,)),
        ],
        input_output_aliases={} if init is None else {6 + len(blocks): 0},
        cost_estimate=cost,
        compiler_params=pltpu.CompilerParams(vmem_limit_bytes=66_000_000),
    )(tgt, src, cls, order, span, trans_table, *blocks, *extra)


def pair_lists(pair_near, pair_far, pair_class, pair_live):
    packed = jnp.stack([pair_near, pair_far, pair_class, pair_live])
    return [packed] + [passed_along(packed, "box", o) for o in range(1, REACH + 1)]


def pair_items(lists, pair_near, pair_far, pair_class, pair_live, box_dev, classes):
    tgt = [pair_near]
    src = [pair_far]
    cls = [pair_class]
    live = [pair_live]
    for o, lst in enumerate(lists):
        near, far, k, alive = lst[0], lst[1], lst[2], lst[3]
        tgt.append(far - o * box_dev)
        base = 0 if o == 0 else (REACH + o) * box_dev
        src.append(near + base)
        cls.append((k + classes // 2) % classes)
        live.append(jnp.where(far // box_dev == o, alive, 0))
    return [jnp.concatenate(x).astype(jnp.int32) for x in (tgt, src, cls, live)]


def body(
    child_pattern, octant, shift_angle, trans_table, pair_near, pair_far, pair_class, pair_live
):
    dir_count = lax.axis_size("dir")
    dir_index = lax.axis_index("dir")
    box_dev = child_pattern.shape[0] // 8
    classes = trans_table.shape[0]
    lists = pair_lists(pair_near, pair_far, pair_class, pair_live)
    theta_map = interp_rows(THETA1, THETA2, THETA2)
    phi_map = interp_rows(PHI1, PHI2, PHI2)
    cos_table = jnp.cos(shift_angle)
    sin_table = jnp.sin(shift_angle)
    grouped = child_pattern.reshape(box_dev, 8, 4, PHI1 // dir_count, THETA1)
    octants = octant.reshape(box_dev, 8)
    slots = jnp.arange(8, dtype=jnp.int32)
    by_octant = jnp.sum(
        jnp.where(octants[:, :, None] == slots[None, None, :], slots[None, :, None], 0), axis=1
    )
    chunks = 1
    while chunks < 4 and box_dev % (2 * chunks * dir_count) == 0:
        chunks *= 2
    per_chunk = box_dev // chunks
    per_dev = per_chunk // dir_count
    parts = []
    blocks = []
    offsets = []

    def send(c, part):
        moved = [part]
        moved += [passed_along(part, "box", -o) for o in range(1, REACH + 1)]
        moved += [passed_along(part, "box", o) for o in range(1, REACH + 1)]
        for b, block in enumerate(moved):
            blocks.append(block)
            offsets.append(b * box_dev + c * per_chunk)

    for c in range(chunks):
        owners = c * per_chunk + jnp.arange(per_chunk, dtype=jnp.int32)
        piece = grouped[owners[:, None], by_octant[c * per_chunk : (c + 1) * per_chunk]]
        gathered = lax.all_to_all(piece, "dir", split_axis=0, concat_axis=3, tiled=True)
        if c >= 2:
            lo = (c - 2) * (2 * REACH + 1) + 1
            hi = (c - 1) * (2 * REACH + 1)
            sent, gathered = lax.optimization_barrier((blocks[lo:hi], gathered))
            blocks[lo:hi] = sent
        if parts:
            parts[-1], gathered = lax.optimization_barrier((parts[-1], gathered))
            send(c - 1, parts[-1])
        else:
            lists, gathered = lax.optimization_barrier((lists, gathered))
        full_dirs = interpolate(gathered, theta_map, phi_map)
        summed = shift_sum(full_dirs, cos_table, sin_table)
        parts.append(lax.all_to_all(summed, "dir", split_axis=2, concat_axis=0, tiled=True))
    send(chunks - 1, parts[-1])
    items = pair_items(lists, pair_near, pair_far, pair_class, pair_live, box_dev, classes)
    tgt, src, cls, live = items
    late = (src >= box_dev) & (src % box_dev >= (chunks - 1) * per_chunk)
    key = jnp.where(live != 0, late.astype(jnp.int32), 2)
    order = jnp.argsort(key, stable=True).astype(jnp.int32)
    n_early = jnp.sum(key == 0).astype(jnp.int32)
    n_live = n_early + jnp.sum(key == 1).astype(jnp.int32)
    early_items = (tgt, src, cls, order, jnp.stack([jnp.int32(0), n_early]))
    late_items = (tgt, src, cls, order, jnp.stack([n_early, n_live]))
    cut = len(blocks) - 2 * REACH
    partial, aggregated = translate_pairs(
        early_items, trans_table, blocks[:cut], offsets[:cut], box_dev
    )
    (incoming,) = translate_pairs(
        late_items, trans_table, blocks[cut:], offsets[cut:], box_dev, init=partial
    )
    return (aggregated, incoming)


def solution(mesh):
    placed = (
        P("box", None, "dir", None),
        P("box"),
        P(),
        P(None, None, "dir", None),
        P("box"),
        P("box"),
        P("box"),
        P("box"),
    )
    return jax.shard_map(
        body,
        mesh=mesh,
        in_specs=placed,
        out_specs=(P("box", None, "dir", None), P("box", None, "dir", None)),
        check_vma=False,
    )
```

```python
import functools
import math

import jax
import jax.numpy as jnp
from jax import lax
from jax.experimental import pallas as pl
from jax.experimental.pallas import tpu as pltpu
from jax.sharding import PartitionSpec as P

REACH = 2
THETA1 = 128
PHI1 = 128
THETA2 = 256
PHI2 = 256
ROWS = 32
TABLE_PIECES = 4


HIGHEST = lax.Precision.HIGHEST


def passed_along(value, axis, steps):
    count = lax.axis_size(axis)
    first, last = (max(0, -steps), min(count, count - steps))
    return lax.ppermute(value, axis, [(source, source + steps) for source in range(first, last)])


def interp_rows(size_in, size_out, count):
    target_pos = jnp.arange(count, dtype=jnp.int32)
    source_pos = jnp.arange(size_in, dtype=jnp.int32)
    offset = target_pos[:, None] - 2 * source_pos[None, :]
    is_odd = offset % 2 == 1
    safe_off = jnp.where(is_odd, offset, 1).astype(jnp.float32)
    kernel = jnp.sin(math.pi * safe_off / 2.0) / (size_in * jnp.tan(math.pi * safe_off / size_out))
    inner = jnp.where(is_odd, kernel, jnp.zeros_like(kernel))
    return jnp.where(offset == 0, jnp.ones_like(kernel), inner)


def interpolate(fields, theta_map, phi_map):
    widened = jnp.einsum("...t,ut->...u", fields, theta_map, precision=lax.Precision.HIGH)
    return jnp.einsum("qp,...pu->...qu", phi_map, widened, precision=lax.Precision.HIGH)


def select_rows(indices, table):
    count = table.shape[0]
    flat_ids = indices.reshape(-1)
    row_ids = jnp.arange(count, dtype=jnp.int32)
    onehot = (flat_ids[:, None] == row_ids[None, :]).astype(table.dtype)
    flat_table = table.reshape(count, -1)
    picked = jnp.dot(onehot, flat_table, precision=HIGHEST, preferred_element_type=jnp.float32)
    return picked.reshape(indices.shape + table.shape[1:])


def shift_sum(fields, cos_table, sin_table):
    groups = fields.shape[0]
    cosine = cos_table[None, :, None]
    sine = sin_table[None, :, None]
    shaped = fields.reshape(groups, 8, 2, 2, fields.shape[3], fields.shape[4])
    real_part = shaped[:, :, :, 0]
    imag_part = shaped[:, :, :, 1]
    new_real = jnp.sum(cosine * real_part - sine * imag_part, axis=1)
    new_imag = jnp.sum(sine * real_part + cosine * imag_part, axis=1)
    return jnp.stack([new_real, new_imag], axis=2).reshape(
        groups, 4, fields.shape[3], fields.shape[4]
    )


def pair_kernel(offsets, has_init, tgt_ref, src_ref, cls_ref, order_ref, span_ref, table_hbm, *rest):
    blocks = rest[: len(offsets)]
    out_hbm, table, sources, acc, sems, out_sem = rest[-6:]
    agg_hbm = None if has_init else rest[-7]
    if agg_hbm is not None:
        out_hbm, agg_hbm = agg_hbm, out_hbm
    rows = table.shape[2]
    classes = table.shape[0]
    pieces = [(p * classes // TABLE_PIECES, (p + 1) * classes // TABLE_PIECES) for p in range(TABLE_PIECES)]
    copies = [
        pltpu.make_async_copy(table_hbm.at[pl.ds(a, b - a)], table.at[pl.ds(a, b - a)], sems.at[p])
        for p, (a, b) in enumerate(pieces)
    ]
    for b, (block, first) in enumerate(zip(blocks, offsets)):
        copies.append(
            pltpu.make_async_copy(
                block, sources.at[pl.ds(first, block.shape[0])], sems.at[TABLE_PIECES + b]
            )
        )
    if has_init:
        copies.append(
            pltpu.make_async_copy(rest[len(offsets)], acc, sems.at[TABLE_PIECES + len(blocks)])
        )
    for c in copies:
        c.start()
    if not has_init:
        acc[...] = jnp.zeros_like(acc)
    for c in copies:
        c.wait()

    def item(i, carry):
        if True:
            j = order_ref[i]
            t = tgt_ref[j]
            s = src_ref[j]
            k = cls_ref[j]

            def chunk(j, inner):
                r0 = pl.multiple_of(j * ROWS, ROWS)
                win = pl.ds(r0, ROWS)
                tr = table[k, 0, win, :].astype(jnp.float32)
                ti = table[k, 1, win, :].astype(jnp.float32)
                for q in range(2):
                    pr = sources[s, 2 * q, win, :]
                    pi = sources[s, 2 * q + 1, win, :]
                    acc[t, 2 * q, win, :] += tr * pr - ti * pi
                    acc[t, 2 * q + 1, win, :] += ti * pr + tr * pi
                return inner

            lax.fori_loop(0, rows // ROWS, chunk, 0, unroll=True)

        return carry

    if agg_hbm is not None:
        local = pltpu.make_async_copy(sources.at[pl.ds(0, acc.shape[0])], agg_hbm, out_sem.at[1])
        local.start()
    lax.fori_loop(span_ref[0], span_ref[1], item, 0)
    done = pltpu.make_async_copy(acc, out_hbm, out_sem.at[0])
    done.start()
    done.wait()
    if agg_hbm is not None:
        local.wait()


def translate_pairs(items, trans_table, blocks, offsets, box_dev, init=None):
    tgt, src, cls, order, span = items
    shape = (box_dev,) + blocks[0].shape[1:]
    smem = pl.BlockSpec(memory_space=pltpu.SMEM)
    anywhere = pl.BlockSpec(memory_space=pl.ANY)
    extra = [] if init is None else [init]
    size = math.prod(shape)
    cost = pl.CostEstimate(
        flops=8 * size * tgt.shape[0] // 4,
        transcendentals=0,
        bytes_accessed=trans_table.size * 2 + 4 * size * (len(blocks) + 2),
    )
    return pl.pallas_call(
        functools.partial(pair_kernel, tuple(offsets), init is not None),
        out_shape=[jax.ShapeDtypeStruct(shape, jnp.float32)] * (1 if init is not None else 2),
        in_specs=[smem] * 5 + [anywhere] * (1 + len(blocks) + len(extra)),
        out_specs=[anywhere] * (1 if init is not None else 2),
        scratch_shapes=[
            pltpu.VMEM(trans_table.shape, trans_table.dtype),
            pltpu.VMEM(((2 * REACH + 1) * box_dev,) + shape[1:], jnp.float32),
            pltpu.VMEM(shape, jnp.float32),
            pltpu.SemaphoreType.DMA((TABLE_PIECES + 1 + len(blocks),)),
            pltpu.SemaphoreType.DMA((2,)),
        ],
        input_output_aliases={} if init is None else {6 + len(blocks): 0},
        cost_estimate=cost,
        compiler_params=pltpu.CompilerParams(vmem_limit_bytes=66_000_000),
    )(tgt, src, cls, order, span, trans_table, *blocks, *extra)


def pair_lists(pair_near, pair_far, pair_class, pair_live):
    packed = jnp.stack([pair_near, pair_far, pair_class, pair_live])
    return [packed] + [passed_along(packed, "box", o) for o in range(1, REACH + 1)]


def pair_items(lists, pair_near, pair_far, pair_class, pair_live, box_dev, classes):
    tgt = [pair_near]
    src = [pair_far]
    cls = [pair_class]
    live = [pair_live]
    for o, lst in enumerate(lists):
        near, far, k, alive = lst[0], lst[1], lst[2], lst[3]
        tgt.append(far - o * box_dev)
        base = 0 if o == 0 else (REACH + o) * box_dev
        src.append(near + base)
        cls.append((k + classes // 2) % classes)
        live.append(jnp.where(far // box_dev == o, alive, 0))
    return [jnp.concatenate(x).astype(jnp.int32) for x in (tgt, src, cls, live)]


def body(
    child_pattern, octant, shift_angle, trans_table, pair_near, pair_far, pair_class, pair_live
):
    dir_count = lax.axis_size("dir")
    dir_index = lax.axis_index("dir")
    box_dev = child_pattern.shape[0] // 8
    classes = trans_table.shape[0]
    lists = pair_lists(pair_near, pair_far, pair_class, pair_live)
    theta_map = interp_rows(THETA1, THETA2, THETA2)
    phi_map = interp_rows(PHI1, PHI2, PHI2)
    cos_table = jnp.cos(shift_angle)
    sin_table = jnp.sin(shift_angle)
    grouped = child_pattern.reshape(box_dev, 8, 4, PHI1 // dir_count, THETA1)
    octants = octant.reshape(box_dev, 8)
    slots = jnp.arange(8, dtype=jnp.int32)
    by_octant = jnp.sum(
        jnp.where(octants[:, :, None] == slots[None, None, :], slots[None, :, None], 0), axis=1
    )
    chunks = 1
    while chunks < 4 and box_dev % (2 * chunks * dir_count) == 0:
        chunks *= 2
    per_chunk = box_dev // chunks
    per_dev = per_chunk // dir_count
    parts = []
    blocks = []
    offsets = []

    def send(c, part):
        moved = [part]
        moved += [passed_along(part, "box", -o) for o in range(1, REACH + 1)]
        moved += [passed_along(part, "box", o) for o in range(1, REACH + 1)]
        for b, block in enumerate(moved):
            blocks.append(block)
            offsets.append(b * box_dev + c * per_chunk)

    for c in range(chunks):
        owners = c * per_chunk + jnp.arange(per_chunk, dtype=jnp.int32)
        piece = grouped[owners[:, None], by_octant[c * per_chunk : (c + 1) * per_chunk]]
        gathered = lax.all_to_all(piece, "dir", split_axis=0, concat_axis=3, tiled=True)
        if c >= 2:
            lo = (c - 2) * (2 * REACH + 1) + 1
            hi = (c - 1) * (2 * REACH + 1)
            sent, gathered = lax.optimization_barrier((blocks[lo:hi], gathered))
            blocks[lo:hi] = sent
        if parts:
            parts[-1], gathered = lax.optimization_barrier((parts[-1], gathered))
            send(c - 1, parts[-1])
        else:
            lists, gathered = lax.optimization_barrier((lists, gathered))
        full_dirs = interpolate(gathered, theta_map, phi_map)
        summed = shift_sum(full_dirs, cos_table, sin_table)
        parts.append(lax.all_to_all(summed, "dir", split_axis=2, concat_axis=0, tiled=True))
    send(chunks - 1, parts[-1])
    items = pair_items(lists, pair_near, pair_far, pair_class, pair_live, box_dev, classes)
    tgt, src, cls, live = items
    late = (src >= box_dev) & (src % box_dev >= (chunks - 1) * per_chunk)
    key = jnp.where(live != 0, late.astype(jnp.int32), 2)
    order = jnp.argsort(key, stable=True).astype(jnp.int32)
    n_early = jnp.sum(key == 0).astype(jnp.int32)
    n_live = n_early + jnp.sum(key == 1).astype(jnp.int32)
    early_items = (tgt, src, cls, order, jnp.stack([jnp.int32(0), n_early]))
    late_items = (tgt, src, cls, order, jnp.stack([n_early, n_live]))
    cut = len(blocks) - 2 * REACH
    partial, aggregated = translate_pairs(
        early_items, trans_table, blocks[:cut], offsets[:cut], box_dev
    )
    (incoming,) = translate_pairs(
        late_items, trans_table, blocks[cut:], offsets[cut:], box_dev, init=partial
    )
    return (aggregated, incoming)


def solution(mesh):
    placed = (
        P("box", None, "dir", None),
        P("box"),
        P(),
        P(None, None, "dir", None),
        P("box"),
        P("box"),
        P("box"),
        P("box"),
    )
    return jax.shard_map(
        body,
        mesh=mesh,
        in_specs=placed,
        out_specs=(P("box", None, "dir", None), P("box", None, "dir", None)),
        check_vma=False,
    )
```

```python
import functools
import math

import jax
import jax.numpy as jnp
from jax import lax
from jax.experimental import pallas as pl
from jax.experimental.pallas import tpu as pltpu
from jax.sharding import PartitionSpec as P

REACH = 2
THETA1 = 128
PHI1 = 128
THETA2 = 256
PHI2 = 256
ROWS = 32
TABLE_PIECES = 8


HIGHEST = lax.Precision.HIGHEST


def passed_along(value, axis, steps):
    count = lax.axis_size(axis)
    first, last = (max(0, -steps), min(count, count - steps))
    return lax.ppermute(value, axis, [(source, source + steps) for source in range(first, last)])


def interp_rows(size_in, size_out, count):
    target_pos = jnp.arange(count, dtype=jnp.int32)
    source_pos = jnp.arange(size_in, dtype=jnp.int32)
    offset = target_pos[:, None] - 2 * source_pos[None, :]
    is_odd = offset % 2 == 1
    safe_off = jnp.where(is_odd, offset, 1).astype(jnp.float32)
    kernel = jnp.sin(math.pi * safe_off / 2.0) / (size_in * jnp.tan(math.pi * safe_off / size_out))
    inner = jnp.where(is_odd, kernel, jnp.zeros_like(kernel))
    return jnp.where(offset == 0, jnp.ones_like(kernel), inner)


def interpolate(fields, theta_map, phi_map):
    widened = jnp.einsum("...t,ut->...u", fields, theta_map, precision=lax.Precision.HIGH)
    return jnp.einsum("qp,...pu->...qu", phi_map, widened, precision=lax.Precision.HIGH)


def select_rows(indices, table):
    count = table.shape[0]
    flat_ids = indices.reshape(-1)
    row_ids = jnp.arange(count, dtype=jnp.int32)
    onehot = (flat_ids[:, None] == row_ids[None, :]).astype(table.dtype)
    flat_table = table.reshape(count, -1)
    picked = jnp.dot(onehot, flat_table, precision=HIGHEST, preferred_element_type=jnp.float32)
    return picked.reshape(indices.shape + table.shape[1:])


def shift_sum(fields, cos_table, sin_table):
    groups = fields.shape[0]
    cosine = cos_table[None, :, None]
    sine = sin_table[None, :, None]
    shaped = fields.reshape(groups, 8, 2, 2, fields.shape[3], fields.shape[4])
    real_part = shaped[:, :, :, 0]
    imag_part = shaped[:, :, :, 1]
    new_real = jnp.sum(cosine * real_part - sine * imag_part, axis=1)
    new_imag = jnp.sum(sine * real_part + cosine * imag_part, axis=1)
    return jnp.stack([new_real, new_imag], axis=2).reshape(
        groups, 4, fields.shape[3], fields.shape[4]
    )


def pair_kernel(offsets, has_init, tgt_ref, src_ref, cls_ref, order_ref, span_ref, table_hbm, *rest):
    blocks = rest[: len(offsets)]
    out_hbm, table, sources, acc, sems, out_sem = rest[-6:]
    agg_hbm = None if has_init else rest[-7]
    if agg_hbm is not None:
        out_hbm, agg_hbm = agg_hbm, out_hbm
    rows = table.shape[2]
    classes = table.shape[0]
    pieces = [(p * classes // TABLE_PIECES, (p + 1) * classes // TABLE_PIECES) for p in range(TABLE_PIECES)]
    copies = [
        pltpu.make_async_copy(table_hbm.at[pl.ds(a, b - a)], table.at[pl.ds(a, b - a)], sems.at[p])
        for p, (a, b) in enumerate(pieces)
    ]
    for b, (block, first) in enumerate(zip(blocks, offsets)):
        copies.append(
            pltpu.make_async_copy(
                block, sources.at[pl.ds(first, block.shape[0])], sems.at[TABLE_PIECES + b]
            )
        )
    if has_init:
        copies.append(
            pltpu.make_async_copy(rest[len(offsets)], acc, sems.at[TABLE_PIECES + len(blocks)])
        )
    for c in copies:
        c.start()
    if not has_init:
        acc[...] = jnp.zeros_like(acc)
    for c in copies:
        c.wait()

    def item(i, carry):
        if True:
            j = order_ref[i]
            t = tgt_ref[j]
            s = src_ref[j]
            k = cls_ref[j]

            def chunk(j, inner):
                r0 = pl.multiple_of(j * ROWS, ROWS)
                win = pl.ds(r0, ROWS)
                tr = table[k, 0, win, :].astype(jnp.float32)
                ti = table[k, 1, win, :].astype(jnp.float32)
                for q in range(2):
                    pr = sources[s, 2 * q, win, :]
                    pi = sources[s, 2 * q + 1, win, :]
                    acc[t, 2 * q, win, :] += tr * pr - ti * pi
                    acc[t, 2 * q + 1, win, :] += ti * pr + tr * pi
                return inner

            lax.fori_loop(0, rows // ROWS, chunk, 0, unroll=True)

        return carry

    if agg_hbm is not None:
        local = pltpu.make_async_copy(sources.at[pl.ds(0, acc.shape[0])], agg_hbm, out_sem.at[1])
        local.start()
    lax.fori_loop(span_ref[0], span_ref[1], item, 0)
    done = pltpu.make_async_copy(acc, out_hbm, out_sem.at[0])
    done.start()
    done.wait()
    if agg_hbm is not None:
        local.wait()


def translate_pairs(items, trans_table, blocks, offsets, box_dev, init=None):
    tgt, src, cls, order, span = items
    shape = (box_dev,) + blocks[0].shape[1:]
    smem = pl.BlockSpec(memory_space=pltpu.SMEM)
    anywhere = pl.BlockSpec(memory_space=pl.ANY)
    extra = [] if init is None else [init]
    size = math.prod(shape)
    cost = pl.CostEstimate(
        flops=8 * size * tgt.shape[0] // 4,
        transcendentals=0,
        bytes_accessed=trans_table.size * 2 + 4 * size * (len(blocks) + 2),
    )
    return pl.pallas_call(
        functools.partial(pair_kernel, tuple(offsets), init is not None),
        out_shape=[jax.ShapeDtypeStruct(shape, jnp.float32)] * (1 if init is not None else 2),
        in_specs=[smem] * 5 + [anywhere] * (1 + len(blocks) + len(extra)),
        out_specs=[anywhere] * (1 if init is not None else 2),
        scratch_shapes=[
            pltpu.VMEM(trans_table.shape, trans_table.dtype),
            pltpu.VMEM(((2 * REACH + 1) * box_dev,) + shape[1:], jnp.float32),
            pltpu.VMEM(shape, jnp.float32),
            pltpu.SemaphoreType.DMA((TABLE_PIECES + 1 + len(blocks),)),
            pltpu.SemaphoreType.DMA((2,)),
        ],
        input_output_aliases={} if init is None else {6 + len(blocks): 0},
        cost_estimate=cost,
        compiler_params=pltpu.CompilerParams(vmem_limit_bytes=66_000_000),
    )(tgt, src, cls, order, span, trans_table, *blocks, *extra)


def pair_lists(pair_near, pair_far, pair_class, pair_live):
    packed = jnp.stack([pair_near, pair_far, pair_class, pair_live])
    return [packed] + [passed_along(packed, "box", o) for o in range(1, REACH + 1)]


def pair_items(lists, pair_near, pair_far, pair_class, pair_live, box_dev, classes):
    tgt = [pair_near]
    src = [pair_far]
    cls = [pair_class]
    live = [pair_live]
    for o, lst in enumerate(lists):
        near, far, k, alive = lst[0], lst[1], lst[2], lst[3]
        tgt.append(far - o * box_dev)
        base = 0 if o == 0 else (REACH + o) * box_dev
        src.append(near + base)
        cls.append((k + classes // 2) % classes)
        live.append(jnp.where(far // box_dev == o, alive, 0))
    return [jnp.concatenate(x).astype(jnp.int32) for x in (tgt, src, cls, live)]


def body(
    child_pattern, octant, shift_angle, trans_table, pair_near, pair_far, pair_class, pair_live
):
    dir_count = lax.axis_size("dir")
    dir_index = lax.axis_index("dir")
    box_dev = child_pattern.shape[0] // 8
    classes = trans_table.shape[0]
    lists = pair_lists(pair_near, pair_far, pair_class, pair_live)
    theta_map = interp_rows(THETA1, THETA2, THETA2)
    phi_map = interp_rows(PHI1, PHI2, PHI2)
    cos_table = jnp.cos(shift_angle)
    sin_table = jnp.sin(shift_angle)
    grouped = child_pattern.reshape(box_dev, 8, 4, PHI1 // dir_count, THETA1)
    octants = octant.reshape(box_dev, 8)
    slots = jnp.arange(8, dtype=jnp.int32)
    by_octant = jnp.sum(
        jnp.where(octants[:, :, None] == slots[None, None, :], slots[None, :, None], 0), axis=1
    )
    chunks = 1
    while chunks < 4 and box_dev % (2 * chunks * dir_count) == 0:
        chunks *= 2
    per_chunk = box_dev // chunks
    per_dev = per_chunk // dir_count
    parts = []
    blocks = []
    offsets = []

    def send(c, part):
        moved = [part]
        moved += [passed_along(part, "box", -o) for o in range(1, REACH + 1)]
        moved += [passed_along(part, "box", o) for o in range(1, REACH + 1)]
        for b, block in enumerate(moved):
            blocks.append(block)
            offsets.append(b * box_dev + c * per_chunk)

    for c in range(chunks):
        owners = c * per_chunk + jnp.arange(per_chunk, dtype=jnp.int32)
        piece = grouped[owners[:, None], by_octant[c * per_chunk : (c + 1) * per_chunk]]
        gathered = lax.all_to_all(piece, "dir", split_axis=0, concat_axis=3, tiled=True)
        if c >= 2:
            lo = (c - 2) * (2 * REACH + 1) + 1
            hi = (c - 1) * (2 * REACH + 1)
            sent, gathered = lax.optimization_barrier((blocks[lo:hi], gathered))
            blocks[lo:hi] = sent
        if parts:
            parts[-1], gathered = lax.optimization_barrier((parts[-1], gathered))
            send(c - 1, parts[-1])
        else:
            lists, gathered = lax.optimization_barrier((lists, gathered))
        full_dirs = interpolate(gathered, theta_map, phi_map)
        summed = shift_sum(full_dirs, cos_table, sin_table)
        parts.append(lax.all_to_all(summed, "dir", split_axis=2, concat_axis=0, tiled=True))
    send(chunks - 1, parts[-1])
    items = pair_items(lists, pair_near, pair_far, pair_class, pair_live, box_dev, classes)
    tgt, src, cls, live = items
    late = (src >= box_dev) & (src % box_dev >= (chunks - 1) * per_chunk)
    key = jnp.where(live != 0, late.astype(jnp.int32), 2)
    order = jnp.argsort(key, stable=True).astype(jnp.int32)
    n_early = jnp.sum(key == 0).astype(jnp.int32)
    n_live = n_early + jnp.sum(key == 1).astype(jnp.int32)
    early_items = (tgt, src, cls, order, jnp.stack([jnp.int32(0), n_early]))
    late_items = (tgt, src, cls, order, jnp.stack([n_early, n_live]))
    cut = len(blocks) - 2 * REACH
    partial, aggregated = translate_pairs(
        early_items, trans_table, blocks[:cut], offsets[:cut], box_dev
    )
    (incoming,) = translate_pairs(
        late_items, trans_table, blocks[cut:], offsets[cut:], box_dev, init=partial
    )
    return (aggregated, incoming)


def solution(mesh):
    placed = (
        P("box", None, "dir", None),
        P("box"),
        P(),
        P(None, None, "dir", None),
        P("box"),
        P("box"),
        P("box"),
        P("box"),
    )
    return jax.shard_map(
        body,
        mesh=mesh,
        in_specs=placed,
        out_specs=(P("box", None, "dir", None), P("box", None, "dir", None)),
        check_vma=False,
    )
```
